32 devices in a mesh: groups: 2 (over x), ctx: 16 (over z, y, core).
Axes of the slice: x: 2, y: 2, z: 4, core: 2. Of those that a mesh axis runs over, the one named last changes fastest.
Arguments:
- qkv: bfloat16 [4096, 12288], P(('groups', 'ctx')), parts along dimension 0, may hold values from -6 to 6
- doc_ids: int32 [4096], P(('groups', 'ctx')), parts along dimension 0, may hold values from 0 to 7, as said below
- short_w: float32 [7, 12288], replicated, may hold values from -2 to 2
- rates: float32 [256, 16], replicated, may hold values from 0 to 1, as said below
- residues: float32 [256, 16], replicated, may hold values from -1 to 1
Outputs:
- mixed: bfloat16 [4096, 4096], P(('groups', 'ctx')), parts along dimension 0
The draws below stay inside these ranges and needn't reach their ends.
There are 2 independent parts, one for each index of `groups`. The reference program is written for one: setup_inputs(seed, part) draws one part's arguments, and reference() takes and returns one part's arrays. A program takes and returns all parts, laid end to end along the dimension named above; an argument that names none is the same for every part. Nothing has to cross between parts.
Inputs may be any that keep to these rules, and one draw needn't show every extreme that they name: `doc_ids`: never falling along the tokens; every document is one nonempty run. `rates`: positive.
All inputs are finite; a program needn't handle non-finite values.
Results may differ from the reference program's by a relative error of at most 0.005.
Values may be sent and summed in bfloat16 or wider, within the bound.
No kernel may reach another device: no remote copies, remote signals or barrier semaphores. Data moves between devices by JAX's collectives and lax.ppermute only.
A program may use at most 128 MiB of HBM per device.

```python
import jax
import jax.numpy as jnp
from jax import lax

C = 4096
ORDER = 16
SHORT = 7
DOCS = 8
TOK_DEV = 128
FILT = 256
TOKENS = 2048


def pole_rates(key):
    base = jax.random.fold_in(key, 11)
    key_mask, key_slow, key_fast = jax.random.split(base, 3)
    share = 0.5
    slow_mask = jax.random.bernoulli(key_mask, share, (FILT, ORDER))
    slow_log = jax.random.uniform(key_slow, (FILT, ORDER), jnp.float32, jnp.log(0.05 / TOKENS), jnp.log(2.0 / TOKENS))
    fast_log = jax.random.uniform(key_fast, (FILT, ORDER), jnp.float32, jnp.log(1.0 / 48.0), jnp.log(0.125))
    return jnp.exp(jnp.where(slow_mask, slow_log, fast_log)).astype(jnp.float32)


def draw_rates(key, part):
    return pole_rates(key)


def draw_residues(key, part):
    rates_now = pole_rates(key)
    noise_key = jax.random.fold_in(key, 23)
    noise = jnp.clip(jax.random.normal(noise_key, (FILT, ORDER), jnp.float32), -4.0, 4.0)
    return (0.5 * noise * jnp.sqrt(2.0 * rates_now)).astype(jnp.float32)


def draw_doc_ids(key, part):
    base = jax.random.fold_in(key, 31)
    key_edge, key_near, key_lag, key_rank = jax.random.split(base, 4)
    shard_count = TOKENS // TOK_DEV
    at_edge = jax.random.randint(key_edge, (), 1, shard_count).astype(jnp.int32) * TOK_DEV
    near_edge = jax.random.randint(key_near, (), 1, shard_count).astype(jnp.int32) * TOK_DEV + jax.random.randint(key_lag, (), 1, SHORT - 1).astype(jnp.int32)
    rank_order = jax.random.permutation(key_rank, TOKENS).astype(jnp.int32)
    places = jnp.arange(TOKENS).astype(jnp.int32)
    blocked = (places == 0) | (places == at_edge) | (places == near_edge)
    scores = jnp.where(blocked, -1, rank_order).astype(jnp.int32)
    _, others = lax.top_k(scores, DOCS - 3)
    bounds = jnp.concatenate([jnp.stack([at_edge, near_edge]).astype(jnp.int32), others.astype(jnp.int32)], axis=0)
    return jnp.sum((places[:, None] >= bounds[None, :]).astype(jnp.int32), axis=1).astype(jnp.int32)


def steps_of(rng, dims, shards, least, top_value):
    gain, own = 1.0, jax.random.fold_in(rng, 6)
    for dim, blocks in shards:
        heights = jnp.exp(jax.random.uniform(jax.random.fold_in(own, dim), (blocks,), jnp.float32, least / len(shards), top_value / len(shards)))
        gain = gain * jnp.repeat(heights, dims[dim] // blocks).reshape([-1 if axis == dim else 1 for axis in range(len(dims))])
    return gain


def gaussian(rng, extent, spread, limit, pieces=(), kind=jnp.bfloat16):
    loudness = steps_of(rng, extent, pieces, -0.22, 0.18) if pieces else 1.0
    result = jax.random.normal(rng, extent, jnp.float32) * spread * loudness
    return jnp.minimum(jnp.maximum(result, -limit), limit).astype(kind)


def setup_inputs(seed: int = 0, part: int = 0) -> dict:
    seeds = jax.random.split(jax.random.key(seed), 6)
    part_keys = jax.random.split(jax.random.fold_in(seeds[5], part), 6)
    return {
        "qkv": gaussian(part_keys[0], (TOKENS, 3 * C), 1.0, 6.0, ((0, 16),)),
        "doc_ids": draw_doc_ids(jax.random.fold_in(jax.random.fold_in(seeds[5], part), 71), part),
        "short_w": gaussian(seeds[2], (SHORT, 3 * C), SHORT ** -0.5, 2.0, (), jnp.float32),
        "rates": draw_rates(jax.random.fold_in(seeds[5], 71), part),
        "residues": draw_residues(jax.random.fold_in(seeds[5], 71), part),
    }


HIGH = lax.Precision.HIGHEST


def short_conv(extended, ext_rows, weights, length):
    tap_count = weights.shape[0]
    own_docs = ext_rows[tap_count - 1:]
    summed = jnp.zeros((length, extended.shape[1]), jnp.float32)
    for tap_index in range(tap_count):
        begin = tap_count - 1 - tap_index
        window = extended[begin:begin + length].astype(jnp.float32)
        matching = (ext_rows[begin:begin + length] == own_docs).astype(jnp.float32)[:, None]
        summed = summed + weights[tap_index][None, :] * window * matching
    return summed


def block_terms(product, doc_rows, rates, residues):
    length = product.shape[0]
    filters, pole_count = rates.shape
    group_width = product.shape[1] // filters
    places = jnp.arange(length).astype(jnp.float32)
    decays = jnp.exp(-rates[:, :, None] * places[None, None, :])
    kernel = jnp.sum(residues[:, :, None] * decays, axis=1)
    offsets = jnp.arange(length)[:, None] - jnp.arange(length)[None, :]
    visible = (offsets >= 0) & (doc_rows[:, None] == doc_rows[None, :])
    toeplitz = jnp.where(visible[None], kernel[:, jnp.clip(offsets, 0, length - 1)], 0.0)
    values = product.astype(jnp.float32).reshape(length, filters, group_width)
    local_part = jnp.einsum("gts,sgc->tgc", toeplitz, values, precision=HIGH).reshape(length, filters * group_width)
    at_tail = (doc_rows == doc_rows[length - 1]).astype(jnp.float32)
    at_head = (doc_rows == doc_rows[0]).astype(jnp.float32)
    end_weight = jnp.exp(-rates[:, :, None] * (length - 1.0 - places)[None, None, :]) * at_tail[None, None, :]
    states = jnp.einsum("gks,sgc->kgc", end_weight, values, precision=HIGH).reshape(pole_count, filters * group_width)
    passing = jnp.exp(-rates * length) * (doc_rows[0] == doc_rows[length - 1]).astype(jnp.float32)
    in_weight = residues[:, :, None] * jnp.exp(-rates[:, :, None] * (places + 1.0)[None, None, :]) * at_head[None, None, :]
    return local_part, states, passing.T, in_weight


def carried(in_weight, beginning):
    filters, pole_count, length = in_weight.shape
    group_width = beginning.shape[1] // filters
    shaped = beginning.reshape(pole_count, filters, group_width)
    return jnp.einsum("gkt,kgc->tgc", in_weight, shaped, precision=HIGH).reshape(length, filters * group_width)


def reference(qkv, doc_ids, short_w, rates, residues):
    channels = qkv.shape[1] // 3
    group_width = channels // rates.shape[0]
    padded = jnp.concatenate([jnp.zeros((SHORT - 1, qkv.shape[1]), jnp.bfloat16), qkv], axis=0)
    pad_rows = jnp.concatenate([jnp.zeros((SHORT - 1,), jnp.int32) + doc_ids[0], doc_ids], axis=0)

    def advance(carry, block_index):
        state_now, prev_doc = carry
        begin = (block_index * TOK_DEV).astype(jnp.int32)
        extended = lax.dynamic_slice_in_dim(padded, begin, TOK_DEV + SHORT - 1, 0)
        ext_rows = lax.dynamic_slice_in_dim(pad_rows, begin, TOK_DEV + SHORT - 1, 0)
        convolved = short_conv(extended, ext_rows, short_w, TOK_DEV)
        queries = convolved[:, :channels]
        gated = (convolved[:, channels:2 * channels] * convolved[:, 2 * channels:]).astype(jnp.bfloat16)
        doc_rows = ext_rows[SHORT - 1:]
        local_part, states, passing, in_weight = block_terms(gated, doc_rows, rates, residues)
        joined = (doc_rows[0] == prev_doc).astype(jnp.float32)
        beginning = joined * state_now
        long_part = local_part + carried(in_weight, beginning)
        emitted = (queries * long_part).astype(jnp.bfloat16)
        new_state = jnp.repeat(passing, group_width, axis=1) * beginning + states
        return (new_state, doc_rows[TOK_DEV - 1]), emitted

    start_carry = (jnp.zeros((rates.shape[1], channels), jnp.float32), doc_ids[0])
    _, outputs = lax.scan(advance, start_carry, jnp.arange(TOKENS // TOK_DEV).astype(jnp.int32))
    return outputs.reshape(TOKENS, channels)
```

```python
import functools

import jax
import jax.numpy as jnp
from jax import lax
from jax.experimental import pallas as pl
from jax.experimental.pallas import tpu as pltpu
from jax.sharding import PartitionSpec as P

HIGH = lax.Precision.HIGHEST
WIDTH = 256
RIM = 8


def from_behind(shard, axis, by):
    peers = lax.axis_size(axis)
    pairs = [(i, i + by) for i in range(peers) if 0 <= i + by < peers]
    return lax.ppermute(shard, axis, pairs)


def split_bf16(x):
    hi = x.astype(jnp.bfloat16)
    lo = (x - lax.optimization_barrier(hi).astype(jnp.float32)).astype(jnp.bfloat16)
    return hi, lo


def local_kernel(taps, group_width,
                 xq, xk, xv, rq, rk, rv, wq, wk, wv, masks_ref, m_ref, base_ref, ewh_ref, ewl_ref,
                 q_out, loc_out, st_out, ext_s):
    length, width = xq.shape
    groups = width // group_width
    masks = masks_ref[...]

    def conv(x_ref, r_ref, w_ref):
        ext_s[0:RIM, :] = r_ref[...].astype(jnp.float32)
        ext_s[RIM:RIM + length, :] = x_ref[...].astype(jnp.float32)
        w = w_ref[...]
        acc = (w[0:1, :] * ext_s[RIM:RIM + length, :]) * masks[:, 0:1]
        for j in range(1, taps):
            window = ext_s[pl.ds(RIM - j, length), :]
            acc = acc + (w[j:j + 1, :] * window) * masks[:, j:j + 1]
        return acc

    cq = conv(xq, rq, wq)
    ck = conv(xk, rk, wk)
    cv = conv(xv, rv, wv)
    q_out[...] = cq
    gated = (ck * cv).astype(jnp.bfloat16)

    lane_group = lax.broadcasted_iota(jnp.int32, (length, width), 1) // group_width
    zero = jnp.zeros_like(gated)
    xbd = jnp.concatenate([jnp.where(lane_group == g, gated, zero) for g in range(groups)], axis=0)

    visible = m_ref[...] > 0.5
    pieces = []
    for g in range(groups):
        row = jnp.broadcast_to(base_ref[g:g + 1, :], (length, length))
        rolled = pltpu.roll(row, 0, 1, stride=1, stride_axis=0)
        pieces.append(jnp.where(visible, rolled, 0.0))
    toeplitz = jnp.concatenate(pieces, axis=1)
    t_hi = toeplitz.astype(jnp.bfloat16)
    t_lo = (toeplitz - t_hi.astype(jnp.float32)).astype(jnp.bfloat16)
    loc = jnp.dot(t_hi, xbd, preferred_element_type=jnp.float32)
    loc = loc + jnp.dot(t_lo, xbd, preferred_element_type=jnp.float32)
    loc_out[...] = loc
    st = jnp.dot(ewh_ref[...], xbd, preferred_element_type=jnp.float32)
    st = st + jnp.dot(ewl_ref[...], xbd, preferred_element_type=jnp.float32)
    st_out[...] = st


def final_kernel(group_width, pole_count, q_ref, loc_ref, iw_ref, b_ref, o_ref):
    length, width = q_ref.shape
    groups = width // group_width
    b = b_ref[...]
    tiled = jnp.concatenate([b] * groups, axis=0)
    row_group = lax.broadcasted_iota(jnp.int32, tiled.shape, 0) // pole_count
    lane_group = lax.broadcasted_iota(jnp.int32, tiled.shape, 1) // group_width
    bbd = jnp.where(row_group == lane_group, tiled, 0.0)
    car = jnp.dot(iw_ref[...], bbd, precision=HIGH, preferred_element_type=jnp.float32)
    o_ref[...] = (q_ref[...] * (loc_ref[...] + car)).astype(o_ref.dtype)


def on_device(qkv, doc_ids, short_w, rates, residues):
    length = qkv.shape[0]
    taps = short_w.shape[0]
    channels = qkv.shape[1] // 3
    filters, pole_count = rates.shape
    group_width = channels // filters
    width = min(WIDTH, channels)
    nb = channels // width
    gpb = width // group_width
    peers = lax.axis_size("ctx")
    me = lax.axis_index("ctx")

    doc_all = lax.all_gather(doc_ids, "ctx", tiled=True)
    prev_docs = lax.dynamic_slice(doc_all, (jnp.maximum(me * length - RIM, 0),), (RIM,))
    rim = from_behind(qkv[length - RIM:], "ctx", 1)

    ext_docs = jnp.concatenate([prev_docs, doc_ids], axis=0)
    cols = [(ext_docs[RIM - j:RIM - j + length] == doc_ids) for j in range(taps)]
    cols += [jnp.zeros((length,), bool)] * (8 - taps)
    masks = jnp.stack(cols, axis=1).astype(jnp.float32)
    pos = jnp.arange(length)
    visible = ((pos[None, :] <= pos[:, None]) & (doc_ids[:, None] == doc_ids[None, :])).astype(jnp.float32)

    places = jnp.arange(length).astype(jnp.float32)
    lags = ((length - jnp.arange(length)) % length).astype(jnp.float32)
    base = jnp.sum(residues[:, :, None] * jnp.exp(-rates[:, :, None] * lags[None, None, :]), axis=1)
    at_tail = (doc_ids == doc_ids[length - 1]).astype(jnp.float32)
    at_head = (doc_ids == doc_ids[0]).astype(jnp.float32)
    end_weight = jnp.exp(-rates[:, :, None] * (length - 1.0 - places)[None, None, :]) * at_tail[None, None, :]
    end_weight = end_weight.transpose(1, 0, 2).reshape(pole_count, filters * length)
    ew_hi, ew_lo = split_bf16(end_weight)
    in_weight = (residues[:, :, None] * jnp.exp(-rates[:, :, None] * (places + 1.0)[None, None, :])
                 * at_head[None, None, :])
    in_weight = in_weight.transpose(2, 0, 1).reshape(length, filters * pole_count)

    col = lambda off: (lambda j: (0, j + off))
    fixed = lambda j: (0, 0)
    q_part, local_part, states = pl.pallas_call(
        functools.partial(local_kernel, taps, group_width),
        grid=(nb,),
        in_specs=[
            pl.BlockSpec((length, width), col(0)),
            pl.BlockSpec((length, width), col(nb)),
            pl.BlockSpec((length, width), col(2 * nb)),
            pl.BlockSpec((RIM, width), col(0)),
            pl.BlockSpec((RIM, width), col(nb)),
            pl.BlockSpec((RIM, width), col(2 * nb)),
            pl.BlockSpec((taps, width), col(0)),
            pl.BlockSpec((taps, width), col(nb)),
            pl.BlockSpec((taps, width), col(2 * nb)),
            pl.BlockSpec((length, 8), fixed),
            pl.BlockSpec((length, length), fixed),
            pl.BlockSpec((gpb, length), lambda j: (j, 0)),
            pl.BlockSpec((pole_count, gpb * length), col(0)),
            pl.BlockSpec((pole_count, gpb * length), col(0)),
        ],
        out_specs=[
            pl.BlockSpec((length, width), col(0)),
            pl.BlockSpec((length, width), col(0)),
            pl.BlockSpec((pole_count, width), col(0)),
        ],
        out_shape=[
            jax.ShapeDtypeStruct((length, channels), jnp.float32),
            jax.ShapeDtypeStruct((length, channels), jnp.float32),
            jax.ShapeDtypeStruct((pole_count, channels), jnp.float32),
        ],
        scratch_shapes=[pltpu.VMEM((RIM + length, width), jnp.float32)],
        compiler_params=pltpu.CompilerParams(dimension_semantics=("arbitrary",)),
    )(qkv, qkv, qkv, rim, rim, rim, short_w, short_w, short_w, masks, visible, base, ew_hi, ew_lo)

    rate_cols = jnp.repeat(rates.T, group_width, axis=1)
    doc_last = doc_all[length - 1::length]
    mine_last = doc_last[me]
    total = states
    offset = 1
    while offset < peers:
        got = from_behind(total, "ctx", offset)
        source = jnp.maximum(me - offset, 0)
        same = (me >= offset) & (doc_last[source] == mine_last)
        decay = jnp.exp(-rate_cols * float(length * offset))
        total = total + jnp.where(same, decay * got, 0.0)
        offset *= 2
    before = from_behind(total, "ctx", 1)
    joined = (me >= 1) & (doc_last[jnp.maximum(me - 1, 0)] == doc_ids[0])
    beginning = jnp.where(joined, before, 0.0)

    return pl.pallas_call(
        functools.partial(final_kernel, group_width, pole_count),
        grid=(nb,),
        in_specs=[
            pl.BlockSpec((length, width), col(0)),
            pl.BlockSpec((length, width), col(0)),
            pl.BlockSpec((length, gpb * pole_count), col(0)),
            pl.BlockSpec((pole_count, width), col(0)),
        ],
        out_specs=pl.BlockSpec((length, width), col(0)),
        out_shape=jax.ShapeDtypeStruct((length, channels), jnp.bfloat16),
        compiler_params=pltpu.CompilerParams(dimension_semantics=("arbitrary",)),
    )(q_part, local_part, in_weight, beginning)


def solution(mesh):
    return jax.shard_map(
        on_device,
        mesh=mesh,
        in_specs=(P(("groups", "ctx"), None), P(("groups", "ctx")), P(), P(), P()),
        out_specs=P(("groups", "ctx"), None),
        check_vma=False,
    )
```

```python
import functools

import jax
import jax.numpy as jnp
from jax import lax
from jax.experimental import pallas as pl
from jax.experimental.pallas import tpu as pltpu
from jax.sharding import PartitionSpec as P

HIGH = lax.Precision.HIGHEST
WIDTH = 256
RIM = 8


def from_behind(shard, axis, by):
    peers = lax.axis_size(axis)
    pairs = [(i, i + by) for i in range(peers) if 0 <= i + by < peers]
    return lax.ppermute(shard, axis, pairs)


def split_bf16(x):
    hi = x.astype(jnp.bfloat16)
    lo = (x - lax.optimization_barrier(hi).astype(jnp.float32)).astype(jnp.bfloat16)
    return hi, lo


def local_kernel(taps, group_width,
                 xq, xk, xv, rq, rk, rv, wq, wk, wv, masks_ref, m_ref, base_ref, ewh_ref, ewl_ref,
                 q_out, loc_out, st_out, ext_s):
    length, width = xq.shape
    groups = width // group_width
    masks = masks_ref[...]

    def conv(x_ref, r_ref, w_ref):
        ext_s[0:RIM, :] = r_ref[...].astype(jnp.float32)
        ext_s[RIM:RIM + length, :] = x_ref[...].astype(jnp.float32)
        w = w_ref[...]
        acc = (w[0:1, :] * ext_s[RIM:RIM + length, :]) * masks[:, 0:1]
        for j in range(1, taps):
            window = ext_s[pl.ds(RIM - j, length), :]
            acc = acc + (w[j:j + 1, :] * window) * masks[:, j:j + 1]
        return acc

    cq = conv(xq, rq, wq)
    ck = conv(xk, rk, wk)
    cv = conv(xv, rv, wv)
    q_out[...] = cq
    gated = (ck * cv).astype(jnp.bfloat16)

    lane_group = lax.broadcasted_iota(jnp.int32, (length, width), 1) // group_width
    zero = jnp.zeros_like(gated)
    xbd = jnp.concatenate([jnp.where(lane_group == g, gated, zero) for g in range(groups)], axis=0)

    visible = m_ref[...] > 0.5
    pieces = []
    for g in range(groups):
        row = jnp.broadcast_to(base_ref[g:g + 1, :], (length, length))
        rolled = pltpu.roll(row, 0, 1, stride=1, stride_axis=0)
        pieces.append(jnp.where(visible, rolled, 0.0))
    toeplitz = jnp.concatenate(pieces, axis=1)
    t_hi = toeplitz.astype(jnp.bfloat16)
    t_lo = (toeplitz - t_hi.astype(jnp.float32)).astype(jnp.bfloat16)
    loc = jnp.dot(t_hi, xbd, preferred_element_type=jnp.float32)
    loc = loc + jnp.dot(t_lo, xbd, preferred_element_type=jnp.float32)
    loc_out[...] = loc
    st = jnp.dot(ewh_ref[...], xbd, preferred_element_type=jnp.float32)
    st = st + jnp.dot(ewl_ref[...], xbd, preferred_element_type=jnp.float32)
    st_out[...] = st


def final_kernel(group_width, pole_count, q_ref, loc_ref, iwh_ref, iwl_ref, b_ref, o_ref):
    length, width = q_ref.shape
    groups = width // group_width
    b = b_ref[...]
    tiled = jnp.concatenate([b] * groups, axis=0)
    row_group = lax.broadcasted_iota(jnp.int32, tiled.shape, 0) // pole_count
    lane_group = lax.broadcasted_iota(jnp.int32, tiled.shape, 1) // group_width
    bbd = jnp.where(row_group == lane_group, tiled, 0.0)
    b_hi = bbd.astype(jnp.bfloat16)
    b_lo = (bbd - b_hi.astype(jnp.float32)).astype(jnp.bfloat16)
    iw_hi = iwh_ref[...]
    car = jnp.dot(iw_hi, b_hi, preferred_element_type=jnp.float32)
    car = car + jnp.dot(iw_hi, b_lo, preferred_element_type=jnp.float32)
    car = car + jnp.dot(iwl_ref[...], b_hi, preferred_element_type=jnp.float32)
    o_ref[...] = (q_ref[...] * (loc_ref[...] + car)).astype(o_ref.dtype)


def on_device(qkv, doc_ids, short_w, rates, residues):
    length = qkv.shape[0]
    taps = short_w.shape[0]
    channels = qkv.shape[1] // 3
    filters, pole_count = rates.shape
    group_width = channels // filters
    width = min(WIDTH, channels)
    nb = channels // width
    gpb = width // group_width
    peers = lax.axis_size("ctx")
    me = lax.axis_index("ctx")

    tail_docs = jnp.broadcast_to(doc_ids[length - RIM:, None].astype(jnp.bfloat16), (RIM, 128))
    rim = from_behind(jnp.concatenate([qkv[length - RIM:], tail_docs], axis=1), "ctx", 1)
    prev_docs = rim[:, 3 * channels].astype(jnp.int32)

    ext_docs = jnp.concatenate([prev_docs, doc_ids], axis=0)
    cols = [(ext_docs[RIM - j:RIM - j + length] == doc_ids) for j in range(taps)]
    cols += [jnp.zeros((length,), bool)] * (8 - taps)
    masks = jnp.stack(cols, axis=1).astype(jnp.float32)
    pos = jnp.arange(length)
    visible = ((pos[None, :] <= pos[:, None]) & (doc_ids[:, None] == doc_ids[None, :])).astype(jnp.float32)

    places = jnp.arange(length).astype(jnp.float32)
    lags = ((length - jnp.arange(length)) % length).astype(jnp.float32)
    base = jnp.sum(residues[:, :, None] * jnp.exp(-rates[:, :, None] * lags[None, None, :]), axis=1)
    at_tail = (doc_ids == doc_ids[length - 1]).astype(jnp.float32)
    at_head = (doc_ids == doc_ids[0]).astype(jnp.float32)
    end_weight = jnp.exp(-rates[:, :, None] * (length - 1.0 - places)[None, None, :]) * at_tail[None, None, :]
    end_weight = end_weight.transpose(1, 0, 2).reshape(pole_count, filters * length)
    ew_hi, ew_lo = split_bf16(end_weight)
    in_weight = (residues[:, :, None] * jnp.exp(-rates[:, :, None] * (places + 1.0)[None, None, :])
                 * at_head[None, None, :])
    in_weight = in_weight.transpose(2, 0, 1).reshape(length, filters * pole_count)

    col = lambda off: (lambda j: (0, j + off))
    fixed = lambda j: (0, 0)
    q_part, local_part, states = pl.pallas_call(
        functools.partial(local_kernel, taps, group_width),
        grid=(nb,),
        in_specs=[
            pl.BlockSpec((length, width), col(0)),
            pl.BlockSpec((length, width), col(nb)),
            pl.BlockSpec((length, width), col(2 * nb)),
            pl.BlockSpec((RIM, width), col(0)),
            pl.BlockSpec((RIM, width), col(nb)),
            pl.BlockSpec((RIM, width), col(2 * nb)),
            pl.BlockSpec((taps, width), col(0)),
            pl.BlockSpec((taps, width), col(nb)),
            pl.BlockSpec((taps, width), col(2 * nb)),
            pl.BlockSpec((length, 8), fixed),
            pl.BlockSpec((length, length), fixed),
            pl.BlockSpec((gpb, length), lambda j: (j, 0)),
            pl.BlockSpec((pole_count, gpb * length), col(0)),
            pl.BlockSpec((pole_count, gpb * length), col(0)),
        ],
        out_specs=[
            pl.BlockSpec((length, width), col(0)),
            pl.BlockSpec((length, width), col(0)),
            pl.BlockSpec((pole_count, width), col(0)),
        ],
        out_shape=[
            jax.ShapeDtypeStruct((length, channels), jnp.float32),
            jax.ShapeDtypeStruct((length, channels), jnp.float32),
            jax.ShapeDtypeStruct((pole_count, channels), jnp.float32),
        ],
        scratch_shapes=[pltpu.VMEM((RIM + length, width), jnp.float32)],
        compiler_params=pltpu.CompilerParams(dimension_semantics=("arbitrary",)),
    )(qkv, qkv, qkv, rim, rim, rim, short_w, short_w, short_w, masks, visible, base, ew_hi, ew_lo)

    prev_last = prev_docs[RIM - 1]
    flag = ((prev_last == doc_ids[0]) & (doc_ids[0] == doc_ids[length - 1])).astype(jnp.float32)
    offsets = []
    while (1 << len(offsets)) < peers:
        offsets.append(1 << len(offsets))
    spans = jnp.asarray([float(length * o) for o in offsets], jnp.float32)
    decays = jnp.repeat(jnp.exp(-rates.T[None] * spans[:, None, None]), group_width, axis=2)
    total = states
    for step, offset in enumerate(offsets):
        if step + 1 < len(offsets):
            packed = jnp.concatenate([total, jnp.full((pole_count, 128), flag, jnp.float32)], axis=1)
            got = from_behind(packed, "ctx", offset)
            total = total + (flag * decays[step]) * got[:, :channels]
            flag = flag * got[0, channels]
        else:
            got = from_behind(total, "ctx", offset)
            total = total + (flag * decays[step]) * got
    before = from_behind(total, "ctx", 1)
    joined = (me >= 1) & (prev_last == doc_ids[0])
    beginning = jnp.where(joined, before, 0.0)
    iw_hi, iw_lo = split_bf16(in_weight)

    return pl.pallas_call(
        functools.partial(final_kernel, group_width, pole_count),
        grid=(nb,),
        in_specs=[
            pl.BlockSpec((length, width), col(0)),
            pl.BlockSpec((length, width), col(0)),
            pl.BlockSpec((length, gpb * pole_count), col(0)),
            pl.BlockSpec((length, gpb * pole_count), col(0)),
            pl.BlockSpec((pole_count, width), col(0)),
        ],
        out_specs=pl.BlockSpec((length, width), col(0)),
        out_shape=jax.ShapeDtypeStruct((length, channels), jnp.bfloat16),
        compiler_params=pltpu.CompilerParams(dimension_semantics=("arbitrary",)),
    )(q_part, local_part, iw_hi, iw_lo, beginning)


def solution(mesh):
    return jax.shard_map(
        on_device,
        mesh=mesh,
        in_specs=(P(("groups", "ctx"), None), P(("groups", "ctx")), P(), P(), P()),
        out_specs=P(("groups", "ctx"), None),
        check_vma=False,
    )
```

```python
import functools

import jax
import jax.numpy as jnp
from jax import lax
from jax.experimental import pallas as pl
from jax.experimental.pallas import tpu as pltpu
from jax.sharding import PartitionSpec as P

WIDTH = 256
FINAL_WIDTH = 1024
RIM = 8
LANES = 128


def from_behind(shard, axis, by):
    peers = lax.axis_size(axis)
    pairs = [(i, i + by) for i in range(peers) if 0 <= i + by < peers]
    return lax.ppermute(shard, axis, pairs)


def split2(x):
    hi = x.astype(jnp.bfloat16)
    lo = (x - hi.astype(jnp.float32)).astype(jnp.bfloat16)
    return hi, lo


def split3(x):
    hi = x.astype(jnp.bfloat16)
    rest = x - hi.astype(jnp.float32)
    mid = rest.astype(jnp.bfloat16)
    lo = (rest - mid.astype(jnp.float32)).astype(jnp.bfloat16)
    return hi, mid, lo


def local_kernel(taps, group_width, spans,
                 xq, xk, xv, rq, rk, rv, wq, wk, wv, masks_ref, m_ref, rt_ref, et_ref, tail_ref,
                 flag_ref, q_out, loc_out, pk_out, dec_out, ext_s):
    length, width = xq.shape
    groups = width // group_width
    pole_count = rt_ref.shape[1]
    channels = pk_out.shape[1] - LANES
    step = pl.program_id(0)
    masks = masks_ref[...]

    def conv(x_ref, r_ref, w_ref):
        ext_s[0:RIM, :] = r_ref[...].astype(jnp.float32)
        ext_s[RIM:RIM + length, :] = x_ref[...].astype(jnp.float32)
        w = w_ref[...]
        acc = (w[0:1, :] * ext_s[RIM:RIM + length, :]) * masks[:, 0:1]
        for j in range(1, taps):
            window = ext_s[pl.ds(RIM - j, length), :]
            acc = acc + (w[j:j + 1, :] * window) * masks[:, j:j + 1]
        return acc

    cq = conv(xq, rq, wq)
    ck = conv(xk, rk, wk)
    cv = conv(xv, rv, wv)
    q_out[...] = cq
    gated = (ck * cv).astype(jnp.bfloat16)

    lane_group = lax.broadcasted_iota(jnp.int32, (length, width), 1) // group_width
    zero = jnp.zeros_like(gated)
    xbd = jnp.concatenate([jnp.where(lane_group == g, gated, zero) for g in range(groups)], axis=0)

    rt = rt_ref[0]
    et = et_ref[0]
    lane = lax.broadcasted_iota(jnp.int32, (1, length), 1)
    lags = ((length - lane) % length).astype(jnp.float32)
    to_end = (length - 1 - lane).astype(jnp.float32)
    at_tail = tail_ref[0:1, :]
    visible = m_ref[...] > 0.5
    pieces = []
    ends = []
    for g in range(groups):
        a_col = rt[:, g:g + 1]
        r_col = et[:, g:g + 1]
        base = jnp.sum(r_col * jnp.exp(-a_col * lags), axis=0, keepdims=True)
        row = jnp.broadcast_to(base, (length, length))
        rolled = pltpu.roll(row, 0, 1, stride=1, stride_axis=0)
        pieces.append(jnp.where(visible, rolled, 0.0))
        ends.append(jnp.exp(-a_col * to_end) * at_tail)
    lhs = jnp.concatenate([jnp.concatenate(pieces, axis=1), jnp.concatenate(ends, axis=1)], axis=0)
    l_hi, l_lo = split2(lhs)
    rows = length + pole_count
    res = jnp.dot(jnp.concatenate([l_hi, l_lo], axis=0), xbd, preferred_element_type=jnp.float32)
    loc_out[...] = res[0:length] + res[rows:rows + length]
    st = res[length:rows] + res[rows + length:2 * rows]
    pk_out[:, pl.ds(pl.multiple_of(step * width, width), width)] = st

    @pl.when(step == 0)
    def _():
        pk_out[:, channels:channels + LANES] = jnp.broadcast_to(flag_ref[0:1, :], (pole_count, LANES))

    spread = (lax.broadcasted_iota(jnp.int32, (groups, width), 1) // group_width
              == lax.broadcasted_iota(jnp.int32, (groups, width), 0)).astype(jnp.bfloat16)
    rate_cols = None
    for piece in split3(rt):
        part = jnp.dot(piece, spread, preferred_element_type=jnp.float32)
        rate_cols = part if rate_cols is None else rate_cols + part
    for r, span in enumerate(spans):
        dec_out[r] = jnp.exp(-rate_cols * span)


def final_kernel(group_width, pole_count, sub, q_ref, loc_ref, b_ref, rf_ref, ef_ref, head_ref, join_ref, o_ref):
    length, width = q_ref.shape
    groups = sub // group_width
    tcol = (lax.broadcasted_iota(jnp.int32, (length, 1), 0) + 1).astype(jnp.float32)
    iw = ef_ref[...] * jnp.exp(-rf_ref[...] * tcol) * head_ref[...]
    iw_hi, iw_lo = split2(iw)
    b_all = b_ref[...] * join_ref[0:1, 0:1]
    shape = (groups * pole_count, sub)
    row_group = lax.broadcasted_iota(jnp.int32, shape, 0) // pole_count
    lane_group = lax.broadcasted_iota(jnp.int32, shape, 1) // group_width
    same = row_group == lane_group
    for s in range(width // sub):
        cols = slice(s * sub, (s + 1) * sub)
        tiled = jnp.concatenate([b_all[:, cols]] * groups, axis=0)
        b_hi, b_lo = split2(jnp.where(same, tiled, 0.0))
        poles = slice(s * shape[0], (s + 1) * shape[0])
        ih = iw_hi[:, poles]
        car = jnp.dot(ih, b_hi, preferred_element_type=jnp.float32)
        car = car + jnp.dot(ih, b_lo, preferred_element_type=jnp.float32)
        car = car + jnp.dot(iw_lo[:, poles], b_hi, preferred_element_type=jnp.float32)
        o_ref[:, cols] = (q_ref[:, cols] * (loc_ref[:, cols] + car)).astype(o_ref.dtype)


def on_device(qkv, doc_ids, short_w, rates, residues):
    length = qkv.shape[0]
    taps = short_w.shape[0]
    channels = qkv.shape[1] // 3
    filters, pole_count = rates.shape
    group_width = channels // filters
    width = min(WIDTH, channels)
    nb = channels // width
    gpb = width // group_width
    final_width = min(FINAL_WIDTH, channels)
    peers = lax.axis_size("ctx")
    me = lax.axis_index("ctx")

    tail_docs = jnp.broadcast_to(doc_ids[length - RIM:, None].astype(jnp.bfloat16), (RIM, LANES))
    rim = from_behind(jnp.concatenate([qkv[length - RIM:], tail_docs], axis=1), "ctx", 1)
    prev_docs = rim[:, 3 * channels].astype(jnp.int32)
    prev_last = prev_docs[RIM - 1]

    ext_docs = jnp.concatenate([prev_docs, doc_ids], axis=0)
    cols = [(ext_docs[RIM - j:RIM - j + length] == doc_ids) for j in range(taps)]
    cols += [jnp.zeros((length,), bool)] * (8 - taps)
    masks = jnp.stack(cols, axis=1).astype(jnp.float32)
    pos = jnp.arange(length)
    visible = ((pos[None, :] <= pos[:, None]) & (doc_ids[:, None] == doc_ids[None, :])).astype(jnp.float32)
    at_tail = jnp.broadcast_to((doc_ids == doc_ids[length - 1]).astype(jnp.float32)[None, :], (8, length))
    at_head = (doc_ids == doc_ids[0]).astype(jnp.float32)[:, None]
    flag = ((prev_last == doc_ids[0]) & (doc_ids[0] == doc_ids[length - 1])).astype(jnp.float32)
    flag_row = jnp.full((8, LANES), flag, jnp.float32)
    joined = ((me >= 1) & (prev_last == doc_ids[0])).astype(jnp.float32)
    join_row = jnp.full((8, LANES), joined, jnp.float32)

    rates_t = rates.reshape(nb, gpb, pole_count).transpose(0, 2, 1)
    residues_t = residues.reshape(nb, gpb, pole_count).transpose(0, 2, 1)
    offsets = []
    while (1 << len(offsets)) < peers:
        offsets.append(1 << len(offsets))
    rounds = max(len(offsets), 1)
    spans = tuple(float(length * o) for o in offsets) or (float(length),)

    col = lambda off: (lambda j: (0, j + off))
    fixed = lambda j: (0, 0)
    q_part, local_part, packed, decays = pl.pallas_call(
        functools.partial(local_kernel, taps, group_width, spans),
        grid=(nb,),
        in_specs=[
            pl.BlockSpec((length, width), col(0)),
            pl.BlockSpec((length, width), col(nb)),
            pl.BlockSpec((length, width), col(2 * nb)),
            pl.BlockSpec((RIM, width), col(0)),
            pl.BlockSpec((RIM, width), col(nb)),
            pl.BlockSpec((RIM, width), col(2 * nb)),
            pl.BlockSpec((taps, width), col(0)),
            pl.BlockSpec((taps, width), col(nb)),
            pl.BlockSpec((taps, width), col(2 * nb)),
            pl.BlockSpec((length, 8), fixed),
            pl.BlockSpec((length, length), fixed),
            pl.BlockSpec((1, pole_count, gpb), lambda j: (j, 0, 0)),
            pl.BlockSpec((1, pole_count, gpb), lambda j: (j, 0, 0)),
            pl.BlockSpec((8, length), fixed),
            pl.BlockSpec((8, LANES), fixed),
        ],
        out_specs=[
            pl.BlockSpec((length, width), col(0)),
            pl.BlockSpec((length, width), col(0)),
            pl.BlockSpec((pole_count, channels + LANES), fixed),
            pl.BlockSpec((rounds, pole_count, width), lambda j: (0, 0, j)),
        ],
        out_shape=[
            jax.ShapeDtypeStruct((length, channels), jnp.float32),
            jax.ShapeDtypeStruct((length, channels), jnp.float32),
            jax.ShapeDtypeStruct((pole_count, channels + LANES), jnp.float32),
            jax.ShapeDtypeStruct((rounds, pole_count, channels), jnp.float32),
        ],
        scratch_shapes=[pltpu.VMEM((RIM + length, width), jnp.float32)],
        compiler_params=pltpu.CompilerParams(dimension_semantics=("arbitrary",)),
    )(qkv, qkv, qkv, rim, rim, rim, short_w, short_w, short_w, masks, visible, rates_t, residues_t,
      at_tail, flag_row)

    for step, offset in enumerate(offsets):
        got = from_behind(packed, "ctx", offset)
        mine_flag = packed[:, channels:channels + 1]
        body = packed[:, :channels] + (mine_flag * decays[step]) * got[:, :channels]
        flags = jnp.broadcast_to(mine_flag * got[:, channels:channels + 1], (pole_count, LANES))
        packed = jnp.concatenate([body, flags], axis=1)
    before = from_behind(packed, "ctx", 1)

    nbf = channels // final_width
    return pl.pallas_call(
        functools.partial(final_kernel, group_width, pole_count, width),
        grid=(nbf,),
        in_specs=[
            pl.BlockSpec((length, final_width), col(0)),
            pl.BlockSpec((length, final_width), col(0)),
            pl.BlockSpec((pole_count, final_width), col(0)),
            pl.BlockSpec((1, final_width // group_width * pole_count), col(0)),
            pl.BlockSpec((1, final_width // group_width * pole_count), col(0)),
            pl.BlockSpec((length, 1), fixed),
            pl.BlockSpec((8, LANES), fixed),
        ],
        out_specs=pl.BlockSpec((length, final_width), col(0)),
        out_shape=jax.ShapeDtypeStruct((length, channels), jnp.bfloat16),
        compiler_params=pltpu.CompilerParams(dimension_semantics=("arbitrary",)),
    )(q_part, local_part, before, rates.reshape(1, filters * pole_count),
      residues.reshape(1, filters * pole_count), at_head, join_row)


def solution(mesh):
    return jax.shard_map(
        on_device,
        mesh=mesh,
        in_specs=(P(("groups", "ctx"), None), P(("groups", "ctx")), P(), P(), P()),
        out_specs=P(("groups", "ctx"), None),
        check_vma=False,
    )
```

```python
import functools

import jax
import jax.numpy as jnp
from jax import lax
from jax.experimental import pallas as pl
from jax.experimental.pallas import tpu as pltpu
from jax.sharding import PartitionSpec as P

WIDTH = 256
FINAL_WIDTH = 1024
RIM = 8
LANES = 128


def from_behind(shard, axis, by):
    peers = lax.axis_size(axis)
    pairs = [(i, i + by) for i in range(peers) if 0 <= i + by < peers]
    return lax.ppermute(shard, axis, pairs)


def split2(x):
    hi = x.astype(jnp.bfloat16)
    lo = (x - hi.astype(jnp.float32)).astype(jnp.bfloat16)
    return hi, lo


def split3(x):
    hi = x.astype(jnp.bfloat16)
    rest = x - hi.astype(jnp.float32)
    mid = rest.astype(jnp.bfloat16)
    lo = (rest - mid.astype(jnp.float32)).astype(jnp.bfloat16)
    return hi, mid, lo


def local_kernel(taps, group_width, spans,
                 xq, xk, xv, rq, rk, rv, wq, wk, wv, e_ref, rt_ref, et_ref,
                 q_out, loc_out, pk_out, dec_out, info_out, ext_s, shift_s, vis_s, tail_s):
    length, width = xq.shape
    groups = width // group_width
    pole_count = rt_ref.shape[1]
    channels = pk_out.shape[1] - LANES
    span_r = e_ref.shape[1]
    step = pl.program_id(0)

    @pl.when(step == 0)
    def _():
        e_row = e_ref[0:1, :]
        t_col = lax.broadcasted_iota(jnp.int32, (length, span_r), 0)
        r_row = lax.broadcasted_iota(jnp.int32, (length, span_r), 1)
        doc_col = jnp.sum(jnp.where(r_row == t_col, e_row, 0.0), axis=1, keepdims=True)
        eq = e_row == doc_col
        place = jnp.where(r_row < length, r_row, r_row - length - RIM)
        for j in range(taps):
            hit = eq & (place == t_col - j) & (r_row < length + RIM)
            shift_s[j * length:(j + 1) * length, :] = jnp.where(hit, 1.0, 0.0).astype(jnp.bfloat16)
        eqf = jnp.where(eq, 1.0, 0.0)
        causal = r_row[:, :length] <= t_col[:, :length]
        vis_s[...] = jnp.where(causal, eqf[:, :length], 0.0)
        tail_s[...] = jnp.broadcast_to(eqf[length - 1:length, :length], tail_s.shape)
        into = eqf[0:1, length + RIM - 1:length + RIM]
        flag = into * eqf[length - 1:length, 0:1]
        pk_out[:, channels:channels + LANES] = jnp.broadcast_to(flag, (pole_count, LANES))
        lane = lax.broadcasted_iota(jnp.int32, info_out.shape, 1)
        info_out[...] = jnp.where(lane == 0, eqf[:, 0:1], jnp.broadcast_to(into, info_out.shape))
        ext_s[...] = jnp.zeros_like(ext_s)

    shifts = shift_s[...]

    def conv(x_ref, r_ref, w_ref):
        ext_s[0:length, :] = x_ref[...]
        ext_s[length:length + RIM, :] = r_ref[...]
        windows = jnp.dot(shifts, ext_s[...], preferred_element_type=jnp.float32)
        w = w_ref[...]
        acc = w[0:1, :] * windows[0:length]
        for j in range(1, taps):
            acc = acc + w[j:j + 1, :] * windows[j * length:(j + 1) * length]
        return acc

    cq = conv(xq, rq, wq)
    ck = conv(xk, rk, wk)
    cv = conv(xv, rv, wv)
    q_out[...] = cq
    gated = (ck * cv).astype(jnp.bfloat16)

    lane_group = lax.broadcasted_iota(jnp.int32, (length, width), 1) // group_width
    zero = jnp.zeros_like(gated)
    xbd = jnp.concatenate([jnp.where(lane_group == g, gated, zero) for g in range(groups)], axis=0)

    rt = rt_ref[0]
    et = et_ref[0]
    lane = lax.broadcasted_iota(jnp.int32, (1, length), 1)
    lags = ((length - lane) % length).astype(jnp.float32)
    to_end = (length - 1 - lane).astype(jnp.float32)
    at_tail = tail_s[0:1, :]
    visible = vis_s[...] > 0.5
    pieces = []
    ends = []
    for g in range(groups):
        a_col = rt[:, g:g + 1]
        r_col = et[:, g:g + 1]
        base = jnp.sum(r_col * jnp.exp(-a_col * lags), axis=0, keepdims=True)
        row = jnp.broadcast_to(base, (length, length))
        rolled = pltpu.roll(row, 0, 1, stride=1, stride_axis=0)
        pieces.append(jnp.where(visible, rolled, 0.0))
        ends.append(jnp.exp(-a_col * to_end) * at_tail)
    lhs = jnp.concatenate([jnp.concatenate(pieces, axis=1), jnp.concatenate(ends, axis=1)], axis=0)
    l_hi, l_lo = split2(lhs)
    rows = length + pole_count
    res = jnp.dot(jnp.concatenate([l_hi, l_lo], axis=0), xbd, preferred_element_type=jnp.float32)
    loc_out[...] = res[0:length] + res[rows:rows + length]
    st = res[length:rows] + res[rows + length:2 * rows]
    pk_out[:, pl.ds(pl.multiple_of(step * width, width), width)] = st

    spread = (lax.broadcasted_iota(jnp.int32, (groups, width), 1) // group_width
              == lax.broadcasted_iota(jnp.int32, (groups, width), 0)).astype(jnp.bfloat16)
    rate_cols = None
    for piece in split3(rt):
        part = jnp.dot(piece, spread, preferred_element_type=jnp.float32)
        rate_cols = part if rate_cols is None else rate_cols + part
    for r, span in enumerate(spans):
        dec_out[r] = jnp.exp(-rate_cols * span)


def final_kernel(group_width, pole_count, sub, q_ref, loc_ref, b_ref, rf_ref, ef_ref, info_ref, o_ref):
    length, width = q_ref.shape
    groups = sub // group_width
    tcol = (lax.broadcasted_iota(jnp.int32, (length, 1), 0) + 1).astype(jnp.float32)
    iw = ef_ref[...] * jnp.exp(-rf_ref[...] * tcol) * info_ref[:, 0:1]
    iw_hi, iw_lo = split2(iw)
    b_all = b_ref[...] * info_ref[0:1, 1:2]
    shape = (groups * pole_count, sub)
    row_group = lax.broadcasted_iota(jnp.int32, shape, 0) // pole_count
    lane_group = lax.broadcasted_iota(jnp.int32, shape, 1) // group_width
    same = row_group == lane_group
    for s in range(width // sub):
        cols = slice(s * sub, (s + 1) * sub)
        tiled = jnp.concatenate([b_all[:, cols]] * groups, axis=0)
        b_hi, b_lo = split2(jnp.where(same, tiled, 0.0))
        poles = slice(s * shape[0], (s + 1) * shape[0])
        ih = iw_hi[:, poles]
        car = jnp.dot(ih, b_hi, preferred_element_type=jnp.float32)
        car = car + jnp.dot(ih, b_lo, preferred_element_type=jnp.float32)
        car = car + jnp.dot(iw_lo[:, poles], b_hi, preferred_element_type=jnp.float32)
        o_ref[:, cols] = (q_ref[:, cols] * (loc_ref[:, cols] + car)).astype(o_ref.dtype)


def on_device(qkv, doc_ids, short_w, rates, residues):
    length = qkv.shape[0]
    taps = short_w.shape[0]
    channels = qkv.shape[1] // 3
    filters, pole_count = rates.shape
    group_width = channels // filters
    width = min(WIDTH, channels)
    nb = channels // width
    gpb = width // group_width
    final_width = min(FINAL_WIDTH, channels)
    peers = lax.axis_size("ctx")
    me = lax.axis_index("ctx")

    tail_docs = jnp.broadcast_to(doc_ids[length - RIM:, None].astype(jnp.bfloat16), (RIM, LANES))
    rim = from_behind(jnp.concatenate([qkv[length - RIM:], tail_docs], axis=1), "ctx", 1)
    prev_docs = rim[:, 3 * channels].astype(jnp.int32)
    prev_last = prev_docs[RIM - 1]

    span_r = 2 * LANES
    e_vec = jnp.concatenate([doc_ids, prev_docs, jnp.full((span_r - length - RIM,), -1, jnp.int32)]).astype(jnp.float32)
    e_rows = jnp.broadcast_to(e_vec[None, :], (8, span_r))

    rates_t = rates.reshape(nb, gpb, pole_count).transpose(0, 2, 1)
    residues_t = residues.reshape(nb, gpb, pole_count).transpose(0, 2, 1)
    offsets = []
    while (1 << len(offsets)) < peers:
        offsets.append(1 << len(offsets))
    rounds = max(len(offsets), 1)
    spans = tuple(float(length * o) for o in offsets) or (float(length),)

    col = lambda off: (lambda j: (0, j + off))
    fixed = lambda j: (0, 0)
    q_part, local_part, packed, decays, info = pl.pallas_call(
        functools.partial(local_kernel, taps, group_width, spans),
        grid=(nb,),
        in_specs=[
            pl.BlockSpec((length, width), col(0)),
            pl.BlockSpec((length, width), col(nb)),
            pl.BlockSpec((length, width), col(2 * nb)),
            pl.BlockSpec((RIM, width), col(0)),
            pl.BlockSpec((RIM, width), col(nb)),
            pl.BlockSpec((RIM, width), col(2 * nb)),
            pl.BlockSpec((taps, width), col(0)),
            pl.BlockSpec((taps, width), col(nb)),
            pl.BlockSpec((taps, width), col(2 * nb)),
            pl.BlockSpec((8, span_r), fixed),
            pl.BlockSpec((1, pole_count, gpb), lambda j: (j, 0, 0)),
            pl.BlockSpec((1, pole_count, gpb), lambda j: (j, 0, 0)),
        ],
        out_specs=[
            pl.BlockSpec((length, width), col(0)),
            pl.BlockSpec((length, width), col(0)),
            pl.BlockSpec((pole_count, channels + LANES), fixed),
            pl.BlockSpec((rounds, pole_count, width), lambda j: (0, 0, j)),
            pl.BlockSpec((length, LANES), fixed),
        ],
        out_shape=[
            jax.ShapeDtypeStruct((length, channels), jnp.float32),
            jax.ShapeDtypeStruct((length, channels), jnp.float32),
            jax.ShapeDtypeStruct((pole_count, channels + LANES), jnp.float32),
            jax.ShapeDtypeStruct((rounds, pole_count, channels), jnp.float32),
            jax.ShapeDtypeStruct((length, LANES), jnp.float32),
        ],
        scratch_shapes=[
            pltpu.VMEM((span_r, width), jnp.bfloat16),
            pltpu.VMEM((taps * length, span_r), jnp.bfloat16),
            pltpu.VMEM((length, length), jnp.float32),
            pltpu.VMEM((8, length), jnp.float32),
        ],
        compiler_params=pltpu.CompilerParams(dimension_semantics=("arbitrary",)),
    )(qkv, qkv, qkv, rim, rim, rim, short_w, short_w, short_w, e_rows, rates_t, residues_t)

    for step, offset in enumerate(offsets):
        got = from_behind(packed, "ctx", offset)
        mine_flag = packed[:, channels:channels + 1]
        body = packed[:, :channels] + (mine_flag * decays[step]) * got[:, :channels]
        flags = jnp.broadcast_to(mine_flag * got[:, channels:channels + 1], (pole_count, LANES))
        packed = jnp.concatenate([body, flags], axis=1)
    before = from_behind(packed, "ctx", 1)

    nbf = channels // final_width
    return pl.pallas_call(
        functools.partial(final_kernel, group_width, pole_count, width),
        grid=(nbf,),
        in_specs=[
            pl.BlockSpec((length, final_width), col(0)),
            pl.BlockSpec((length, final_width), col(0)),
            pl.BlockSpec((pole_count, final_width), col(0)),
            pl.BlockSpec((1, final_width // group_width * pole_count), col(0)),
            pl.BlockSpec((1, final_width // group_width * pole_count), col(0)),
            pl.BlockSpec((length, LANES), fixed),
        ],
        out_specs=pl.BlockSpec((length, final_width), col(0)),
        out_shape=jax.ShapeDtypeStruct((length, channels), jnp.bfloat16),
        compiler_params=pltpu.CompilerParams(dimension_semantics=("arbitrary",)),
    )(q_part, local_part, before, rates.reshape(1, filters * pole_count),
      residues.reshape(1, filters * pole_count), info)


def solution(mesh):
    return jax.shard_map(
        on_device,
        mesh=mesh,
        in_specs=(P(("groups", "ctx"), None), P(("groups", "ctx")), P(), P(), P()),
        out_specs=P(("groups", "ctx"), None),
        check_vma=False,
    )
```

```python
import functools

import jax
import jax.numpy as jnp
from jax import lax
from jax.experimental import pallas as pl
from jax.experimental.pallas import tpu as pltpu
from jax.sharding import PartitionSpec as P

WIDTH = 256
FINAL_WIDTH = 1024
RIM = 8
LANES = 128


def from_behind(shard, axis, by):
    peers = lax.axis_size(axis)
    pairs = [(i, i + by) for i in range(peers) if 0 <= i + by < peers]
    return lax.ppermute(shard, axis, pairs)


def split2(x):
    hi = x.astype(jnp.bfloat16)
    lo = (x - hi.astype(jnp.float32)).astype(jnp.bfloat16)
    return hi, lo


def split3(x):
    hi = x.astype(jnp.bfloat16)
    rest = x - hi.astype(jnp.float32)
    mid = rest.astype(jnp.bfloat16)
    lo = (rest - mid.astype(jnp.float32)).astype(jnp.bfloat16)
    return hi, mid, lo


def local_kernel(taps, group_width, spans,
                 xq, xk, xv, rq, rk, rv, wq, wk, wv, e_ref, rt_ref, et_ref,
                 q_out, loc_out, pk_out, dec_out, info_out, ext_s, shift_s, vis_s, tail_s):
    length, width = xq.shape
    groups = width // group_width
    pole_count = rt_ref.shape[1]
    channels = pk_out.shape[1] - LANES
    span_r = e_ref.shape[1]
    step = pl.program_id(0)

    @pl.when(step == 0)
    def _():
        e_row = e_ref[0:1, :]
        t_col = lax.broadcasted_iota(jnp.int32, (length, span_r), 0)
        r_row = lax.broadcasted_iota(jnp.int32, (length, span_r), 1)
        doc_col = jnp.sum(jnp.where(r_row == t_col, e_row, 0.0), axis=1, keepdims=True)
        eq = e_row == doc_col
        place = jnp.where(r_row < length, r_row, r_row - length - RIM)
        for j in range(taps):
            hit = eq & (place == t_col - j) & (r_row < length + RIM)
            shift_s[j * length:(j + 1) * length, :] = jnp.where(hit, 1.0, 0.0).astype(jnp.bfloat16)
        eqf = jnp.where(eq, 1.0, 0.0)
        causal = r_row[:, :length] <= t_col[:, :length]
        vis_s[...] = jnp.where(causal, eqf[:, :length], 0.0)
        tail_s[...] = jnp.broadcast_to(eqf[length - 1:length, :length], tail_s.shape)
        into = eqf[0:1, length + RIM - 1:length + RIM]
        flag = into * eqf[length - 1:length, 0:1]
        pk_out[:, channels:channels + LANES] = jnp.broadcast_to(flag, (pole_count, LANES))
        lane = lax.broadcasted_iota(jnp.int32, info_out.shape, 1)
        info_out[...] = jnp.where(lane == 0, eqf[:, 0:1], jnp.broadcast_to(into, info_out.shape))
        ext_s[...] = jnp.zeros_like(ext_s)

    shifts = shift_s[...]

    def conv(x_ref, r_ref, w_ref):
        ext_s[0:length, :] = x_ref[...]
        ext_s[length:length + RIM, :] = r_ref[...]
        windows = jnp.dot(shifts, ext_s[...], preferred_element_type=jnp.float32)
        w = w_ref[...]
        acc = w[0:1, :] * windows[0:length]
        for j in range(1, taps):
            acc = acc + w[j:j + 1, :] * windows[j * length:(j + 1) * length]
        return acc

    cq = conv(xq, rq, wq)
    ck = conv(xk, rk, wk)
    cv = conv(xv, rv, wv)
    q_out[...] = cq
    gated = (ck * cv).astype(jnp.bfloat16)

    lane_group = lax.broadcasted_iota(jnp.int32, (length, width), 1) // group_width
    zero = jnp.zeros_like(gated)
    xbd = jnp.concatenate([jnp.where(lane_group == g, gated, zero) for g in range(groups)], axis=0)

    rt = rt_ref[0]
    et = et_ref[0]
    lane = lax.broadcasted_iota(jnp.int32, (1, length), 1)
    lags = ((length - lane) % length).astype(jnp.float32)
    to_end = (length - 1 - lane).astype(jnp.float32)
    at_tail = tail_s[0:1, :]
    visible = vis_s[...] > 0.5
    pieces = []
    ends = []
    for g in range(groups):
        a_col = rt[:, g:g + 1]
        r_col = et[:, g:g + 1]
        base = jnp.sum(r_col * jnp.exp(-a_col * lags), axis=0, keepdims=True)
        row = jnp.broadcast_to(base, (length, length))
        rolled = pltpu.roll(row, 0, 1, stride=1, stride_axis=0)
        pieces.append(jnp.where(visible, rolled, 0.0))
        ends.append(jnp.exp(-a_col * to_end) * at_tail)
    lhs = jnp.concatenate([jnp.concatenate(pieces, axis=1), jnp.concatenate(ends, axis=1)], axis=0)
    l_hi, l_lo = split2(lhs)
    rows = length + pole_count
    res = jnp.dot(jnp.concatenate([l_hi, l_lo], axis=0), xbd, preferred_element_type=jnp.float32)
    loc_out[...] = res[0:length] + res[rows:rows + length]
    st = res[length:rows] + res[rows + length:2 * rows]
    pk_out[:, pl.ds(pl.multiple_of(step * width, width), width)] = st

    spread = (lax.broadcasted_iota(jnp.int32, (groups, width), 1) // group_width
              == lax.broadcasted_iota(jnp.int32, (groups, width), 0)).astype(jnp.bfloat16)
    rate_cols = None
    for piece in split3(rt):
        part = jnp.dot(piece, spread, preferred_element_type=jnp.float32)
        rate_cols = part if rate_cols is None else rate_cols + part
    for r, span in enumerate(spans):
        dec_out[r] = jnp.exp(-rate_cols * span)


def final_kernel(group_width, pole_count, sub, q_ref, loc_ref, b_ref, rf_ref, ef_ref, info_ref, o_ref):
    length, width = q_ref.shape
    groups = sub // group_width
    tcol = (lax.broadcasted_iota(jnp.int32, (length, 1), 0) + 1).astype(jnp.float32)
    iw = ef_ref[...] * jnp.exp(-rf_ref[...] * tcol) * info_ref[:, 0:1]
    iw_hi, iw_lo = split2(iw)
    b_all = b_ref[...] * info_ref[0:1, 1:2]
    shape = (groups * pole_count, sub)
    row_group = lax.broadcasted_iota(jnp.int32, shape, 0) // pole_count
    lane_group = lax.broadcasted_iota(jnp.int32, shape, 1) // group_width
    same = row_group == lane_group
    for s in range(width // sub):
        cols = slice(s * sub, (s + 1) * sub)
        tiled = jnp.concatenate([b_all[:, cols]] * groups, axis=0)
        b_hi, b_lo = split2(jnp.where(same, tiled, 0.0))
        poles = slice(s * shape[0], (s + 1) * shape[0])
        ih = iw_hi[:, poles]
        car = jnp.dot(ih, b_hi, preferred_element_type=jnp.float32)
        car = car + jnp.dot(ih, b_lo, preferred_element_type=jnp.float32)
        car = car + jnp.dot(iw_lo[:, poles], b_hi, preferred_element_type=jnp.float32)
        o_ref[:, cols] = (q_ref[:, cols] * (loc_ref[:, cols] + car)).astype(o_ref.dtype)


def swap_cores(shard, axis):
    peers = lax.axis_size(axis)
    return lax.ppermute(shard, axis, [(i, i ^ 1) for i in range(peers)])


def chip_scan(packed, decays, channels, pole_count, peers, me):
    core = me % 2
    odd = core == 1
    half = channels // 2
    mine = lambda x: lax.dynamic_slice_in_dim(x, core * half, half, axis=1)
    got = swap_cores(packed, "ctx")
    own_s, own_f = packed[:, :channels], packed[:, channels:channels + 1]
    other_s, other_f = got[:, :channels], got[:, channels:channels + 1]
    even_s = jnp.where(odd, other_s, own_s)
    odd_s = jnp.where(odd, own_s, other_s)
    even_f = jnp.where(odd, other_f, own_f)
    odd_f = jnp.where(odd, own_f, other_f)
    step_decay = decays[0]
    total = (odd_f * mine(step_decay)) * mine(even_s) + mine(odd_s)
    flag = even_f * odd_f
    chips = peers // 2
    offset = 1
    while offset < chips:
        rung = offset.bit_length()
        load = jnp.concatenate([total, jnp.broadcast_to(flag, (pole_count, LANES))], axis=1)
        got = from_behind(load, "ctx", 2 * offset)
        total = total + (flag * mine(decays[rung])) * got[:, :half]
        flag = flag * got[:, half:half + 1]
        offset *= 2
    prefix = from_behind(total, "ctx", 2)
    partner = swap_cores(prefix, "ctx")
    full = jnp.where(odd, jnp.concatenate([partner, prefix], axis=1), jnp.concatenate([prefix, partner], axis=1))
    return jnp.where(odd, (even_f * step_decay) * full + even_s, full)


def on_device(qkv, doc_ids, short_w, rates, residues):
    length = qkv.shape[0]
    taps = short_w.shape[0]
    channels = qkv.shape[1] // 3
    filters, pole_count = rates.shape
    group_width = channels // filters
    width = min(WIDTH, channels)
    nb = channels // width
    gpb = width // group_width
    final_width = min(FINAL_WIDTH, channels)
    peers = lax.axis_size("ctx")
    me = lax.axis_index("ctx")

    tail_docs = jnp.broadcast_to(doc_ids[length - RIM:, None].astype(jnp.bfloat16), (RIM, LANES))
    rim = from_behind(jnp.concatenate([qkv[length - RIM:], tail_docs], axis=1), "ctx", 1)
    prev_docs = rim[:, 3 * channels].astype(jnp.int32)
    prev_last = prev_docs[RIM - 1]

    span_r = 2 * LANES
    e_vec = jnp.concatenate([doc_ids, prev_docs, jnp.full((span_r - length - RIM,), -1, jnp.int32)]).astype(jnp.float32)
    e_rows = jnp.broadcast_to(e_vec[None, :], (8, span_r))

    rates_t = rates.reshape(nb, gpb, pole_count).transpose(0, 2, 1)
    residues_t = residues.reshape(nb, gpb, pole_count).transpose(0, 2, 1)
    offsets = []
    while (1 << len(offsets)) < peers:
        offsets.append(1 << len(offsets))
    rounds = max(len(offsets), 1)
    spans = tuple(float(length * o) for o in offsets) or (float(length),)

    col = lambda off: (lambda j: (0, j + off))
    fixed = lambda j: (0, 0)
    q_part, local_part, packed, decays, info = pl.pallas_call(
        functools.partial(local_kernel, taps, group_width, spans),
        grid=(nb,),
        in_specs=[
            pl.BlockSpec((length, width), col(0)),
            pl.BlockSpec((length, width), col(nb)),
            pl.BlockSpec((length, width), col(2 * nb)),
            pl.BlockSpec((RIM, width), col(0)),
            pl.BlockSpec((RIM, width), col(nb)),
            pl.BlockSpec((RIM, width), col(2 * nb)),
            pl.BlockSpec((taps, width), col(0)),
            pl.BlockSpec((taps, width), col(nb)),
            pl.BlockSpec((taps, width), col(2 * nb)),
            pl.BlockSpec((8, span_r), fixed),
            pl.BlockSpec((1, pole_count, gpb), lambda j: (j, 0, 0)),
            pl.BlockSpec((1, pole_count, gpb), lambda j: (j, 0, 0)),
        ],
        out_specs=[
            pl.BlockSpec((length, width), col(0)),
            pl.BlockSpec((length, width), col(0)),
            pl.BlockSpec((pole_count, channels + LANES), fixed),
            pl.BlockSpec((rounds, pole_count, width), lambda j: (0, 0, j)),
            pl.BlockSpec((length, LANES), fixed),
        ],
        out_shape=[
            jax.ShapeDtypeStruct((length, channels), jnp.float32),
            jax.ShapeDtypeStruct((length, channels), jnp.float32),
            jax.ShapeDtypeStruct((pole_count, channels + LANES), jnp.float32),
            jax.ShapeDtypeStruct((rounds, pole_count, channels), jnp.float32),
            jax.ShapeDtypeStruct((length, LANES), jnp.float32),
        ],
        scratch_shapes=[
            pltpu.VMEM((span_r, width), jnp.bfloat16),
            pltpu.VMEM((taps * length, span_r), jnp.bfloat16),
            pltpu.VMEM((length, length), jnp.float32),
            pltpu.VMEM((8, length), jnp.float32),
        ],
        compiler_params=pltpu.CompilerParams(dimension_semantics=("arbitrary",)),
    )(qkv, qkv, qkv, rim, rim, rim, short_w, short_w, short_w, e_rows, rates_t, residues_t)

    before = chip_scan(packed, decays, channels, pole_count, peers, me)

    nbf = channels // final_width
    return pl.pallas_call(
        functools.partial(final_kernel, group_width, pole_count, width),
        grid=(nbf,),
        in_specs=[
            pl.BlockSpec((length, final_width), col(0)),
            pl.BlockSpec((length, final_width), col(0)),
            pl.BlockSpec((pole_count, final_width), col(0)),
            pl.BlockSpec((1, final_width // group_width * pole_count), col(0)),
            pl.BlockSpec((1, final_width // group_width * pole_count), col(0)),
            pl.BlockSpec((length, LANES), fixed),
        ],
        out_specs=pl.BlockSpec((length, final_width), col(0)),
        out_shape=jax.ShapeDtypeStruct((length, channels), jnp.bfloat16),
        compiler_params=pltpu.CompilerParams(dimension_semantics=("arbitrary",)),
    )(q_part, local_part, before, rates.reshape(1, filters * pole_count),
      residues.reshape(1, filters * pole_count), info)


def solution(mesh):
    return jax.shard_map(
        on_device,
        mesh=mesh,
        in_specs=(P(("groups", "ctx"), None), P(("groups", "ctx")), P(), P(), P()),
        out_specs=P(("groups", "ctx"), None),
        check_vma=False,
    )
```

```python
import functools

import jax
import jax.numpy as jnp
from jax import lax
from jax.experimental import pallas as pl
from jax.experimental.pallas import tpu as pltpu
from jax.sharding import PartitionSpec as P

WIDTH = 256
FINAL_WIDTH = 1024
RIM = 8
LANES = 128


def from_behind(shard, axis, by):
    peers = lax.axis_size(axis)
    pairs = [(i, i + by) for i in range(peers) if 0 <= i + by < peers]
    return lax.ppermute(shard, axis, pairs)


def split2(x):
    hi = x.astype(jnp.bfloat16)
    lo = (x - hi.astype(jnp.float32)).astype(jnp.bfloat16)
    return hi, lo


def split3(x):
    hi = x.astype(jnp.bfloat16)
    rest = x - hi.astype(jnp.float32)
    mid = rest.astype(jnp.bfloat16)
    lo = (rest - mid.astype(jnp.float32)).astype(jnp.bfloat16)
    return hi, mid, lo


def local_kernel(taps, group_width, spans,
                 xq, xk, xv, rq, rk, rv, wq, wk, wv, e_ref, rt_ref, et_ref,
                 q_out, loc_out, pk_out, dec_out, info_out, ext_s, shift_s, vis_s, tail_s):
    length, width = xq.shape
    groups = width // group_width
    pole_count = rt_ref.shape[1]
    channels = pk_out.shape[1] - LANES
    span_r = e_ref.shape[1]
    step = pl.program_id(0)

    @pl.when(step == 0)
    def _():
        e_row = e_ref[0:1, :]
        t_col = lax.broadcasted_iota(jnp.int32, (length, span_r), 0)
        r_row = lax.broadcasted_iota(jnp.int32, (length, span_r), 1)
        doc_col = jnp.sum(jnp.where(r_row == t_col, e_row, 0.0), axis=1, keepdims=True)
        eq = e_row == doc_col
        place = jnp.where(r_row < length, r_row, r_row - length - RIM)
        for j in range(taps):
            hit = eq & (place == t_col - j) & (r_row < length + RIM)
            shift_s[j * length:(j + 1) * length, :] = jnp.where(hit, 1.0, 0.0).astype(jnp.bfloat16)
        eqf = jnp.where(eq, 1.0, 0.0)
        causal = r_row[:, :length] <= t_col[:, :length]
        vis_s[...] = jnp.where(causal, eqf[:, :length], 0.0)
        tail_s[...] = jnp.broadcast_to(eqf[length - 1:length, :length], tail_s.shape)
        into = eqf[0:1, length + RIM - 1:length + RIM]
        flag = into * eqf[length - 1:length, 0:1]
        pk_out[:, channels:channels + LANES] = jnp.broadcast_to(flag, (pole_count, LANES))
        lane = lax.broadcasted_iota(jnp.int32, info_out.shape, 1)
        info_out[...] = jnp.where(lane == 0, eqf[:, 0:1], jnp.broadcast_to(into, info_out.shape))
        ext_s[...] = jnp.zeros_like(ext_s)

    shifts = shift_s[...]

    def conv(x_ref, r_ref, w_ref):
        ext_s[0:length, :] = x_ref[...]
        ext_s[length:length + RIM, :] = r_ref[...]
        windows = jnp.dot(shifts, ext_s[...], preferred_element_type=jnp.float32)
        w = w_ref[...]
        acc = w[0:1, :] * windows[0:length]
        for j in range(1, taps):
            acc = acc + w[j:j + 1, :] * windows[j * length:(j + 1) * length]
        return acc

    cq = conv(xq, rq, wq)
    ck = conv(xk, rk, wk)
    cv = conv(xv, rv, wv)
    q_out[...] = cq
    gated = (ck * cv).astype(jnp.bfloat16)

    lane_group = lax.broadcasted_iota(jnp.int32, (length, width), 1) // group_width
    zero = jnp.zeros_like(gated)
    xbd = jnp.concatenate([jnp.where(lane_group == g, gated, zero) for g in range(groups)], axis=0)

    rt = rt_ref[0]
    et = et_ref[0]
    lane = lax.broadcasted_iota(jnp.int32, (1, length), 1)
    lags = ((length - lane) % length).astype(jnp.float32)
    to_end = (length - 1 - lane).astype(jnp.float32)
    at_tail = tail_s[0:1, :]
    visible = vis_s[...] > 0.5
    pieces = []
    ends = []
    for g in range(groups):
        a_col = rt[:, g:g + 1]
        r_col = et[:, g:g + 1]
        base = jnp.sum(r_col * jnp.exp(-a_col * lags), axis=0, keepdims=True)
        row = jnp.broadcast_to(base, (length, length))
        rolled = pltpu.roll(row, 0, 1, stride=1, stride_axis=0)
        pieces.append(jnp.where(visible, rolled, 0.0))
        ends.append(jnp.exp(-a_col * to_end) * at_tail)
    lhs = jnp.concatenate([jnp.concatenate(pieces, axis=1), jnp.concatenate(ends, axis=1)], axis=0)
    l_hi, l_lo = split2(lhs)
    rows = length + pole_count
    res = jnp.dot(jnp.concatenate([l_hi, l_lo], axis=0), xbd, preferred_element_type=jnp.float32)
    loc_out[...] = res[0:length] + res[rows:rows + length]
    st = res[length:rows] + res[rows + length:2 * rows]
    pk_out[:, pl.ds(pl.multiple_of(step * width, width), width)] = st

    spread = (lax.broadcasted_iota(jnp.int32, (groups, width), 1) // group_width
              == lax.broadcasted_iota(jnp.int32, (groups, width), 0)).astype(jnp.bfloat16)
    rate_cols = None
    for piece in split3(rt):
        part = jnp.dot(piece, spread, preferred_element_type=jnp.float32)
        rate_cols = part if rate_cols is None else rate_cols + part
    for r, span in enumerate(spans):
        dec_out[r] = jnp.exp(-rate_cols * span)


def final_kernel(group_width, pole_count, sub, q_ref, loc_ref, b_ref, rf_ref, ef_ref, info_ref, o_ref):
    length, width = q_ref.shape
    groups = sub // group_width
    tcol = (lax.broadcasted_iota(jnp.int32, (length, 1), 0) + 1).astype(jnp.float32)
    iw = ef_ref[...] * jnp.exp(-rf_ref[...] * tcol) * info_ref[:, 0:1]
    iw_hi, iw_lo = split2(iw)
    b_all = b_ref[...] * info_ref[0:1, 1:2]
    shape = (groups * pole_count, sub)
    row_group = lax.broadcasted_iota(jnp.int32, shape, 0) // pole_count
    lane_group = lax.broadcasted_iota(jnp.int32, shape, 1) // group_width
    same = row_group == lane_group
    for s in range(width // sub):
        cols = slice(s * sub, (s + 1) * sub)
        tiled = jnp.concatenate([b_all[:, cols]] * groups, axis=0)
        b_hi, b_lo = split2(jnp.where(same, tiled, 0.0))
        poles = slice(s * shape[0], (s + 1) * shape[0])
        ih = iw_hi[:, poles]
        car = jnp.dot(ih, b_hi, preferred_element_type=jnp.float32)
        car = car + jnp.dot(ih, b_lo, preferred_element_type=jnp.float32)
        car = car + jnp.dot(iw_lo[:, poles], b_hi, preferred_element_type=jnp.float32)
        o_ref[:, cols] = (q_ref[:, cols] * (loc_ref[:, cols] + car)).astype(o_ref.dtype)


def swap_cores(shard, axis):
    peers = lax.axis_size(axis)
    return lax.ppermute(shard, axis, [(i, i ^ 1) for i in range(peers)])


def chip_scan(packed, decays, channels, pole_count, peers, me):
    core = me % 2
    odd = core == 1
    half = channels // 2
    mine = lambda x: lax.dynamic_slice_in_dim(x, core * half, half, axis=1)
    got = swap_cores(packed, "ctx")
    own_s, own_f = packed[:, :channels], packed[:, channels:channels + 1]
    other_s, other_f = got[:, :channels], got[:, channels:channels + 1]
    even_s = jnp.where(odd, other_s, own_s)
    odd_s = jnp.where(odd, own_s, other_s)
    even_f = jnp.where(odd, other_f, own_f)
    odd_f = jnp.where(odd, own_f, other_f)
    step_decay = decays[0]
    total = (odd_f * mine(step_decay)) * mine(even_s) + mine(odd_s)
    flag = even_f * odd_f
    chips = peers // 2
    load = jnp.concatenate([total, jnp.broadcast_to(flag, (pole_count, LANES))], axis=1)
    every = lax.all_gather(load, "ctx")
    chip = me // 2
    two_step = decays[1]
    halves = []
    for side in range(2):
        decay_half = two_step[:, side * half:(side + 1) * half]
        acc = jnp.zeros((pole_count, half), jnp.float32)
        for earlier in range(chips):
            part = every[2 * earlier + side]
            carry = (part[:, half:half + 1] * decay_half) * acc + part[:, :half]
            acc = jnp.where(earlier < chip, carry, acc)
        halves.append(acc)
    full = jnp.concatenate(halves, axis=1)
    return jnp.where(odd, (even_f * step_decay) * full + even_s, full)


def on_device(qkv, doc_ids, short_w, rates, residues):
    length = qkv.shape[0]
    taps = short_w.shape[0]
    channels = qkv.shape[1] // 3
    filters, pole_count = rates.shape
    group_width = channels // filters
    width = min(WIDTH, channels)
    nb = channels // width
    gpb = width // group_width
    final_width = min(FINAL_WIDTH, channels)
    peers = lax.axis_size("ctx")
    me = lax.axis_index("ctx")

    tail_docs = jnp.broadcast_to(doc_ids[length - RIM:, None].astype(jnp.bfloat16), (RIM, LANES))
    rim = from_behind(jnp.concatenate([qkv[length - RIM:], tail_docs], axis=1), "ctx", 1)
    prev_docs = rim[:, 3 * channels].astype(jnp.int32)
    prev_last = prev_docs[RIM - 1]

    span_r = 2 * LANES
    e_vec = jnp.concatenate([doc_ids, prev_docs, jnp.full((span_r - length - RIM,), -1, jnp.int32)]).astype(jnp.float32)
    e_rows = jnp.broadcast_to(e_vec[None, :], (8, span_r))

    rates_t = rates.reshape(nb, gpb, pole_count).transpose(0, 2, 1)
    residues_t = residues.reshape(nb, gpb, pole_count).transpose(0, 2, 1)
    offsets = []
    while (1 << len(offsets)) < peers:
        offsets.append(1 << len(offsets))
    rounds = max(len(offsets), 1)
    spans = tuple(float(length * o) for o in offsets) or (float(length),)

    col = lambda off: (lambda j: (0, j + off))
    fixed = lambda j: (0, 0)
    q_part, local_part, packed, decays, info = pl.pallas_call(
        functools.partial(local_kernel, taps, group_width, spans),
        grid=(nb,),
        in_specs=[
            pl.BlockSpec((length, width), col(0)),
            pl.BlockSpec((length, width), col(nb)),
            pl.BlockSpec((length, width), col(2 * nb)),
            pl.BlockSpec((RIM, width), col(0)),
            pl.BlockSpec((RIM, width), col(nb)),
            pl.BlockSpec((RIM, width), col(2 * nb)),
            pl.BlockSpec((taps, width), col(0)),
            pl.BlockSpec((taps, width), col(nb)),
            pl.BlockSpec((taps, width), col(2 * nb)),
            pl.BlockSpec((8, span_r), fixed),
            pl.BlockSpec((1, pole_count, gpb), lambda j: (j, 0, 0)),
            pl.BlockSpec((1, pole_count, gpb), lambda j: (j, 0, 0)),
        ],
        out_specs=[
            pl.BlockSpec((length, width), col(0)),
            pl.BlockSpec((length, width), col(0)),
            pl.BlockSpec((pole_count, channels + LANES), fixed),
            pl.BlockSpec((rounds, pole_count, width), lambda j: (0, 0, j)),
            pl.BlockSpec((length, LANES), fixed),
        ],
        out_shape=[
            jax.ShapeDtypeStruct((length, channels), jnp.float32),
            jax.ShapeDtypeStruct((length, channels), jnp.float32),
            jax.ShapeDtypeStruct((pole_count, channels + LANES), jnp.float32),
            jax.ShapeDtypeStruct((rounds, pole_count, channels), jnp.float32),
            jax.ShapeDtypeStruct((length, LANES), jnp.float32),
        ],
        scratch_shapes=[
            pltpu.VMEM((span_r, width), jnp.bfloat16),
            pltpu.VMEM((taps * length, span_r), jnp.bfloat16),
            pltpu.VMEM((length, length), jnp.float32),
            pltpu.VMEM((8, length), jnp.float32),
        ],
        compiler_params=pltpu.CompilerParams(dimension_semantics=("arbitrary",)),
    )(qkv, qkv, qkv, rim, rim, rim, short_w, short_w, short_w, e_rows, rates_t, residues_t)

    before = chip_scan(packed, decays, channels, pole_count, peers, me)

    nbf = channels // final_width
    return pl.pallas_call(
        functools.partial(final_kernel, group_width, pole_count, width),
        grid=(nbf,),
        in_specs=[
            pl.BlockSpec((length, final_width), col(0)),
            pl.BlockSpec((length, final_width), col(0)),
            pl.BlockSpec((pole_count, final_width), col(0)),
            pl.BlockSpec((1, final_width // group_width * pole_count), col(0)),
            pl.BlockSpec((1, final_width // group_width * pole_count), col(0)),
            pl.BlockSpec((length, LANES), fixed),
        ],
        out_specs=pl.BlockSpec((length, final_width), col(0)),
        out_shape=jax.ShapeDtypeStruct((length, channels), jnp.bfloat16),
        compiler_params=pltpu.CompilerParams(dimension_semantics=("arbitrary",)),
    )(q_part, local_part, before, rates.reshape(1, filters * pole_count),
      residues.reshape(1, filters * pole_count), info)


def solution(mesh):
    return jax.shard_map(
        on_device,
        mesh=mesh,
        in_specs=(P(("groups", "ctx"), None), P(("groups", "ctx")), P(), P(), P()),
        out_specs=P(("groups", "ctx"), None),
        check_vma=False,
    )
```

```python
import functools

import jax
import jax.numpy as jnp
from jax import lax
from jax.experimental import pallas as pl
from jax.experimental.pallas import tpu as pltpu
from jax.sharding import PartitionSpec as P

WIDTH = 256
FINAL_WIDTH = 1024
RIM = 8
LANES = 128


def from_behind(shard, axis, by):
    peers = lax.axis_size(axis)
    pairs = [(i, i + by) for i in range(peers) if 0 <= i + by < peers]
    return lax.ppermute(shard, axis, pairs)


def split2(x):
    hi = x.astype(jnp.bfloat16)
    lo = (x - hi.astype(jnp.float32)).astype(jnp.bfloat16)
    return hi, lo


def split3(x):
    hi = x.astype(jnp.bfloat16)
    rest = x - hi.astype(jnp.float32)
    mid = rest.astype(jnp.bfloat16)
    lo = (rest - mid.astype(jnp.float32)).astype(jnp.bfloat16)
    return hi, mid, lo


def local_kernel(taps, group_width, spans,
                 xq, xk, xv, rq, rk, rv, wq, wk, wv, e_ref, rt_ref, et_ref,
                 q_out, loc_out, pk_out, dec_out, info_out, ext_s, shift_s, vis_s, tail_s):
    length, width = xq.shape
    groups = width // group_width
    pole_count = rt_ref.shape[1]
    channels = pk_out.shape[1] - LANES
    span_r = e_ref.shape[1]
    step = pl.program_id(0)

    @pl.when(step == 0)
    def _():
        e_row = e_ref[0:1, :]
        t_col = lax.broadcasted_iota(jnp.int32, (length, span_r), 0)
        r_row = lax.broadcasted_iota(jnp.int32, (length, span_r), 1)
        doc_col = jnp.sum(jnp.where(r_row == t_col, e_row, 0.0), axis=1, keepdims=True)
        eq = e_row == doc_col
        place = jnp.where(r_row < length, r_row, r_row - length - RIM)
        for j in range(taps):
            hit = eq & (place == t_col - j) & (r_row < length + RIM)
            shift_s[j * length:(j + 1) * length, :] = jnp.where(hit, 1.0, 0.0).astype(jnp.bfloat16)
        eqf = jnp.where(eq, 1.0, 0.0)
        causal = r_row[:, :length] <= t_col[:, :length]
        vis_s[...] = jnp.where(causal, eqf[:, :length], 0.0)
        tail_s[...] = jnp.broadcast_to(eqf[length - 1:length, :length], tail_s.shape)
        into = eqf[0:1, length + RIM - 1:length + RIM]
        flag = into * eqf[length - 1:length, 0:1]
        pk_out[:, channels:channels + LANES] = jnp.broadcast_to(flag, (pole_count, LANES))
        lane = lax.broadcasted_iota(jnp.int32, info_out.shape, 1)
        info_out[...] = jnp.where(lane == 0, eqf[:, 0:1], jnp.broadcast_to(into, info_out.shape))
        ext_s[...] = jnp.zeros_like(ext_s)

    shifts = shift_s[...]

    def conv(x_ref, r_ref, w_ref):
        ext_s[0:length, :] = x_ref[...]
        ext_s[length:length + RIM, :] = r_ref[...]
        windows = jnp.dot(shifts, ext_s[...], preferred_element_type=jnp.float32)
        w = w_ref[...]
        acc = w[0:1, :] * windows[0:length]
        for j in range(1, taps):
            acc = acc + w[j:j + 1, :] * windows[j * length:(j + 1) * length]
        return acc

    cq = conv(xq, rq, wq)
    ck = conv(xk, rk, wk)
    cv = conv(xv, rv, wv)
    q_out[...] = cq
    gated = (ck * cv).astype(jnp.bfloat16)

    lane_group = lax.broadcasted_iota(jnp.int32, (length, width), 1) // group_width
    zero = jnp.zeros_like(gated)
    xbd = jnp.concatenate([jnp.where(lane_group == g, gated, zero) for g in range(groups)], axis=0)

    rt = rt_ref[0]
    et = et_ref[0]
    lane = lax.broadcasted_iota(jnp.int32, (1, length), 1)
    lags = ((length - lane) % length).astype(jnp.float32)
    to_end = (length - 1 - lane).astype(jnp.float32)
    at_tail = tail_s[0:1, :]
    visible = vis_s[...] > 0.5
    pieces = []
    ends = []
    for g in range(groups):
        a_col = rt[:, g:g + 1]
        r_col = et[:, g:g + 1]
        base = jnp.sum(r_col * jnp.exp(-a_col * lags), axis=0, keepdims=True)
        row = jnp.broadcast_to(base, (length, length))
        rolled = pltpu.roll(row, 0, 1, stride=1, stride_axis=0)
        pieces.append(jnp.where(visible, rolled, 0.0))
        ends.append(jnp.exp(-a_col * to_end) * at_tail)
    e_hi, e_lo = split2(jnp.concatenate(ends, axis=1))
    t_hi = jnp.concatenate(pieces, axis=1).astype(jnp.bfloat16)
    res = jnp.dot(jnp.concatenate([t_hi, e_hi, e_lo], axis=0), xbd, preferred_element_type=jnp.float32)
    loc_out[...] = res[0:length]
    st = res[length:length + pole_count] + res[length + pole_count:length + 2 * pole_count]
    pk_out[:, pl.ds(pl.multiple_of(step * width, width), width)] = st

    spread = (lax.broadcasted_iota(jnp.int32, (groups, width), 1) // group_width
              == lax.broadcasted_iota(jnp.int32, (groups, width), 0)).astype(jnp.bfloat16)
    rate_cols = None
    for piece in split3(rt):
        part = jnp.dot(piece, spread, preferred_element_type=jnp.float32)
        rate_cols = part if rate_cols is None else rate_cols + part
    for r, span in enumerate(spans):
        dec_out[r] = jnp.exp(-rate_cols * span)


def final_kernel(group_width, pole_count, sub, q_ref, loc_ref, b_ref, rf_ref, ef_ref, info_ref, o_ref):
    length, width = q_ref.shape
    groups = sub // group_width
    tcol = (lax.broadcasted_iota(jnp.int32, (length, 1), 0) + 1).astype(jnp.float32)
    iw = ef_ref[...] * jnp.exp(-rf_ref[...] * tcol) * info_ref[:, 0:1]
    iw_hi, iw_lo = split2(iw)
    b_all = b_ref[...] * info_ref[0:1, 1:2]
    shape = (groups * pole_count, sub)
    row_group = lax.broadcasted_iota(jnp.int32, shape, 0) // pole_count
    lane_group = lax.broadcasted_iota(jnp.int32, shape, 1) // group_width
    same = row_group == lane_group
    for s in range(width // sub):
        cols = slice(s * sub, (s + 1) * sub)
        tiled = jnp.concatenate([b_all[:, cols]] * groups, axis=0)
        b_hi, b_lo = split2(jnp.where(same, tiled, 0.0))
        poles = slice(s * shape[0], (s + 1) * shape[0])
        ih = iw_hi[:, poles]
        car = jnp.dot(ih, b_hi, preferred_element_type=jnp.float32)
        car = car + jnp.dot(ih, b_lo, preferred_element_type=jnp.float32)
        car = car + jnp.dot(iw_lo[:, poles], b_hi, preferred_element_type=jnp.float32)
        o_ref[:, cols] = (q_ref[:, cols] * (loc_ref[:, cols] + car)).astype(o_ref.dtype)


def swap_cores(shard, axis):
    peers = lax.axis_size(axis)
    return lax.ppermute(shard, axis, [(i, i ^ 1) for i in range(peers)])


def chip_scan(packed, decays, channels, pole_count, peers, me):
    core = me % 2
    odd = core == 1
    half = channels // 2
    mine = lambda x: lax.dynamic_slice_in_dim(x, core * half, half, axis=1)
    got = swap_cores(packed, "ctx")
    own_s, own_f = packed[:, :channels], packed[:, channels:channels + 1]
    other_s, other_f = got[:, :channels], got[:, channels:channels + 1]
    even_s = jnp.where(odd, other_s, own_s)
    odd_s = jnp.where(odd, own_s, other_s)
    even_f = jnp.where(odd, other_f, own_f)
    odd_f = jnp.where(odd, own_f, other_f)
    step_decay = decays[0]
    total = (odd_f * mine(step_decay)) * mine(even_s) + mine(odd_s)
    flag = even_f * odd_f
    chips = peers // 2
    offset = 1
    while offset < chips:
        rung = offset.bit_length()
        load = jnp.concatenate([total, jnp.broadcast_to(flag, (pole_count, LANES))], axis=1)
        got = from_behind(load, "ctx", 2 * offset)
        total = total + (flag * mine(decays[rung])) * got[:, :half]
        flag = flag * got[:, half:half + 1]
        offset *= 2
    prefix = from_behind(total, "ctx", 2)
    partner = lax.ppermute(total, "ctx", [(i, (i ^ 1) + 2) for i in range(peers - 2)])
    full = jnp.where(odd, jnp.concatenate([partner, prefix], axis=1), jnp.concatenate([prefix, partner], axis=1))
    return jnp.where(odd, (even_f * step_decay) * full + even_s, full)


def on_device(qkv, doc_ids, short_w, rates, residues):
    length = qkv.shape[0]
    taps = short_w.shape[0]
    channels = qkv.shape[1] // 3
    filters, pole_count = rates.shape
    group_width = channels // filters
    width = min(WIDTH, channels)
    nb = channels // width
    gpb = width // group_width
    final_width = min(FINAL_WIDTH, channels)
    peers = lax.axis_size("ctx")
    me = lax.axis_index("ctx")

    tail_docs = jnp.broadcast_to(doc_ids[length - RIM:, None].astype(jnp.bfloat16), (RIM, LANES))
    rim = from_behind(jnp.concatenate([qkv[length - RIM:], tail_docs], axis=1), "ctx", 1)
    prev_docs = rim[:, 3 * channels].astype(jnp.int32)
    prev_last = prev_docs[RIM - 1]

    span_r = 2 * LANES
    e_vec = jnp.concatenate([doc_ids, prev_docs, jnp.full((span_r - length - RIM,), -1, jnp.int32)]).astype(jnp.float32)
    e_rows = jnp.broadcast_to(e_vec[None, :], (8, span_r))

    both_t = jnp.stack([rates, residues]).reshape(2, nb, gpb, pole_count).transpose(0, 1, 3, 2)
    rates_t, residues_t = both_t[0], both_t[1]
    offsets = []
    while (1 << len(offsets)) < peers:
        offsets.append(1 << len(offsets))
    rounds = max(len(offsets), 1)
    spans = tuple(float(length * o) for o in offsets) or (float(length),)

    col = lambda off: (lambda j: (0, j + off))
    fixed = lambda j: (0, 0)
    q_part, local_part, packed, decays, info = pl.pallas_call(
        functools.partial(local_kernel, taps, group_width, spans),
        grid=(nb,),
        in_specs=[
            pl.BlockSpec((length, width), col(0)),
            pl.BlockSpec((length, width), col(nb)),
            pl.BlockSpec((length, width), col(2 * nb)),
            pl.BlockSpec((RIM, width), col(0)),
            pl.BlockSpec((RIM, width), col(nb)),
            pl.BlockSpec((RIM, width), col(2 * nb)),
            pl.BlockSpec((taps, width), col(0)),
            pl.BlockSpec((taps, width), col(nb)),
            pl.BlockSpec((taps, width), col(2 * nb)),
            pl.BlockSpec((8, span_r), fixed),
            pl.BlockSpec((1, pole_count, gpb), lambda j: (j, 0, 0)),
            pl.BlockSpec((1, pole_count, gpb), lambda j: (j, 0, 0)),
        ],
        out_specs=[
            pl.BlockSpec((length, width), col(0)),
            pl.BlockSpec((length, width), col(0)),
            pl.BlockSpec((pole_count, channels + LANES), fixed),
            pl.BlockSpec((rounds, pole_count, width), lambda j: (0, 0, j)),
            pl.BlockSpec((length, LANES), fixed),
        ],
        out_shape=[
            jax.ShapeDtypeStruct((length, channels), jnp.float32),
            jax.ShapeDtypeStruct((length, channels), jnp.float32),
            jax.ShapeDtypeStruct((pole_count, channels + LANES), jnp.float32),
            jax.ShapeDtypeStruct((rounds, pole_count, channels), jnp.float32),
            jax.ShapeDtypeStruct((length, LANES), jnp.float32),
        ],
        scratch_shapes=[
            pltpu.VMEM((span_r, width), jnp.bfloat16),
            pltpu.VMEM((taps * length, span_r), jnp.bfloat16),
            pltpu.VMEM((length, length), jnp.float32),
            pltpu.VMEM((8, length), jnp.float32),
        ],
        compiler_params=pltpu.CompilerParams(dimension_semantics=("arbitrary",)),
    )(qkv, qkv, qkv, rim, rim, rim, short_w, short_w, short_w, e_rows, rates_t, residues_t)

    before = chip_scan(packed, decays, channels, pole_count, peers, me)

    nbf = channels // final_width
    return pl.pallas_call(
        functools.partial(final_kernel, group_width, pole_count, width),
        grid=(nbf,),
        in_specs=[
            pl.BlockSpec((length, final_width), col(0)),
            pl.BlockSpec((length, final_width), col(0)),
            pl.BlockSpec((pole_count, final_width), col(0)),
            pl.BlockSpec((1, final_width // group_width * pole_count), col(0)),
            pl.BlockSpec((1, final_width // group_width * pole_count), col(0)),
            pl.BlockSpec((length, LANES), fixed),
        ],
        out_specs=pl.BlockSpec((length, final_width), col(0)),
        out_shape=jax.ShapeDtypeStruct((length, channels), jnp.bfloat16),
        compiler_params=pltpu.CompilerParams(dimension_semantics=("arbitrary",)),
    )(q_part, local_part, before, rates.reshape(1, filters * pole_count),
      residues.reshape(1, filters * pole_count), info)


def solution(mesh):
    return jax.shard_map(
        on_device,
        mesh=mesh,
        in_specs=(P(("groups", "ctx"), None), P(("groups", "ctx")), P(), P(), P()),
        out_specs=P(("groups", "ctx"), None),
        check_vma=False,
    )
```

```python
import functools

import jax
import jax.numpy as jnp
from jax import lax
from jax.experimental import pallas as pl
from jax.experimental.pallas import tpu as pltpu
from jax.sharding import PartitionSpec as P

WIDTH = 256
FINAL_WIDTH = 1024
RIM = 8
LANES = 128


def from_behind(shard, axis, by):
    peers = lax.axis_size(axis)
    pairs = [(i, i + by) for i in range(peers) if 0 <= i + by < peers]
    return lax.ppermute(shard, axis, pairs)


def split2(x):
    hi = x.astype(jnp.bfloat16)
    lo = (x - hi.astype(jnp.float32)).astype(jnp.bfloat16)
    return hi, lo


def split3(x):
    hi = x.astype(jnp.bfloat16)
    rest = x - hi.astype(jnp.float32)
    mid = rest.astype(jnp.bfloat16)
    lo = (rest - mid.astype(jnp.float32)).astype(jnp.bfloat16)
    return hi, mid, lo


def local_kernel(taps, group_width, spans,
                 xq, xk, xv, rq, rk, rv, wq, wk, wv, e_ref, rt_ref, et_ref,
                 q_out, loc_out, pk_out, dec_out, info_out, ext_s, shift_s, vis_s, tail_s):
    length, width = xq.shape
    groups = width // group_width
    pole_count = rt_ref.shape[1]
    channels = pk_out.shape[1] - LANES
    span_r = e_ref.shape[1]
    step = pl.program_id(0)

    @pl.when(step == 0)
    def _():
        e_row = e_ref[0:1, :]
        t_col = lax.broadcasted_iota(jnp.int32, (length, span_r), 0)
        r_row = lax.broadcasted_iota(jnp.int32, (length, span_r), 1)
        doc_col = jnp.sum(jnp.where(r_row == t_col, e_row, 0.0), axis=1, keepdims=True)
        eq = e_row == doc_col
        place = jnp.where(r_row < length, r_row, r_row - length - RIM)
        for j in range(taps):
            hit = eq & (place == t_col - j) & (r_row < length + RIM)
            shift_s[j * length:(j + 1) * length, :] = jnp.where(hit, 1.0, 0.0).astype(jnp.bfloat16)
        eqf = jnp.where(eq, 1.0, 0.0)
        causal = r_row[:, :length] <= t_col[:, :length]
        vis_s[...] = jnp.where(causal, eqf[:, :length], 0.0)
        tail_s[...] = jnp.broadcast_to(eqf[length - 1:length, :length], tail_s.shape)
        into = eqf[0:1, length + RIM - 1:length + RIM]
        flag = into * eqf[length - 1:length, 0:1]
        pk_out[:, channels:channels + LANES] = jnp.broadcast_to(flag, (pole_count, LANES))
        lane = lax.broadcasted_iota(jnp.int32, info_out.shape, 1)
        info_out[...] = jnp.where(lane == 0, eqf[:, 0:1], jnp.broadcast_to(into, info_out.shape))
        ext_s[...] = jnp.zeros_like(ext_s)

    shifts = shift_s[...]

    def conv(x_ref, r_ref, w_ref):
        ext_s[0:length, :] = x_ref[...]
        ext_s[length:length + RIM, :] = r_ref[...]
        windows = jnp.dot(shifts, ext_s[...], preferred_element_type=jnp.float32)
        w = w_ref[...]
        acc = w[0:1, :] * windows[0:length]
        for j in range(1, taps):
            acc = acc + w[j:j + 1, :] * windows[j * length:(j + 1) * length]
        return acc

    cq = conv(xq, rq, wq)
    ck = conv(xk, rk, wk)
    cv = conv(xv, rv, wv)
    q_out[...] = cq
    gated = (ck * cv).astype(jnp.bfloat16)

    lane_group = lax.broadcasted_iota(jnp.int32, (length, width), 1) // group_width
    zero = jnp.zeros_like(gated)
    xbd = jnp.concatenate([jnp.where(lane_group == g, gated, zero) for g in range(groups)], axis=0)

    rt = rt_ref[0]
    et = et_ref[0]
    lane = lax.broadcasted_iota(jnp.int32, (1, length), 1)
    lags = ((length - lane) % length).astype(jnp.float32)
    to_end = (length - 1 - lane).astype(jnp.float32)
    at_tail = tail_s[0:1, :]
    visible = vis_s[...] > 0.5
    pieces = []
    ends = []
    for g in range(groups):
        a_col = rt[:, g:g + 1]
        r_col = et[:, g:g + 1]
        base = jnp.sum(r_col * jnp.exp(-a_col * lags), axis=0, keepdims=True)
        row = jnp.broadcast_to(base, (length, length))
        rolled = pltpu.roll(row, 0, 1, stride=1, stride_axis=0)
        pieces.append(jnp.where(visible, rolled, 0.0))
        ends.append(jnp.exp(-a_col * to_end) * at_tail)
    e_hi, e_lo = split2(jnp.concatenate(ends, axis=1))
    t_hi = jnp.concatenate(pieces, axis=1).astype(jnp.bfloat16)
    res = jnp.dot(jnp.concatenate([t_hi, e_hi, e_lo], axis=0), xbd, preferred_element_type=jnp.float32)
    loc_out[...] = res[0:length]
    st = res[length:length + pole_count] + res[length + pole_count:length + 2 * pole_count]
    pk_out[:, pl.ds(pl.multiple_of(step * width, width), width)] = st

    spread = (lax.broadcasted_iota(jnp.int32, (groups, width), 1) // group_width
              == lax.broadcasted_iota(jnp.int32, (groups, width), 0)).astype(jnp.bfloat16)
    rate_cols = None
    for piece in split3(rt):
        part = jnp.dot(piece, spread, preferred_element_type=jnp.float32)
        rate_cols = part if rate_cols is None else rate_cols + part
    for r, span in enumerate(spans):
        dec_out[r] = jnp.exp(-rate_cols * span)


def final_kernel(group_width, pole_count, sub, hb, q_ref, loc_ref, zo_ref, zp_ref, pk_ref, gt_ref, pf_ref, gf_ref,
                 d1_ref, rr_ref, info_ref, o_ref):
    length, width = q_ref.shape
    groups = sub // group_width
    core = lax.axis_index("ctx") % 2
    odd = core == 1
    mine_half = (pl.program_id(0) // hb) == core
    full = jnp.where(mine_half, zo_ref[...], zp_ref[...])
    even_s = jnp.where(odd, gt_ref[...], pk_ref[...])
    even_f = jnp.where(odd, gf_ref[:, 0:1], pf_ref[:, 0:1])
    joined = jnp.where(odd, (even_f * d1_ref[0]) * full + even_s, full)
    b_all = joined * info_ref[0:1, 1:2]
    tcol = (lax.broadcasted_iota(jnp.int32, (length, 1), 0) + 1).astype(jnp.float32)
    iw = rr_ref[1] * jnp.exp(-rr_ref[0] * tcol) * info_ref[:, 0:1]
    iw_hi, iw_lo = split2(iw)
    shape = (groups * pole_count, sub)
    row_group = lax.broadcasted_iota(jnp.int32, shape, 0) // pole_count
    lane_group = lax.broadcasted_iota(jnp.int32, shape, 1) // group_width
    same = row_group == lane_group
    for s in range(width // sub):
        cols = slice(s * sub, (s + 1) * sub)
        tiled = jnp.concatenate([b_all[:, cols]] * groups, axis=0)
        b_hi, b_lo = split2(jnp.where(same, tiled, 0.0))
        poles = slice(s * shape[0], (s + 1) * shape[0])
        ih = iw_hi[:, poles]
        car = jnp.dot(ih, b_hi, preferred_element_type=jnp.float32)
        car = car + jnp.dot(ih, b_lo, preferred_element_type=jnp.float32)
        car = car + jnp.dot(iw_lo[:, poles], b_hi, preferred_element_type=jnp.float32)
        o_ref[:, cols] = (q_ref[:, cols] * (loc_ref[:, cols] + car)).astype(o_ref.dtype)


def swap_cores(shard, axis):
    peers = lax.axis_size(axis)
    return lax.ppermute(shard, axis, [(i, i ^ 1) for i in range(peers)])


def chip_scan(packed, decays, span_of, channels, pole_count, peers, me):
    core = me % 2
    odd = core == 1
    half = channels // 2
    mine = lambda x: lax.dynamic_slice_in_dim(x, core * half, half, axis=1)
    got = swap_cores(packed, "ctx")
    own_s, own_f = packed[:, :channels], packed[:, channels:channels + 1]
    other_s, other_f = got[:, :channels], got[:, channels:channels + 1]
    even_s = jnp.where(odd, other_s, own_s)
    odd_s = jnp.where(odd, own_s, other_s)
    even_f = jnp.where(odd, other_f, own_f)
    odd_f = jnp.where(odd, own_f, other_f)
    total = (odd_f * mine(decays[span_of[1]])) * mine(even_s) + mine(odd_s)
    flag = even_f * odd_f
    chips = peers // 2
    prefix = jnp.zeros_like(total)
    prefix_flag = jnp.ones_like(flag)
    offset = 1
    while offset < chips:
        load = jnp.concatenate([total, jnp.broadcast_to(flag, (pole_count, LANES))], axis=1)
        got_load = from_behind(load, "ctx", 2 * offset)
        came, came_flag = got_load[:, :half], got_load[:, half:half + 1]
        if offset == 1:
            prefix = prefix + prefix_flag * came
        else:
            prefix = prefix + (prefix_flag * mine(decays[span_of[2 * offset - 2]])) * came
        prefix_flag = prefix_flag * came_flag
        if 2 * offset < chips:
            total = total + (flag * mine(decays[span_of[2 * offset]])) * came
            flag = flag * came_flag
        offset *= 2
    return prefix, swap_cores(prefix, "ctx"), got


def scan_spans(peers):
    chips = peers // 2
    spans = {1}
    offset = 1
    while offset < chips:
        if offset > 1:
            spans.add(2 * offset - 2)
        if 2 * offset < chips:
            spans.add(2 * offset)
        offset *= 2
    return sorted(spans)


def on_device(qkv, doc_ids, short_w, rates, residues):
    length = qkv.shape[0]
    taps = short_w.shape[0]
    channels = qkv.shape[1] // 3
    filters, pole_count = rates.shape
    group_width = channels // filters
    width = min(WIDTH, channels)
    nb = channels // width
    gpb = width // group_width
    final_width = min(FINAL_WIDTH, channels)
    peers = lax.axis_size("ctx")
    me = lax.axis_index("ctx")

    tail_docs = jnp.broadcast_to(doc_ids[length - RIM:, None].astype(jnp.bfloat16), (RIM, LANES))
    rim = from_behind(jnp.concatenate([qkv[length - RIM:], tail_docs], axis=1), "ctx", 1)
    prev_docs = rim[:, 3 * channels].astype(jnp.int32)
    prev_last = prev_docs[RIM - 1]

    span_r = 2 * LANES
    e_vec = jnp.concatenate([doc_ids, prev_docs, jnp.full((span_r - length - RIM,), -1, jnp.int32)]).astype(jnp.float32)
    e_rows = jnp.broadcast_to(e_vec[None, :], (8, span_r))

    both_t = jnp.stack([rates, residues]).reshape(2, nb, gpb, pole_count).transpose(0, 1, 3, 2)
    rates_t, residues_t = both_t[0], both_t[1]
    span_list = scan_spans(peers)
    span_of = {v: i for i, v in enumerate(span_list)}
    rounds = len(span_list)
    spans = tuple(float(length * v) for v in span_list)

    col = lambda off: (lambda j: (0, j + off))
    fixed = lambda j: (0, 0)
    q_part, local_part, packed, decays, info = pl.pallas_call(
        functools.partial(local_kernel, taps, group_width, spans),
        grid=(nb,),
        in_specs=[
            pl.BlockSpec((length, width), col(0)),
            pl.BlockSpec((length, width), col(nb)),
            pl.BlockSpec((length, width), col(2 * nb)),
            pl.BlockSpec((RIM, width), col(0)),
            pl.BlockSpec((RIM, width), col(nb)),
            pl.BlockSpec((RIM, width), col(2 * nb)),
            pl.BlockSpec((taps, width), col(0)),
            pl.BlockSpec((taps, width), col(nb)),
            pl.BlockSpec((taps, width), col(2 * nb)),
            pl.BlockSpec((8, span_r), fixed),
            pl.BlockSpec((1, pole_count, gpb), lambda j: (j, 0, 0)),
            pl.BlockSpec((1, pole_count, gpb), lambda j: (j, 0, 0)),
        ],
        out_specs=[
            pl.BlockSpec((length, width), col(0)),
            pl.BlockSpec((length, width), col(0)),
            pl.BlockSpec((pole_count, channels + LANES), fixed),
            pl.BlockSpec((rounds, pole_count, width), lambda j: (0, 0, j)),
            pl.BlockSpec((length, LANES), fixed),
        ],
        out_shape=[
            jax.ShapeDtypeStruct((length, channels), jnp.float32),
            jax.ShapeDtypeStruct((length, channels), jnp.float32),
            jax.ShapeDtypeStruct((pole_count, channels + LANES), jnp.float32),
            jax.ShapeDtypeStruct((rounds, pole_count, channels), jnp.float32),
            jax.ShapeDtypeStruct((length, LANES), jnp.float32),
        ],
        scratch_shapes=[
            pltpu.VMEM((span_r, width), jnp.bfloat16),
            pltpu.VMEM((taps * length, span_r), jnp.bfloat16),
            pltpu.VMEM((length, length), jnp.float32),
            pltpu.VMEM((8, length), jnp.float32),
        ],
        compiler_params=pltpu.CompilerParams(dimension_semantics=("arbitrary",)),
    )(qkv, qkv, qkv, rim, rim, rim, short_w, short_w, short_w, e_rows, rates_t, residues_t)

    prefix, partner, got = chip_scan(packed, decays, span_of, channels, pole_count, peers, me)
    half = channels // 2
    hb = max(half // final_width, 1)
    flag_block = channels // LANES
    rate_rows = jnp.stack([rates, residues]).reshape(2, 1, filters * pole_count)

    nbf = channels // final_width
    iw_width = final_width // group_width * pole_count
    return pl.pallas_call(
        functools.partial(final_kernel, group_width, pole_count, width, hb),
        grid=(nbf,),
        in_specs=[
            pl.BlockSpec((length, final_width), col(0)),
            pl.BlockSpec((length, final_width), col(0)),
            pl.BlockSpec((pole_count, final_width), lambda j: (0, j % hb)),
            pl.BlockSpec((pole_count, final_width), lambda j: (0, j % hb)),
            pl.BlockSpec((pole_count, final_width), col(0)),
            pl.BlockSpec((pole_count, final_width), col(0)),
            pl.BlockSpec((pole_count, LANES), lambda j: (0, flag_block)),
            pl.BlockSpec((pole_count, LANES), lambda j: (0, flag_block)),
            pl.BlockSpec((1, pole_count, final_width), lambda j: (span_of[1], 0, j)),
            pl.BlockSpec((2, 1, iw_width), lambda j: (0, 0, j)),
            pl.BlockSpec((length, LANES), fixed),
        ],
        out_specs=pl.BlockSpec((length, final_width), col(0)),
        out_shape=jax.ShapeDtypeStruct((length, channels), jnp.bfloat16),
        compiler_params=pltpu.CompilerParams(dimension_semantics=("arbitrary",)),
    )(q_part, local_part, prefix, partner, packed, got, packed, got, decays, rate_rows, info)


def solution(mesh):
    return jax.shard_map(
        on_device,
        mesh=mesh,
        in_specs=(P(("groups", "ctx"), None), P(("groups", "ctx")), P(), P(), P()),
        out_specs=P(("groups", "ctx"), None),
        check_vma=False,
    )
```

```python
import functools

import jax
import jax.numpy as jnp
from jax import lax
from jax.experimental import pallas as pl
from jax.experimental.pallas import tpu as pltpu
from jax.sharding import PartitionSpec as P

WIDTH = 256
FINAL_WIDTH = 1024
RIM = 8
LANES = 128


def from_behind(shard, axis, by):
    peers = lax.axis_size(axis)
    pairs = [(i, i + by) for i in range(peers) if 0 <= i + by < peers]
    return lax.ppermute(shard, axis, pairs)


def split2(x):
    hi = x.astype(jnp.bfloat16)
    lo = (x - hi.astype(jnp.float32)).astype(jnp.bfloat16)
    return hi, lo


def split3(x):
    hi = x.astype(jnp.bfloat16)
    rest = x - hi.astype(jnp.float32)
    mid = rest.astype(jnp.bfloat16)
    lo = (rest - mid.astype(jnp.float32)).astype(jnp.bfloat16)
    return hi, mid, lo


def local_kernel(taps, group_width, spans,
                 xq, xk, xv, rq, rk, rv, wq, wk, wv, e_ref, rt_ref, et_ref,
                 q_out, loc_out, pk_out, dec_out, info_out, ext_s, shift_s, vis_s, tail_s):
    length, width = xq.shape
    groups = width // group_width
    pole_count = rt_ref.shape[1]
    channels = pk_out.shape[1] - LANES
    span_r = e_ref.shape[1]
    step = pl.program_id(0)

    @pl.when(step == 0)
    def _():
        e_row = e_ref[0:1, :]
        t_col = lax.broadcasted_iota(jnp.int32, (length, span_r), 0)
        r_row = lax.broadcasted_iota(jnp.int32, (length, span_r), 1)
        doc_col = jnp.sum(jnp.where(r_row == t_col, e_row, 0.0), axis=1, keepdims=True)
        eq = e_row == doc_col
        place = jnp.where(r_row < length, r_row, r_row - length - RIM)
        for j in range(taps):
            hit = eq & (place == t_col - j) & (r_row < length + RIM)
            shift_s[j * length:(j + 1) * length, :] = jnp.where(hit, 1.0, 0.0).astype(jnp.bfloat16)
        eqf = jnp.where(eq, 1.0, 0.0)
        causal = r_row[:, :length] <= t_col[:, :length]
        vis_s[...] = jnp.where(causal, eqf[:, :length], 0.0)
        tail_s[...] = jnp.broadcast_to(eqf[length - 1:length, :length], tail_s.shape)
        into = eqf[0:1, length + RIM - 1:length + RIM]
        flag = into * eqf[length - 1:length, 0:1]
        pk_out[:, channels:channels + LANES] = jnp.broadcast_to(flag, (pole_count, LANES))
        lane = lax.broadcasted_iota(jnp.int32, info_out.shape, 1)
        info_out[...] = jnp.where(lane == 0, eqf[:, 0:1], jnp.broadcast_to(into, info_out.shape))
        ext_s[...] = jnp.zeros_like(ext_s)


    def conv(x_ref, r_ref, w_ref):
        ext_s[0:length, :] = x_ref[...]
        ext_s[length:length + RIM, :] = r_ref[...]
        ext = ext_s[...]
        w = w_ref[...]
        acc = w[0:1, :] * x_ref[...].astype(jnp.float32)
        for j in range(1, taps):
            window = jnp.dot(shift_s[j * length:(j + 1) * length, :], ext, preferred_element_type=jnp.float32)
            acc = acc + w[j:j + 1, :] * window
        return acc

    cq = conv(xq, rq, wq)
    ck = conv(xk, rk, wk)
    cv = conv(xv, rv, wv)
    q_out[...] = cq
    gated = (ck * cv).astype(jnp.bfloat16)

    lane_group = lax.broadcasted_iota(jnp.int32, (length, width), 1) // group_width
    zero = jnp.zeros_like(gated)
    xbd = jnp.concatenate([jnp.where(lane_group == g, gated, zero) for g in range(groups)], axis=0)

    rt = rt_ref[0]
    et = et_ref[0]
    lane = lax.broadcasted_iota(jnp.int32, (1, length), 1)
    lags = ((length - lane) % length).astype(jnp.float32)
    to_end = (length - 1 - lane).astype(jnp.float32)
    at_tail = tail_s[0:1, :]
    visible = vis_s[...] > 0.5
    pieces = []
    ends = []
    for g in range(groups):
        a_col = rt[:, g:g + 1]
        r_col = et[:, g:g + 1]
        base = jnp.sum(r_col * jnp.exp(-a_col * lags), axis=0, keepdims=True)
        row = jnp.broadcast_to(base.astype(jnp.bfloat16), (length, length))
        rolled = pltpu.roll(row, 0, 1, stride=1, stride_axis=0)
        pieces.append(jnp.where(visible, rolled, jnp.zeros_like(rolled)))
        ends.append(jnp.exp(-a_col * to_end) * at_tail)
    e_hi, e_lo = split2(jnp.concatenate(ends, axis=1))
    t_hi = jnp.concatenate(pieces, axis=1)
    res = jnp.dot(jnp.concatenate([t_hi, e_hi, e_lo], axis=0), xbd, preferred_element_type=jnp.float32)
    loc_out[...] = res[0:length]
    st = res[length:length + pole_count] + res[length + pole_count:length + 2 * pole_count]
    pk_out[:, pl.ds(pl.multiple_of(step * width, width), width)] = st

    spread = (lax.broadcasted_iota(jnp.int32, (groups, width), 1) // group_width
              == lax.broadcasted_iota(jnp.int32, (groups, width), 0)).astype(jnp.bfloat16)
    rate_cols = None
    for piece in split3(rt):
        part = jnp.dot(piece, spread, preferred_element_type=jnp.float32)
        rate_cols = part if rate_cols is None else rate_cols + part
    for r, span in enumerate(spans):
        dec_out[r] = jnp.exp(-rate_cols * span)


def final_kernel(group_width, pole_count, sub, hb, q_ref, loc_ref, zo_ref, zp_ref, pk_ref, gt_ref, pf_ref, gf_ref,
                 d1_ref, rr_ref, info_ref, o_ref):
    length, width = q_ref.shape
    groups = sub // group_width
    core = lax.axis_index("ctx") % 2
    odd = core == 1
    mine_half = (pl.program_id(0) // hb) == core
    full = jnp.where(mine_half, zo_ref[...], zp_ref[...])
    even_s = jnp.where(odd, gt_ref[...], pk_ref[...])
    even_f = jnp.where(odd, gf_ref[:, 0:1], pf_ref[:, 0:1])
    joined = jnp.where(odd, (even_f * d1_ref[0]) * full + even_s, full)
    b_all = joined * info_ref[0:1, 1:2]
    tcol = (lax.broadcasted_iota(jnp.int32, (length, 1), 0) + 1).astype(jnp.float32)
    iw = rr_ref[1] * jnp.exp(-rr_ref[0] * tcol) * info_ref[:, 0:1]
    iw_hi, iw_lo = split2(iw)
    shape = (groups * pole_count, sub)
    row_group = lax.broadcasted_iota(jnp.int32, shape, 0) // pole_count
    lane_group = lax.broadcasted_iota(jnp.int32, shape, 1) // group_width
    same = row_group == lane_group
    for s in range(width // sub):
        cols = slice(s * sub, (s + 1) * sub)
        tiled = jnp.concatenate([b_all[:, cols]] * groups, axis=0)
        b_hi, b_lo = split2(jnp.where(same, tiled, 0.0))
        poles = slice(s * shape[0], (s + 1) * shape[0])
        ih = iw_hi[:, poles]
        car = jnp.dot(ih, b_hi, preferred_element_type=jnp.float32)
        car = car + jnp.dot(ih, b_lo, preferred_element_type=jnp.float32)
        car = car + jnp.dot(iw_lo[:, poles], b_hi, preferred_element_type=jnp.float32)
        o_ref[:, cols] = (q_ref[:, cols] * (loc_ref[:, cols] + car)).astype(o_ref.dtype)


def swap_cores(shard, axis):
    peers = lax.axis_size(axis)
    return lax.ppermute(shard, axis, [(i, i ^ 1) for i in range(peers)])


def chip_scan(packed, decays, span_of, channels, pole_count, peers, me):
    core = me % 2
    odd = core == 1
    half = channels // 2
    mine = lambda x: lax.dynamic_slice_in_dim(x, core * half, half, axis=1)
    got = swap_cores(packed, "ctx")
    own_s, own_f = packed[:, :channels], packed[:, channels:channels + 1]
    other_s, other_f = got[:, :channels], got[:, channels:channels + 1]
    even_s = jnp.where(odd, other_s, own_s)
    odd_s = jnp.where(odd, own_s, other_s)
    even_f = jnp.where(odd, other_f, own_f)
    odd_f = jnp.where(odd, own_f, other_f)
    total = (odd_f * mine(decays[span_of[1]])) * mine(even_s) + mine(odd_s)
    flag = even_f * odd_f
    chips = peers // 2
    prefix = jnp.zeros_like(total)
    prefix_flag = jnp.ones_like(flag)
    offset = 1
    while offset < chips:
        load = jnp.concatenate([total, jnp.broadcast_to(flag, (pole_count, LANES))], axis=1)
        got_load = from_behind(load, "ctx", 2 * offset)
        came, came_flag = got_load[:, :half], got_load[:, half:half + 1]
        if offset == 1:
            prefix = prefix + prefix_flag * came
        else:
            prefix = prefix + (prefix_flag * mine(decays[span_of[2 * offset - 2]])) * came
        prefix_flag = prefix_flag * came_flag
        if 2 * offset < chips:
            total = total + (flag * mine(decays[span_of[2 * offset]])) * came
            flag = flag * came_flag
        offset *= 2
    return prefix, swap_cores(prefix, "ctx"), got


def scan_spans(peers):
    chips = peers // 2
    spans = {1}
    offset = 1
    while offset < chips:
        if offset > 1:
            spans.add(2 * offset - 2)
        if 2 * offset < chips:
            spans.add(2 * offset)
        offset *= 2
    return sorted(spans)


def on_device(qkv, doc_ids, short_w, rates, residues):
    length = qkv.shape[0]
    taps = short_w.shape[0]
    channels = qkv.shape[1] // 3
    filters, pole_count = rates.shape
    group_width = channels // filters
    width = min(WIDTH, channels)
    nb = channels // width
    gpb = width // group_width
    final_width = min(FINAL_WIDTH, channels)
    peers = lax.axis_size("ctx")
    me = lax.axis_index("ctx")

    tail_docs = jnp.broadcast_to(doc_ids[length - RIM:, None].astype(jnp.bfloat16), (RIM, LANES))
    rim = from_behind(jnp.concatenate([qkv[length - RIM:], tail_docs], axis=1), "ctx", 1)
    prev_docs = rim[:, 3 * channels].astype(jnp.int32)
    prev_last = prev_docs[RIM - 1]

    span_r = 2 * LANES
    e_vec = jnp.concatenate([doc_ids, prev_docs, jnp.full((span_r - length - RIM,), -1, jnp.int32)]).astype(jnp.float32)
    e_rows = jnp.broadcast_to(e_vec[None, :], (8, span_r))

    both_t = jnp.stack([rates, residues]).reshape(2, nb, gpb, pole_count).transpose(0, 1, 3, 2)
    rates_t, residues_t = both_t[0], both_t[1]
    span_list = scan_spans(peers)
    span_of = {v: i for i, v in enumerate(span_list)}
    rounds = len(span_list)
    spans = tuple(float(length * v) for v in span_list)

    col = lambda off: (lambda j: (0, j + off))
    fixed = lambda j: (0, 0)
    q_part, local_part, packed, decays, info = pl.pallas_call(
        functools.partial(local_kernel, taps, group_width, spans),
        grid=(nb,),
        in_specs=[
            pl.BlockSpec((length, width), col(0)),
            pl.BlockSpec((length, width), col(nb)),
            pl.BlockSpec((length, width), col(2 * nb)),
            pl.BlockSpec((RIM, width), col(0)),
            pl.BlockSpec((RIM, width), col(nb)),
            pl.BlockSpec((RIM, width), col(2 * nb)),
            pl.BlockSpec((taps, width), col(0)),
            pl.BlockSpec((taps, width), col(nb)),
            pl.BlockSpec((taps, width), col(2 * nb)),
            pl.BlockSpec((8, span_r), fixed),
            pl.BlockSpec((1, pole_count, gpb), lambda j: (j, 0, 0)),
            pl.BlockSpec((1, pole_count, gpb), lambda j: (j, 0, 0)),
        ],
        out_specs=[
            pl.BlockSpec((length, width), col(0)),
            pl.BlockSpec((length, width), col(0)),
            pl.BlockSpec((pole_count, channels + LANES), fixed),
            pl.BlockSpec((rounds, pole_count, width), lambda j: (0, 0, j)),
            pl.BlockSpec((length, LANES), fixed),
        ],
        out_shape=[
            jax.ShapeDtypeStruct((length, channels), jnp.float32),
            jax.ShapeDtypeStruct((length, channels), jnp.float32),
            jax.ShapeDtypeStruct((pole_count, channels + LANES), jnp.float32),
            jax.ShapeDtypeStruct((rounds, pole_count, channels), jnp.float32),
            jax.ShapeDtypeStruct((length, LANES), jnp.float32),
        ],
        scratch_shapes=[
            pltpu.VMEM((span_r, width), jnp.bfloat16),
            pltpu.VMEM((taps * length, span_r), jnp.bfloat16),
            pltpu.VMEM((length, length), jnp.float32),
            pltpu.VMEM((8, length), jnp.float32),
        ],
        compiler_params=pltpu.CompilerParams(dimension_semantics=("arbitrary",)),
    )(qkv, qkv, qkv, rim, rim, rim, short_w, short_w, short_w, e_rows, rates_t, residues_t)

    prefix, partner, got = chip_scan(packed, decays, span_of, channels, pole_count, peers, me)
    half = channels // 2
    hb = max(half // final_width, 1)
    flag_block = channels // LANES
    rate_rows = jnp.stack([rates, residues]).reshape(2, 1, filters * pole_count)

    nbf = channels // final_width
    iw_width = final_width // group_width * pole_count
    return pl.pallas_call(
        functools.partial(final_kernel, group_width, pole_count, width, hb),
        grid=(nbf,),
        in_specs=[
            pl.BlockSpec((length, final_width), col(0)),
            pl.BlockSpec((length, final_width), col(0)),
            pl.BlockSpec((pole_count, final_width), lambda j: (0, j % hb)),
            pl.BlockSpec((pole_count, final_width), lambda j: (0, j % hb)),
            pl.BlockSpec((pole_count, final_width), col(0)),
            pl.BlockSpec((pole_count, final_width), col(0)),
            pl.BlockSpec((pole_count, LANES), lambda j: (0, flag_block)),
            pl.BlockSpec((pole_count, LANES), lambda j: (0, flag_block)),
            pl.BlockSpec((1, pole_count, final_width), lambda j: (span_of[1], 0, j)),
            pl.BlockSpec((2, 1, iw_width), lambda j: (0, 0, j)),
            pl.BlockSpec((length, LANES), fixed),
        ],
        out_specs=pl.BlockSpec((length, final_width), col(0)),
        out_shape=jax.ShapeDtypeStruct((length, channels), jnp.bfloat16),
        compiler_params=pltpu.CompilerParams(dimension_semantics=("arbitrary",)),
    )(q_part, local_part, prefix, partner, packed, got, packed, got, decays, rate_rows, info)


def solution(mesh):
    return jax.shard_map(
        on_device,
        mesh=mesh,
        in_specs=(P(("groups", "ctx"), None), P(("groups", "ctx")), P(), P(), P()),
        out_specs=P(("groups", "ctx"), None),
        check_vma=False,
    )
```

```python
import functools

import jax
import jax.numpy as jnp
from jax import lax
from jax.experimental import pallas as pl
from jax.experimental.pallas import tpu as pltpu
from jax.sharding import PartitionSpec as P


WIDTH = 256
FINAL_WIDTH = 1024
RIM = 8
PIECES = 4
LANES = 128


def from_behind(shard, axis, by):
    peers = lax.axis_size(axis)
    pairs = [(i, i + by) for i in range(peers) if 0 <= i + by < peers]
    return lax.ppermute(shard, axis, pairs)


def split2(x):
    hi = x.astype(jnp.bfloat16)
    lo = (x - hi.astype(jnp.float32)).astype(jnp.bfloat16)
    return hi, lo


def split3(x):
    hi = x.astype(jnp.bfloat16)
    rest = x - hi.astype(jnp.float32)
    mid = rest.astype(jnp.bfloat16)
    lo = (rest - mid.astype(jnp.float32)).astype(jnp.bfloat16)
    return hi, mid, lo


def doc_tables(taps, e_ref, shift_ref, vis_ref, tail_ref):
    length = vis_ref.shape[0]
    span_r = e_ref.shape[1]
    e_row = e_ref[0:1, :]
    t_col = lax.broadcasted_iota(jnp.int32, (length, span_r), 0)
    r_row = lax.broadcasted_iota(jnp.int32, (length, span_r), 1)
    doc_col = jnp.sum(jnp.where(r_row == t_col, e_row, 0.0), axis=1, keepdims=True)
    eq = e_row == doc_col
    place = jnp.where(r_row < length, r_row, r_row - length - RIM)
    for j in range(taps):
        hit = eq & (place == t_col - j) & (r_row < length + RIM)
        shift_ref[j * length:(j + 1) * length, :] = jnp.where(hit, 1.0, 0.0).astype(jnp.bfloat16)
    eqf = jnp.where(eq, 1.0, 0.0)
    causal = r_row[:, :length] <= t_col[:, :length]
    vis_ref[...] = jnp.where(causal, eqf[:, :length], 0.0)
    tail_ref[...] = jnp.broadcast_to(eqf[length - 1:length, :length], tail_ref.shape)
    return eqf


def short_conv(taps, ext_s, shift_ref, x_ref, r_ref, w_ref):
    length = x_ref.shape[0]
    ext_s[0:length, :] = x_ref[...]
    ext_s[length:length + RIM, :] = r_ref[...]
    ext = ext_s[...]
    w = w_ref[...]
    acc = w[0:1, :] * x_ref[...].astype(jnp.float32)
    for j in range(1, taps):
        window = jnp.dot(shift_ref[j * length:(j + 1) * length, :], ext, preferred_element_type=jnp.float32)
        acc = acc + w[j:j + 1, :] * window
    return acc


def block_diagonal(gated, group_width):
    length, width = gated.shape
    lane_group = lax.broadcasted_iota(jnp.int32, (length, width), 1) // group_width
    zero = jnp.zeros_like(gated)
    return jnp.concatenate([jnp.where(lane_group == g, gated, zero) for g in range(width // group_width)], axis=0)


def states_kernel(taps, group_width, spans,
                  xk, xv, rk, rv, wk, wv, e_ref, rt_ref,
                  g_out, pk_out, dec_out, info_out, shift_out, vis_out, ext_s, tail_s):
    length, width = xk.shape
    groups = width // group_width
    pole_count = rt_ref.shape[1]
    channels = pk_out.shape[1] - LANES
    step = pl.program_id(0)

    @pl.when(step == 0)
    def _():
        eqf = doc_tables(taps, e_ref, shift_out, vis_out, tail_s)
        into = eqf[0:1, length + RIM - 1:length + RIM]
        flag = into * eqf[length - 1:length, 0:1]
        pk_out[:, channels:channels + LANES] = jnp.broadcast_to(flag, (pole_count, LANES))
        lane = lax.broadcasted_iota(jnp.int32, info_out.shape, 1)
        info_out[...] = jnp.where(lane == 0, eqf[:, 0:1], jnp.broadcast_to(into, info_out.shape))
        ext_s[...] = jnp.zeros_like(ext_s)

    ck = short_conv(taps, ext_s, shift_out, xk, rk, wk)
    cv = short_conv(taps, ext_s, shift_out, xv, rv, wv)
    gated = (ck * cv).astype(jnp.bfloat16)
    g_out[...] = gated
    xbd = block_diagonal(gated, group_width)

    rt = rt_ref[0]
    lane = lax.broadcasted_iota(jnp.int32, (1, length), 1)
    to_end = (length - 1 - lane).astype(jnp.float32)
    at_tail = tail_s[0:1, :]
    ends = [jnp.exp(-rt[:, g:g + 1] * to_end) * at_tail for g in range(groups)]
    e_hi, e_lo = split2(jnp.concatenate(ends, axis=1))
    res = jnp.dot(jnp.concatenate([e_hi, e_lo], axis=0), xbd, preferred_element_type=jnp.float32)
    st = res[0:pole_count] + res[pole_count:2 * pole_count]
    pk_out[:, pl.ds(pl.multiple_of(step * width, width), width)] = st

    spread = (lax.broadcasted_iota(jnp.int32, (groups, width), 1) // group_width
              == lax.broadcasted_iota(jnp.int32, (groups, width), 0)).astype(jnp.bfloat16)
    rate_cols = None
    for piece in split3(rt):
        part = jnp.dot(piece, spread, preferred_element_type=jnp.float32)
        rate_cols = part if rate_cols is None else rate_cols + part
    for r, span in enumerate(spans):
        dec_out[r] = jnp.exp(-rate_cols * span)


def toeplitz_kernel(taps, group_width, aliased, *refs):
    if aliased:
        xq, rq, wq, g_ref, shift_ref, vis_ref, rt_ref, et_ref, _, _, q_out, loc_out, ext_s = refs
    else:
        xq, rq, wq, g_ref, shift_ref, vis_ref, rt_ref, et_ref, q_out, loc_out, ext_s = refs
    length, width = xq.shape
    groups = width // group_width

    @pl.when(pl.program_id(0) == 0)
    def _():
        ext_s[...] = jnp.zeros_like(ext_s)

    q_out[...] = short_conv(taps, ext_s, shift_ref, xq, rq, wq)
    xbd = block_diagonal(g_ref[...], group_width)
    rt = rt_ref[0]
    et = et_ref[0]
    lane = lax.broadcasted_iota(jnp.int32, (1, length), 1)
    lags = ((length - lane) % length).astype(jnp.float32)
    visible = vis_ref[...] > 0.5
    pieces = []
    for g in range(groups):
        base = jnp.sum(et[:, g:g + 1] * jnp.exp(-rt[:, g:g + 1] * lags), axis=0, keepdims=True)
        row = jnp.broadcast_to(base.astype(jnp.bfloat16), (length, length))
        rolled = pltpu.roll(row, 0, 1, stride=1, stride_axis=0)
        pieces.append(jnp.where(visible, rolled, jnp.zeros_like(rolled)))
    loc_out[...] = jnp.dot(jnp.concatenate(pieces, axis=1), xbd, preferred_element_type=jnp.float32)


def final_kernel(group_width, pole_count, sub, hb, q_ref, loc_ref, zo_ref, zp_ref, pk_ref, gt_ref, pf_ref, gf_ref,
                 d1_ref, rr_ref, info_ref, o_ref):
    length, width = q_ref.shape
    groups = sub // group_width
    core = lax.axis_index("ctx") % 2
    odd = core == 1
    mine_half = (pl.program_id(0) // hb) == core
    full = jnp.where(mine_half, zo_ref[...], zp_ref[...])
    even_s = jnp.where(odd, gt_ref[...], pk_ref[...])
    even_f = jnp.where(odd, gf_ref[:, 0:1], pf_ref[:, 0:1])
    joined = jnp.where(odd, (even_f * d1_ref[0]) * full + even_s, full)
    b_all = joined * info_ref[0:1, 1:2]
    tcol = (lax.broadcasted_iota(jnp.int32, (length, 1), 0) + 1).astype(jnp.float32)
    iw = rr_ref[1] * jnp.exp(-rr_ref[0] * tcol) * info_ref[:, 0:1]
    iw_hi, iw_lo = split2(iw)
    shape = (groups * pole_count, sub)
    row_group = lax.broadcasted_iota(jnp.int32, shape, 0) // pole_count
    lane_group = lax.broadcasted_iota(jnp.int32, shape, 1) // group_width
    same = row_group == lane_group
    for s in range(width // sub):
        cols = slice(s * sub, (s + 1) * sub)
        tiled = jnp.concatenate([b_all[:, cols]] * groups, axis=0)
        b_hi, b_lo = split2(jnp.where(same, tiled, 0.0))
        poles = slice(s * shape[0], (s + 1) * shape[0])
        ih = iw_hi[:, poles]
        car = jnp.dot(ih, b_hi, preferred_element_type=jnp.float32)
        car = car + jnp.dot(ih, b_lo, preferred_element_type=jnp.float32)
        car = car + jnp.dot(iw_lo[:, poles], b_hi, preferred_element_type=jnp.float32)
        o_ref[:, cols] = (q_ref[:, cols] * (loc_ref[:, cols] + car)).astype(o_ref.dtype)


def swap_cores(shard, axis):
    peers = lax.axis_size(axis)
    return lax.ppermute(shard, axis, [(i, i ^ 1) for i in range(peers)])


def chip_scan(packed, decays, span_of, channels, pole_count, peers, me):
    core = me % 2
    odd = core == 1
    half = channels // 2
    mine = lambda x: lax.dynamic_slice_in_dim(x, core * half, half, axis=1)
    got = swap_cores(packed, "ctx")
    own_s, own_f = packed[:, :channels], packed[:, channels:channels + 1]
    other_s, other_f = got[:, :channels], got[:, channels:channels + 1]
    even_s = jnp.where(odd, other_s, own_s)
    odd_s = jnp.where(odd, own_s, other_s)
    even_f = jnp.where(odd, other_f, own_f)
    odd_f = jnp.where(odd, own_f, other_f)
    total = (odd_f * mine(decays[span_of[1]])) * mine(even_s) + mine(odd_s)
    flag = even_f * odd_f
    chips = peers // 2
    prefix = jnp.zeros_like(total)
    prefix_flag = jnp.ones_like(flag)
    offset = 1
    while offset < chips:
        load = jnp.concatenate([total, jnp.broadcast_to(flag, (pole_count, LANES))], axis=1)
        got_load = from_behind(load, "ctx", 2 * offset)
        came, came_flag = got_load[:, :half], got_load[:, half:half + 1]
        if offset == 1:
            prefix = prefix + prefix_flag * came
        else:
            prefix = prefix + (prefix_flag * mine(decays[span_of[2 * offset - 2]])) * came
        prefix_flag = prefix_flag * came_flag
        if 2 * offset < chips:
            total = total + (flag * mine(decays[span_of[2 * offset]])) * came
            flag = flag * came_flag
        offset *= 2
    return prefix, swap_cores(prefix, "ctx"), got


def scan_spans(peers):
    chips = peers // 2
    spans = {1}
    offset = 1
    while offset < chips:
        if offset > 1:
            spans.add(2 * offset - 2)
        if 2 * offset < chips:
            spans.add(2 * offset)
        offset *= 2
    return sorted(spans)


def device_body(qkv, doc_ids, short_w, rates, residues):
    length = qkv.shape[0]
    taps = short_w.shape[0]
    channels = qkv.shape[1] // 3
    filters, pole_count = rates.shape
    group_width = channels // filters
    width = min(WIDTH, channels)
    nb = channels // width
    gpb = width // group_width
    final_width = min(FINAL_WIDTH, channels)
    peers = lax.axis_size("ctx")
    me = lax.axis_index("ctx")

    tail_docs = jnp.broadcast_to(doc_ids[length - RIM:, None].astype(jnp.bfloat16), (RIM, LANES))
    rim = from_behind(jnp.concatenate([qkv[length - RIM:], tail_docs], axis=1), "ctx", 1)
    prev_docs = rim[:, 3 * channels].astype(jnp.int32)

    span_r = 2 * LANES
    e_vec = jnp.concatenate([doc_ids, prev_docs, jnp.full((span_r - length - RIM,), -1, jnp.int32)]).astype(jnp.float32)
    e_rows = jnp.broadcast_to(e_vec[None, :], (8, span_r))

    both_t = jnp.stack([rates, residues]).reshape(2, nb, gpb, pole_count).transpose(0, 1, 3, 2)
    rates_t, residues_t = both_t[0], both_t[1]
    span_list = scan_spans(peers)
    span_of = {v: i for i, v in enumerate(span_list)}
    rounds = len(span_list)
    spans = tuple(float(length * v) for v in span_list)

    col = lambda off: (lambda j: (0, j + off))
    fixed = lambda j: (0, 0)
    span_r = 2 * LANES
    gated, packed, decays, info, shift_tbl, vis_tbl = pl.pallas_call(
        functools.partial(states_kernel, taps, group_width, spans),
        grid=(nb,),
        in_specs=[
            pl.BlockSpec((length, width), col(nb)),
            pl.BlockSpec((length, width), col(2 * nb)),
            pl.BlockSpec((RIM, width), col(nb)),
            pl.BlockSpec((RIM, width), col(2 * nb)),
            pl.BlockSpec((taps, width), col(nb)),
            pl.BlockSpec((taps, width), col(2 * nb)),
            pl.BlockSpec((8, span_r), fixed),
            pl.BlockSpec((1, pole_count, gpb), lambda j: (j, 0, 0)),
        ],
        out_specs=[
            pl.BlockSpec((length, width), col(0)),
            pl.BlockSpec((pole_count, channels + LANES), fixed),
            pl.BlockSpec((rounds, pole_count, width), lambda j: (0, 0, j)),
            pl.BlockSpec((length, LANES), fixed),
            pl.BlockSpec((taps * length, span_r), fixed),
            pl.BlockSpec((length, length), fixed),
        ],
        out_shape=[
            jax.ShapeDtypeStruct((length, channels), jnp.bfloat16),
            jax.ShapeDtypeStruct((pole_count, channels + LANES), jnp.float32),
            jax.ShapeDtypeStruct((rounds, pole_count, channels), jnp.float32),
            jax.ShapeDtypeStruct((length, LANES), jnp.float32),
            jax.ShapeDtypeStruct((taps * length, span_r), jnp.bfloat16),
            jax.ShapeDtypeStruct((length, length), jnp.float32),
        ],
        scratch_shapes=[pltpu.VMEM((span_r, width), jnp.bfloat16), pltpu.VMEM((8, length), jnp.float32)],
        compiler_params=pltpu.CompilerParams(dimension_semantics=("arbitrary",)),
    )(qkv, qkv, rim, rim, short_w, short_w, e_rows, rates_t)

    per_piece = max(nb // PIECES, 1)
    q_part = local_part = None
    for first in range(0, nb, per_piece):
        count = min(per_piece, nb - first)
        at = lambda off, first=first: (lambda j: (0, j + first + off))
        specs = [
            pl.BlockSpec((length, width), at(0)),
            pl.BlockSpec((RIM, width), at(0)),
            pl.BlockSpec((taps, width), at(0)),
            pl.BlockSpec((length, width), at(0)),
            pl.BlockSpec((taps * length, span_r), fixed),
            pl.BlockSpec((length, length), fixed),
            pl.BlockSpec((1, pole_count, gpb), lambda j, first=first: (j + first, 0, 0)),
            pl.BlockSpec((1, pole_count, gpb), lambda j, first=first: (j + first, 0, 0)),
        ]
        args = [qkv, rim, short_w, gated, shift_tbl, vis_tbl, rates_t, residues_t]
        aliased = q_part is not None
        if aliased:
            specs += [pl.BlockSpec(memory_space=pl.ANY)] * 2
            args += [q_part, local_part]
        q_part, local_part = pl.pallas_call(
            functools.partial(toeplitz_kernel, taps, group_width, aliased),
            grid=(count,),
            in_specs=specs,
            out_specs=[pl.BlockSpec((length, width), at(0)), pl.BlockSpec((length, width), at(0))],
            out_shape=[
                jax.ShapeDtypeStruct((length, channels), jnp.float32),
                jax.ShapeDtypeStruct((length, channels), jnp.float32),
            ],
            scratch_shapes=[pltpu.VMEM((span_r, width), jnp.bfloat16)],
            input_output_aliases={8: 0, 9: 1} if aliased else {},
            compiler_params=pltpu.CompilerParams(dimension_semantics=("arbitrary",)),
        )(*args)

    prefix, partner, got = chip_scan(packed, decays, span_of, channels, pole_count, peers, me)
    half = channels // 2
    hb = max(half // final_width, 1)
    flag_block = channels // LANES
    rate_rows = jnp.stack([rates, residues]).reshape(2, 1, filters * pole_count)

    nbf = channels // final_width
    iw_width = final_width // group_width * pole_count
    return pl.pallas_call(
        functools.partial(final_kernel, group_width, pole_count, width, hb),
        grid=(nbf,),
        in_specs=[
            pl.BlockSpec((length, final_width), col(0)),
            pl.BlockSpec((length, final_width), col(0)),
            pl.BlockSpec((pole_count, final_width), lambda j: (0, j % hb)),
            pl.BlockSpec((pole_count, final_width), lambda j: (0, j % hb)),
            pl.BlockSpec((pole_count, final_width), col(0)),
            pl.BlockSpec((pole_count, final_width), col(0)),
            pl.BlockSpec((pole_count, LANES), lambda j: (0, flag_block)),
            pl.BlockSpec((pole_count, LANES), lambda j: (0, flag_block)),
            pl.BlockSpec((1, pole_count, final_width), lambda j: (span_of[1], 0, j)),
            pl.BlockSpec((2, 1, iw_width), lambda j: (0, 0, j)),
            pl.BlockSpec((length, LANES), fixed),
        ],
        out_specs=pl.BlockSpec((length, final_width), col(0)),
        out_shape=jax.ShapeDtypeStruct((length, channels), jnp.bfloat16),
        compiler_params=pltpu.CompilerParams(dimension_semantics=("arbitrary",)),
    )(q_part, local_part, prefix, partner, packed, got, packed, got, decays, rate_rows, info)


def solution(mesh):
    return jax.shard_map(
        device_body,
        mesh=mesh,
        in_specs=(P(("groups", "ctx"), None), P(("groups", "ctx")), P(), P(), P()),
        out_specs=P(("groups", "ctx"), None),
        check_vma=False,
    )
```

```python
import functools

import jax
import jax.numpy as jnp
from jax import lax
from jax.experimental import pallas as pl
from jax.experimental.pallas import tpu as pltpu
from jax.sharding import PartitionSpec as P

WIDTH = 256
FINAL_WIDTH = 1024
RIM = 8
LANES = 128


def from_behind(shard, axis, by):
    peers = lax.axis_size(axis)
    pairs = [(i, i + by) for i in range(peers) if 0 <= i + by < peers]
    return lax.ppermute(shard, axis, pairs)


def split2(x):
    hi = x.astype(jnp.bfloat16)
    lo = (x - hi.astype(jnp.float32)).astype(jnp.bfloat16)
    return hi, lo


def split3(x):
    hi = x.astype(jnp.bfloat16)
    rest = x - hi.astype(jnp.float32)
    mid = rest.astype(jnp.bfloat16)
    lo = (rest - mid.astype(jnp.float32)).astype(jnp.bfloat16)
    return hi, mid, lo


def exact_transpose(x):
    n = x.shape[1]
    eye = (lax.broadcasted_iota(jnp.int32, (n, n), 0) == lax.broadcasted_iota(jnp.int32, (n, n), 1))
    eye = eye.astype(jnp.bfloat16)
    out = None
    for piece in split3(x):
        part = lax.dot_general(eye, piece, (((1,), (1,)), ((), ())), preferred_element_type=jnp.float32)
        out = part if out is None else out + part
    return out


def exact_spread(x, spread):
    out = None
    for piece in split3(x):
        part = jnp.dot(piece, spread, preferred_element_type=jnp.float32)
        out = part if out is None else out + part
    return out


def local_kernel(taps, group_width, spans,
                 xq, xk, xv, rq, rk, rv, wq, wk, wv, doc_ref, rimdoc_ref, ra_ref, re_ref,
                 q_out, loc_out, pk_out, dec_out, info_out, rr_out, ext_s, shift_s, vis_s, tail_s):
    length, width = xq.shape
    groups = width // group_width
    pole_count = ra_ref.shape[1]
    channels = pk_out.shape[1] - LANES
    span_r = 2 * LANES
    step = pl.program_id(0)

    @pl.when(step == 0)
    def _():
        rim_docs = rimdoc_ref[...].astype(jnp.float32)
        diag = (lax.broadcasted_iota(jnp.int32, rim_docs.shape, 0)
                == lax.broadcasted_iota(jnp.int32, rim_docs.shape, 1))
        prev_row = jnp.sum(jnp.where(diag, rim_docs, 0.0), axis=0, keepdims=True)
        lane8 = lax.broadcasted_iota(jnp.int32, prev_row.shape, 1)
        e_row = jnp.concatenate([doc_ref[...].astype(jnp.float32), jnp.where(lane8 < RIM, prev_row, -1.0)], axis=1)
        t_col = lax.broadcasted_iota(jnp.int32, (length, span_r), 0)
        r_row = lax.broadcasted_iota(jnp.int32, (length, span_r), 1)
        doc_col = jnp.sum(jnp.where(r_row == t_col, e_row, 0.0), axis=1, keepdims=True)
        eq = e_row == doc_col
        place = jnp.where(r_row < length, r_row, r_row - length - RIM)
        for j in range(taps):
            hit = eq & (place == t_col - j) & (r_row < length + RIM)
            shift_s[j * length:(j + 1) * length, :] = jnp.where(hit, 1.0, 0.0).astype(jnp.bfloat16)
        eqf = jnp.where(eq, 1.0, 0.0)
        causal = r_row[:, :length] <= t_col[:, :length]
        vis_s[...] = jnp.where(causal, eqf[:, :length], 0.0)
        tail_s[...] = jnp.broadcast_to(eqf[length - 1:length, :length], tail_s.shape)
        into = eqf[0:1, length + RIM - 1:length + RIM]
        flag = into * eqf[length - 1:length, 0:1]
        pk_out[:, channels:channels + LANES] = jnp.broadcast_to(flag, (pole_count, LANES))
        lane = lax.broadcasted_iota(jnp.int32, info_out.shape, 1)
        info_out[...] = jnp.where(lane == 0, eqf[:, 0:1], jnp.broadcast_to(into, info_out.shape))
        ext_s[...] = jnp.zeros_like(ext_s)


    def conv(x_ref, r_ref, w_ref):
        ext_s[0:length, :] = x_ref[...]
        ext_s[length:length + RIM, :] = r_ref[...]
        ext = ext_s[...]
        w = w_ref[...]
        acc = w[0:1, :] * x_ref[...].astype(jnp.float32)
        for j in range(1, taps):
            window = jnp.dot(shift_s[j * length:(j + 1) * length, :], ext, preferred_element_type=jnp.float32)
            acc = acc + w[j:j + 1, :] * window
        return acc

    cq = conv(xq, rq, wq)
    ck = conv(xk, rk, wk)
    cv = conv(xv, rv, wv)
    q_out[...] = cq
    gated = (ck * cv).astype(jnp.bfloat16)

    lane_group = lax.broadcasted_iota(jnp.int32, (length, width), 1) // group_width
    zero = jnp.zeros_like(gated)
    xbd = jnp.concatenate([jnp.where(lane_group == g, gated, zero) for g in range(groups)], axis=0)

    rt = exact_transpose(ra_ref[...])
    et = exact_transpose(re_ref[...])
    lane = lax.broadcasted_iota(jnp.int32, (1, length), 1)
    lags = ((length - lane) % length).astype(jnp.float32)
    to_end = (length - 1 - lane).astype(jnp.float32)
    at_tail = tail_s[0:1, :]
    visible = vis_s[...] > 0.5
    pieces = []
    ends = []
    for g in range(groups):
        a_col = rt[:, g:g + 1]
        r_col = et[:, g:g + 1]
        base = jnp.sum(r_col * jnp.exp(-a_col * lags), axis=0, keepdims=True)
        row = jnp.broadcast_to(base.astype(jnp.bfloat16), (length, length))
        rolled = pltpu.roll(row, 0, 1, stride=1, stride_axis=0)
        pieces.append(jnp.where(visible, rolled, jnp.zeros_like(rolled)))
        ends.append(jnp.exp(-a_col * to_end) * at_tail)
    e_hi, e_lo = split2(jnp.concatenate(ends, axis=1))
    t_hi = jnp.concatenate(pieces, axis=1)
    res = jnp.dot(jnp.concatenate([t_hi, e_hi, e_lo], axis=0), xbd, preferred_element_type=jnp.float32)
    loc_out[...] = res[0:length]
    st = res[length:length + pole_count] + res[length + pole_count:length + 2 * pole_count]
    pk_out[:, pl.ds(pl.multiple_of(step * width, width), width)] = st

    spread = (lax.broadcasted_iota(jnp.int32, (groups, width), 1) // group_width
              == lax.broadcasted_iota(jnp.int32, (groups, width), 0)).astype(jnp.bfloat16)
    rate_cols = exact_spread(rt, spread)
    for r, span in enumerate(spans):
        dec_out[r] = jnp.exp(-rate_cols * span)
    flat = groups * pole_count
    to_pairs = (lax.broadcasted_iota(jnp.int32, (groups, flat), 1) // pole_count
                == lax.broadcasted_iota(jnp.int32, (groups, flat), 0)).astype(jnp.bfloat16)
    pick = (lax.broadcasted_iota(jnp.int32, (pole_count, flat), 0)
            == lax.broadcasted_iota(jnp.int32, (pole_count, flat), 1) % pole_count)
    for plane, table in enumerate((rt, et)):
        row = jnp.sum(jnp.where(pick, exact_spread(table, to_pairs), 0.0), axis=0, keepdims=True)
        rr_out[plane] = jnp.broadcast_to(row, (8, flat))


def final_kernel(group_width, pole_count, sub, hb, q_ref, loc_ref, zo_ref, zp_ref, pk_ref, gt_ref, pf_ref, gf_ref,
                 d1_ref, rr_ref, info_ref, o_ref):
    length, width = q_ref.shape
    groups = sub // group_width
    core = lax.axis_index("ctx") % 2
    odd = core == 1
    mine_half = (pl.program_id(0) // hb) == core
    full = jnp.where(mine_half, zo_ref[...], zp_ref[...])
    even_s = jnp.where(odd, gt_ref[...], pk_ref[...])
    even_f = jnp.where(odd, gf_ref[:, 0:1], pf_ref[:, 0:1])
    joined = jnp.where(odd, (even_f * d1_ref[0]) * full + even_s, full)
    b_all = joined * info_ref[0:1, 1:2]
    tcol = (lax.broadcasted_iota(jnp.int32, (length, 1), 0) + 1).astype(jnp.float32)
    iw = rr_ref[1, 0:1, :] * jnp.exp(-rr_ref[0, 0:1, :] * tcol) * info_ref[:, 0:1]
    iw_hi, iw_lo = split2(iw)
    shape = (groups * pole_count, sub)
    row_group = lax.broadcasted_iota(jnp.int32, shape, 0) // pole_count
    lane_group = lax.broadcasted_iota(jnp.int32, shape, 1) // group_width
    same = row_group == lane_group
    for s in range(width // sub):
        cols = slice(s * sub, (s + 1) * sub)
        tiled = jnp.concatenate([b_all[:, cols]] * groups, axis=0)
        b_hi, b_lo = split2(jnp.where(same, tiled, 0.0))
        poles = slice(s * shape[0], (s + 1) * shape[0])
        ih = iw_hi[:, poles]
        car = jnp.dot(ih, b_hi, preferred_element_type=jnp.float32)
        car = car + jnp.dot(ih, b_lo, preferred_element_type=jnp.float32)
        car = car + jnp.dot(iw_lo[:, poles], b_hi, preferred_element_type=jnp.float32)
        o_ref[:, cols] = (q_ref[:, cols] * (loc_ref[:, cols] + car)).astype(o_ref.dtype)


def swap_cores(shard, axis):
    peers = lax.axis_size(axis)
    return lax.ppermute(shard, axis, [(i, i ^ 1) for i in range(peers)])


def chip_scan(packed, decays, span_of, channels, pole_count, peers, me):
    core = me % 2
    odd = core == 1
    half = channels // 2
    mine = lambda x: lax.dynamic_slice_in_dim(x, core * half, half, axis=1)
    got = swap_cores(packed, "ctx")
    own_s, own_f = packed[:, :channels], packed[:, channels:channels + 1]
    other_s, other_f = got[:, :channels], got[:, channels:channels + 1]
    even_s = jnp.where(odd, other_s, own_s)
    odd_s = jnp.where(odd, own_s, other_s)
    even_f = jnp.where(odd, other_f, own_f)
    odd_f = jnp.where(odd, own_f, other_f)
    total = (odd_f * mine(decays[span_of[1]])) * mine(even_s) + mine(odd_s)
    flag = even_f * odd_f
    chips = peers // 2
    prefix = jnp.zeros_like(total)
    prefix_flag = jnp.ones_like(flag)
    offset = 1
    while offset < chips:
        load = jnp.concatenate([total, jnp.broadcast_to(flag, (pole_count, LANES))], axis=1)
        got_load = from_behind(load, "ctx", 2 * offset)
        came, came_flag = got_load[:, :half], got_load[:, half:half + 1]
        if offset == 1:
            prefix = prefix + prefix_flag * came
        else:
            prefix = prefix + (prefix_flag * mine(decays[span_of[2 * offset - 2]])) * came
        prefix_flag = prefix_flag * came_flag
        if 2 * offset < chips:
            total = total + (flag * mine(decays[span_of[2 * offset]])) * came
            flag = flag * came_flag
        offset *= 2
    return prefix, swap_cores(prefix, "ctx"), got


def scan_spans(peers):
    chips = peers // 2
    spans = {1}
    offset = 1
    while offset < chips:
        if offset > 1:
            spans.add(2 * offset - 2)
        if 2 * offset < chips:
            spans.add(2 * offset)
        offset *= 2
    return sorted(spans)


def on_device(qkv, doc_ids, short_w, rates, residues):
    length = qkv.shape[0]
    taps = short_w.shape[0]
    channels = qkv.shape[1] // 3
    filters, pole_count = rates.shape
    group_width = channels // filters
    width = min(WIDTH, channels)
    nb = channels // width
    gpb = width // group_width
    final_width = min(FINAL_WIDTH, channels)
    peers = lax.axis_size("ctx")
    me = lax.axis_index("ctx")

    tail_docs = jnp.broadcast_to(doc_ids[length - RIM:, None].astype(jnp.bfloat16), (RIM, LANES))
    rim = from_behind(jnp.concatenate([qkv[length - RIM:], tail_docs], axis=1), "ctx", 1)
    span_r = 2 * LANES

    span_list = scan_spans(peers)
    span_of = {v: i for i, v in enumerate(span_list)}
    rounds = len(span_list)
    spans = tuple(float(length * v) for v in span_list)

    col = lambda off: (lambda j: (0, j + off))
    fixed = lambda j: (0, 0)
    q_part, local_part, packed, decays, info, rate_rows = pl.pallas_call(
        functools.partial(local_kernel, taps, group_width, spans),
        grid=(nb,),
        in_specs=[
            pl.BlockSpec((length, width), col(0)),
            pl.BlockSpec((length, width), col(nb)),
            pl.BlockSpec((length, width), col(2 * nb)),
            pl.BlockSpec((RIM, width), col(0)),
            pl.BlockSpec((RIM, width), col(nb)),
            pl.BlockSpec((RIM, width), col(2 * nb)),
            pl.BlockSpec((taps, width), col(0)),
            pl.BlockSpec((taps, width), col(nb)),
            pl.BlockSpec((taps, width), col(2 * nb)),
            pl.BlockSpec((1, length), fixed),
            pl.BlockSpec((RIM, LANES), lambda j: (0, 3 * channels // LANES)),
            pl.BlockSpec((gpb, pole_count), lambda j: (j, 0)),
            pl.BlockSpec((gpb, pole_count), lambda j: (j, 0)),
        ],
        out_specs=[
            pl.BlockSpec((length, width), col(0)),
            pl.BlockSpec((length, width), col(0)),
            pl.BlockSpec((pole_count, channels + LANES), fixed),
            pl.BlockSpec((rounds, pole_count, width), lambda j: (0, 0, j)),
            pl.BlockSpec((length, LANES), fixed),
            pl.BlockSpec((2, 8, gpb * pole_count), lambda j: (0, 0, j)),
        ],
        out_shape=[
            jax.ShapeDtypeStruct((length, channels), jnp.float32),
            jax.ShapeDtypeStruct((length, channels), jnp.float32),
            jax.ShapeDtypeStruct((pole_count, channels + LANES), jnp.float32),
            jax.ShapeDtypeStruct((rounds, pole_count, channels), jnp.float32),
            jax.ShapeDtypeStruct((length, LANES), jnp.float32),
            jax.ShapeDtypeStruct((2, 8, filters * pole_count), jnp.float32),
        ],
        scratch_shapes=[
            pltpu.VMEM((span_r, width), jnp.bfloat16),
            pltpu.VMEM((taps * length, span_r), jnp.bfloat16),
            pltpu.VMEM((length, length), jnp.float32),
            pltpu.VMEM((8, length), jnp.float32),
        ],
        compiler_params=pltpu.CompilerParams(dimension_semantics=("arbitrary",)),
    )(qkv, qkv, qkv, rim, rim, rim, short_w, short_w, short_w, doc_ids.reshape(1, length), rim, rates, residues)

    prefix, partner, got = chip_scan(packed, decays, span_of, channels, pole_count, peers, me)
    half = channels // 2
    hb = max(half // final_width, 1)
    flag_block = channels // LANES

    nbf = channels // final_width
    iw_width = final_width // group_width * pole_count
    return pl.pallas_call(
        functools.partial(final_kernel, group_width, pole_count, width, hb),
        grid=(nbf,),
        in_specs=[
            pl.BlockSpec((length, final_width), col(0)),
            pl.BlockSpec((length, final_width), col(0)),
            pl.BlockSpec((pole_count, final_width), lambda j: (0, j % hb)),
            pl.BlockSpec((pole_count, final_width), lambda j: (0, j % hb)),
            pl.BlockSpec((pole_count, final_width), col(0)),
            pl.BlockSpec((pole_count, final_width), col(0)),
            pl.BlockSpec((pole_count, LANES), lambda j: (0, flag_block)),
            pl.BlockSpec((pole_count, LANES), lambda j: (0, flag_block)),
            pl.BlockSpec((1, pole_count, final_width), lambda j: (span_of[1], 0, j)),
            pl.BlockSpec((2, 8, iw_width), lambda j: (0, 0, j)),
            pl.BlockSpec((length, LANES), fixed),
        ],
        out_specs=pl.BlockSpec((length, final_width), col(0)),
        out_shape=jax.ShapeDtypeStruct((length, channels), jnp.bfloat16),
        compiler_params=pltpu.CompilerParams(dimension_semantics=("arbitrary",)),
    )(q_part, local_part, prefix, partner, packed, got, packed, got, decays, rate_rows, info)


def solution(mesh):
    return jax.shard_map(
        on_device,
        mesh=mesh,
        in_specs=(P(("groups", "ctx"), None), P(("groups", "ctx")), P(), P(), P()),
        out_specs=P(("groups", "ctx"), None),
        check_vma=False,
    )
```

```python
import functools

import jax
import jax.numpy as jnp
from jax import lax
from jax.experimental import pallas as pl
from jax.experimental.pallas import tpu as pltpu
from jax.sharding import PartitionSpec as P

WIDTH = 256
FINAL_WIDTH = 2048
RIM = 8
LANES = 128


def from_behind(shard, axis, by):
    peers = lax.axis_size(axis)
    pairs = [(i, i + by) for i in range(peers) if 0 <= i + by < peers]
    return lax.ppermute(shard, axis, pairs)


def split2(x):
    hi = x.astype(jnp.bfloat16)
    lo = (x - hi.astype(jnp.float32)).astype(jnp.bfloat16)
    return hi, lo


def split3(x):
    hi = x.astype(jnp.bfloat16)
    rest = x - hi.astype(jnp.float32)
    mid = rest.astype(jnp.bfloat16)
    lo = (rest - mid.astype(jnp.float32)).astype(jnp.bfloat16)
    return hi, mid, lo


def local_kernel(taps, group_width, spans,
                 xq, xk, xv, rq, rk, rv, wq, wk, wv, e_ref, rt_ref, et_ref,
                 q_out, loc_out, pk_out, dec_out, info_out, ext_s, shift_s, vis_s, tail_s):
    length, width = xq.shape
    groups = width // group_width
    pole_count = rt_ref.shape[1]
    channels = pk_out.shape[1] - LANES
    span_r = e_ref.shape[1]
    step = pl.program_id(0)

    @pl.when(step == 0)
    def _():
        e_row = e_ref[0:1, :]
        t_col = lax.broadcasted_iota(jnp.int32, (length, span_r), 0)
        r_row = lax.broadcasted_iota(jnp.int32, (length, span_r), 1)
        doc_col = jnp.sum(jnp.where(r_row == t_col, e_row, 0.0), axis=1, keepdims=True)
        eq = e_row == doc_col
        place = jnp.where(r_row < length, r_row, r_row - length - RIM)
        for j in range(taps):
            hit = eq & (place == t_col - j) & (r_row < length + RIM)
            shift_s[j * length:(j + 1) * length, :] = jnp.where(hit, 1.0, 0.0).astype(jnp.bfloat16)
        eqf = jnp.where(eq, 1.0, 0.0)
        causal = r_row[:, :length] <= t_col[:, :length]
        vis_s[...] = jnp.where(causal, eqf[:, :length], 0.0)
        tail_s[...] = jnp.broadcast_to(eqf[length - 1:length, :length], tail_s.shape)
        into = eqf[0:1, length + RIM - 1:length + RIM]
        flag = into * eqf[length - 1:length, 0:1]
        pk_out[:, channels:channels + LANES] = jnp.broadcast_to(flag, (pole_count, LANES))
        lane = lax.broadcasted_iota(jnp.int32, info_out.shape, 1)
        info_out[...] = jnp.where(lane == 0, eqf[:, 0:1], jnp.broadcast_to(into, info_out.shape))
        ext_s[...] = jnp.zeros_like(ext_s)


    def conv(x_ref, r_ref, w_ref):
        ext_s[0:length, :] = x_ref[...]
        ext_s[length:length + RIM, :] = r_ref[...]
        ext = ext_s[...]
        w = w_ref[...]
        acc = w[0:1, :] * x_ref[...].astype(jnp.float32)
        for j in range(1, taps):
            window = jnp.dot(shift_s[j * length:(j + 1) * length, :], ext, preferred_element_type=jnp.float32)
            acc = acc + w[j:j + 1, :] * window
        return acc

    cq = conv(xq, rq, wq)
    ck = conv(xk, rk, wk)
    cv = conv(xv, rv, wv)
    q_out[...] = cq
    gated = (ck * cv).astype(jnp.bfloat16)

    lane_group = lax.broadcasted_iota(jnp.int32, (length, width), 1) // group_width
    zero = jnp.zeros_like(gated)
    xbd = jnp.concatenate([jnp.where(lane_group == g, gated, zero) for g in range(groups)], axis=0)

    rt = rt_ref[0]
    et = et_ref[0]
    lane = lax.broadcasted_iota(jnp.int32, (1, length), 1)
    lags = ((length - lane) % length).astype(jnp.float32)
    to_end = (length - 1 - lane).astype(jnp.float32)
    at_tail = tail_s[0:1, :]
    visible = vis_s[...] > 0.5
    pieces = []
    ends = []
    for g in range(groups):
        a_col = rt[:, g:g + 1]
        r_col = et[:, g:g + 1]
        base = jnp.sum(r_col * jnp.exp(-a_col * lags), axis=0, keepdims=True)
        row = jnp.broadcast_to(base.astype(jnp.bfloat16), (length, length))
        rolled = pltpu.roll(row, 0, 1, stride=1, stride_axis=0)
        pieces.append(jnp.where(visible, rolled, jnp.zeros_like(rolled)))
        ends.append(jnp.exp(-a_col * to_end) * at_tail)
    e_hi, e_lo = split2(jnp.concatenate(ends, axis=1))
    t_hi = jnp.concatenate(pieces, axis=1)
    res = jnp.dot(jnp.concatenate([t_hi, e_hi, e_lo], axis=0), xbd, preferred_element_type=jnp.float32)
    loc_out[...] = res[0:length]
    st = res[length:length + pole_count] + res[length + pole_count:length + 2 * pole_count]
    pk_out[:, pl.ds(pl.multiple_of(step * width, width), width)] = st

    spread = (lax.broadcasted_iota(jnp.int32, (groups, width), 1) // group_width
              == lax.broadcasted_iota(jnp.int32, (groups, width), 0)).astype(jnp.bfloat16)
    rate_cols = None
    for piece in split3(rt):
        part = jnp.dot(piece, spread, preferred_element_type=jnp.float32)
        rate_cols = part if rate_cols is None else rate_cols + part
    for r, span in enumerate(spans):
        dec_out[r] = jnp.exp(-rate_cols * span)


def final_kernel(group_width, pole_count, sub, hb, q_ref, loc_ref, zo_ref, zp_ref, pk_ref, gt_ref, pf_ref, gf_ref,
                 d1_ref, rr_ref, info_ref, o_ref):
    length, width = q_ref.shape
    groups = sub // group_width
    core = lax.axis_index("ctx") % 2
    odd = core == 1
    mine_half = (pl.program_id(0) // hb) == core
    full = jnp.where(mine_half, zo_ref[...], zp_ref[...])
    even_s = jnp.where(odd, gt_ref[...], pk_ref[...])
    even_f = jnp.where(odd, gf_ref[:, 0:1], pf_ref[:, 0:1])
    joined = jnp.where(odd, (even_f * d1_ref[0]) * full + even_s, full)
    b_all = joined * info_ref[0:1, 1:2]
    tcol = (lax.broadcasted_iota(jnp.int32, (length, 1), 0) + 1).astype(jnp.float32)
    iw = rr_ref[1] * jnp.exp(-rr_ref[0] * tcol) * info_ref[:, 0:1]
    iw_hi, iw_lo = split2(iw)
    shape = (groups * pole_count, sub)
    row_group = lax.broadcasted_iota(jnp.int32, shape, 0) // pole_count
    lane_group = lax.broadcasted_iota(jnp.int32, shape, 1) // group_width
    same = row_group == lane_group
    for s in range(width // sub):
        cols = slice(s * sub, (s + 1) * sub)
        tiled = jnp.concatenate([b_all[:, cols]] * groups, axis=0)
        b_hi, b_lo = split2(jnp.where(same, tiled, 0.0))
        poles = slice(s * shape[0], (s + 1) * shape[0])
        ih = iw_hi[:, poles]
        car = jnp.dot(ih, b_hi, preferred_element_type=jnp.float32)
        car = car + jnp.dot(ih, b_lo, preferred_element_type=jnp.float32)
        car = car + jnp.dot(iw_lo[:, poles], b_hi, preferred_element_type=jnp.float32)
        o_ref[:, cols] = (q_ref[:, cols] * (loc_ref[:, cols] + car)).astype(o_ref.dtype)


def swap_cores(shard, axis):
    peers = lax.axis_size(axis)
    return lax.ppermute(shard, axis, [(i, i ^ 1) for i in range(peers)])


def chip_scan(packed, decays, span_of, channels, pole_count, peers, me):
    core = me % 2
    odd = core == 1
    half = channels // 2
    mine = lambda x: lax.dynamic_slice_in_dim(x, core * half, half, axis=1)
    got = swap_cores(packed, "ctx")
    own_s, own_f = packed[:, :channels], packed[:, channels:channels + 1]
    other_s, other_f = got[:, :channels], got[:, channels:channels + 1]
    even_s = jnp.where(odd, other_s, own_s)
    odd_s = jnp.where(odd, own_s, other_s)
    even_f = jnp.where(odd, other_f, own_f)
    odd_f = jnp.where(odd, own_f, other_f)
    total = (odd_f * mine(decays[span_of[1]])) * mine(even_s) + mine(odd_s)
    flag = even_f * odd_f
    chips = peers // 2
    prefix = jnp.zeros_like(total)
    prefix_flag = jnp.ones_like(flag)
    offset = 1
    while offset < chips:
        load = jnp.concatenate([total, jnp.broadcast_to(flag, (pole_count, LANES))], axis=1)
        got_load = from_behind(load, "ctx", 2 * offset)
        came, came_flag = got_load[:, :half], got_load[:, half:half + 1]
        if offset == 1:
            prefix = prefix + prefix_flag * came
        else:
            prefix = prefix + (prefix_flag * mine(decays[span_of[2 * offset - 2]])) * came
        prefix_flag = prefix_flag * came_flag
        if 2 * offset < chips:
            total = total + (flag * mine(decays[span_of[2 * offset]])) * came
            flag = flag * came_flag
        offset *= 2
    return prefix, swap_cores(prefix, "ctx"), got


def scan_spans(peers):
    chips = peers // 2
    spans = {1}
    offset = 1
    while offset < chips:
        if offset > 1:
            spans.add(2 * offset - 2)
        if 2 * offset < chips:
            spans.add(2 * offset)
        offset *= 2
    return sorted(spans)


def on_device(qkv, doc_ids, short_w, rates, residues):
    length = qkv.shape[0]
    taps = short_w.shape[0]
    channels = qkv.shape[1] // 3
    filters, pole_count = rates.shape
    group_width = channels // filters
    width = min(WIDTH, channels)
    nb = channels // width
    gpb = width // group_width
    final_width = min(FINAL_WIDTH, channels)
    peers = lax.axis_size("ctx")
    me = lax.axis_index("ctx")

    tail_docs = jnp.broadcast_to(doc_ids[length - RIM:, None].astype(jnp.bfloat16), (RIM, LANES))
    rim = from_behind(jnp.concatenate([qkv[length - RIM:], tail_docs], axis=1), "ctx", 1)
    prev_docs = rim[:, 3 * channels].astype(jnp.int32)
    prev_last = prev_docs[RIM - 1]

    span_r = 2 * LANES
    e_vec = jnp.concatenate([doc_ids, prev_docs, jnp.full((span_r - length - RIM,), -1, jnp.int32)]).astype(jnp.float32)
    e_rows = jnp.broadcast_to(e_vec[None, :], (8, span_r))

    both_t = jnp.stack([rates, residues]).reshape(2, nb, gpb, pole_count).transpose(0, 1, 3, 2)
    rates_t, residues_t = both_t[0], both_t[1]
    span_list = scan_spans(peers)
    span_of = {v: i for i, v in enumerate(span_list)}
    rounds = len(span_list)
    spans = tuple(float(length * v) for v in span_list)

    col = lambda off: (lambda j: (0, j + off))
    fixed = lambda j: (0, 0)
    q_part, local_part, packed, decays, info = pl.pallas_call(
        functools.partial(local_kernel, taps, group_width, spans),
        grid=(nb,),
        in_specs=[
            pl.BlockSpec((length, width), col(0)),
            pl.BlockSpec((length, width), col(nb)),
            pl.BlockSpec((length, width), col(2 * nb)),
            pl.BlockSpec((RIM, width), col(0)),
            pl.BlockSpec((RIM, width), col(nb)),
            pl.BlockSpec((RIM, width), col(2 * nb)),
            pl.BlockSpec((taps, width), col(0)),
            pl.BlockSpec((taps, width), col(nb)),
            pl.BlockSpec((taps, width), col(2 * nb)),
            pl.BlockSpec((8, span_r), fixed),
            pl.BlockSpec((1, pole_count, gpb), lambda j: (j, 0, 0)),
            pl.BlockSpec((1, pole_count, gpb), lambda j: (j, 0, 0)),
        ],
        out_specs=[
            pl.BlockSpec((length, width), col(0)),
            pl.BlockSpec((length, width), col(0)),
            pl.BlockSpec((pole_count, channels + LANES), fixed),
            pl.BlockSpec((rounds, pole_count, width), lambda j: (0, 0, j)),
            pl.BlockSpec((length, LANES), fixed),
        ],
        out_shape=[
            jax.ShapeDtypeStruct((length, channels), jnp.float32),
            jax.ShapeDtypeStruct((length, channels), jnp.float32),
            jax.ShapeDtypeStruct((pole_count, channels + LANES), jnp.float32),
            jax.ShapeDtypeStruct((rounds, pole_count, channels), jnp.float32),
            jax.ShapeDtypeStruct((length, LANES), jnp.float32),
        ],
        scratch_shapes=[
            pltpu.VMEM((span_r, width), jnp.bfloat16),
            pltpu.VMEM((taps * length, span_r), jnp.bfloat16),
            pltpu.VMEM((length, length), jnp.float32),
            pltpu.VMEM((8, length), jnp.float32),
        ],
        compiler_params=pltpu.CompilerParams(dimension_semantics=("arbitrary",)),
    )(qkv, qkv, qkv, rim, rim, rim, short_w, short_w, short_w, e_rows, rates_t, residues_t)

    prefix, partner, got = chip_scan(packed, decays, span_of, channels, pole_count, peers, me)
    half = channels // 2
    hb = max(half // final_width, 1)
    flag_block = channels // LANES
    rate_rows = jnp.stack([rates, residues]).reshape(2, 1, filters * pole_count)

    nbf = channels // final_width
    iw_width = final_width // group_width * pole_count
    return pl.pallas_call(
        functools.partial(final_kernel, group_width, pole_count, width, hb),
        grid=(nbf,),
        in_specs=[
            pl.BlockSpec((length, final_width), col(0)),
            pl.BlockSpec((length, final_width), col(0)),
            pl.BlockSpec((pole_count, final_width), lambda j: (0, j % hb)),
            pl.BlockSpec((pole_count, final_width), lambda j: (0, j % hb)),
            pl.BlockSpec((pole_count, final_width), col(0)),
            pl.BlockSpec((pole_count, final_width), col(0)),
            pl.BlockSpec((pole_count, LANES), lambda j: (0, flag_block)),
            pl.BlockSpec((pole_count, LANES), lambda j: (0, flag_block)),
            pl.BlockSpec((1, pole_count, final_width), lambda j: (span_of[1], 0, j)),
            pl.BlockSpec((2, 1, iw_width), lambda j: (0, 0, j)),
            pl.BlockSpec((length, LANES), fixed),
        ],
        out_specs=pl.BlockSpec((length, final_width), col(0)),
        out_shape=jax.ShapeDtypeStruct((length, channels), jnp.bfloat16),
        compiler_params=pltpu.CompilerParams(dimension_semantics=("arbitrary",)),
    )(q_part, local_part, prefix, partner, packed, got, packed, got, decays, rate_rows, info)


def solution(mesh):
    return jax.shard_map(
        on_device,
        mesh=mesh,
        in_specs=(P(("groups", "ctx"), None), P(("groups", "ctx")), P(), P(), P()),
        out_specs=P(("groups", "ctx"), None),
        check_vma=False,
    )
```

```python
import functools

import jax
import jax.numpy as jnp
from jax import lax
from jax.experimental import pallas as pl
from jax.experimental.pallas import tpu as pltpu
from jax.sharding import PartitionSpec as P

WIDTH = 512
FINAL_WIDTH = 2048
RIM = 8
LANES = 128


def from_behind(shard, axis, by):
    peers = lax.axis_size(axis)
    pairs = [(i, i + by) for i in range(peers) if 0 <= i + by < peers]
    return lax.ppermute(shard, axis, pairs)


def split2(x):
    hi = x.astype(jnp.bfloat16)
    lo = (x - hi.astype(jnp.float32)).astype(jnp.bfloat16)
    return hi, lo


def split3(x):
    hi = x.astype(jnp.bfloat16)
    rest = x - hi.astype(jnp.float32)
    mid = rest.astype(jnp.bfloat16)
    lo = (rest - mid.astype(jnp.float32)).astype(jnp.bfloat16)
    return hi, mid, lo


def local_kernel(taps, group_width, spans,
                 xq, xk, xv, rq, rk, rv, wq, wk, wv, e_ref, rt_ref, et_ref,
                 q_out, loc_out, pk_out, dec_out, info_out, ext_s, shift_s, vis_s, tail_s):
    length, width = xq.shape
    groups = width // group_width
    pole_count = rt_ref.shape[1]
    channels = pk_out.shape[1] - LANES
    span_r = e_ref.shape[1]
    step = pl.program_id(0)

    @pl.when(step == 0)
    def _():
        e_row = e_ref[0:1, :]
        t_col = lax.broadcasted_iota(jnp.int32, (length, span_r), 0)
        r_row = lax.broadcasted_iota(jnp.int32, (length, span_r), 1)
        doc_col = jnp.sum(jnp.where(r_row == t_col, e_row, 0.0), axis=1, keepdims=True)
        eq = e_row == doc_col
        place = jnp.where(r_row < length, r_row, r_row - length - RIM)
        for j in range(taps):
            hit = eq & (place == t_col - j) & (r_row < length + RIM)
            shift_s[j * length:(j + 1) * length, :] = jnp.where(hit, 1.0, 0.0).astype(jnp.bfloat16)
        eqf = jnp.where(eq, 1.0, 0.0)
        causal = r_row[:, :length] <= t_col[:, :length]
        vis_s[...] = jnp.where(causal, eqf[:, :length], 0.0)
        tail_s[...] = jnp.broadcast_to(eqf[length - 1:length, :length], tail_s.shape)
        into = eqf[0:1, length + RIM - 1:length + RIM]
        flag = into * eqf[length - 1:length, 0:1]
        pk_out[:, channels:channels + LANES] = jnp.broadcast_to(flag, (pole_count, LANES))
        lane = lax.broadcasted_iota(jnp.int32, info_out.shape, 1)
        info_out[...] = jnp.where(lane == 0, eqf[:, 0:1], jnp.broadcast_to(into, info_out.shape))
        ext_s[...] = jnp.zeros_like(ext_s)


    def conv(x_ref, r_ref, w_ref):
        ext_s[0:length, :] = x_ref[...]
        ext_s[length:length + RIM, :] = r_ref[...]
        ext = ext_s[...]
        w = w_ref[...]
        acc = w[0:1, :] * x_ref[...].astype(jnp.float32)
        for j in range(1, taps):
            window = jnp.dot(shift_s[j * length:(j + 1) * length, :], ext, preferred_element_type=jnp.float32)
            acc = acc + w[j:j + 1, :] * window
        return acc

    cq = conv(xq, rq, wq)
    ck = conv(xk, rk, wk)
    cv = conv(xv, rv, wv)
    q_out[...] = cq
    gated = (ck * cv).astype(jnp.bfloat16)

    lane_group = lax.broadcasted_iota(jnp.int32, (length, width), 1) // group_width
    zero = jnp.zeros_like(gated)
    xbd = jnp.concatenate([jnp.where(lane_group == g, gated, zero) for g in range(groups)], axis=0)

    rt = rt_ref[0]
    et = et_ref[0]
    lane = lax.broadcasted_iota(jnp.int32, (1, length), 1)
    lags = ((length - lane) % length).astype(jnp.float32)
    to_end = (length - 1 - lane).astype(jnp.float32)
    at_tail = tail_s[0:1, :]
    visible = vis_s[...] > 0.5
    pieces = []
    ends = []
    for g in range(groups):
        a_col = rt[:, g:g + 1]
        r_col = et[:, g:g + 1]
        base = jnp.sum(r_col * jnp.exp(-a_col * lags), axis=0, keepdims=True)
        row = jnp.broadcast_to(base.astype(jnp.bfloat16), (length, length))
        rolled = pltpu.roll(row, 0, 1, stride=1, stride_axis=0)
        pieces.append(jnp.where(visible, rolled, jnp.zeros_like(rolled)))
        ends.append(jnp.exp(-a_col * to_end) * at_tail)
    e_hi, e_lo = split2(jnp.concatenate(ends, axis=1))
    t_hi = jnp.concatenate(pieces, axis=1)
    res = jnp.dot(jnp.concatenate([t_hi, e_hi, e_lo], axis=0), xbd, preferred_element_type=jnp.float32)
    loc_out[...] = res[0:length]
    st = res[length:length + pole_count] + res[length + pole_count:length + 2 * pole_count]
    pk_out[:, pl.ds(pl.multiple_of(step * width, width), width)] = st

    spread = (lax.broadcasted_iota(jnp.int32, (groups, width), 1) // group_width
              == lax.broadcasted_iota(jnp.int32, (groups, width), 0)).astype(jnp.bfloat16)
    rate_cols = None
    for piece in split3(rt):
        part = jnp.dot(piece, spread, preferred_element_type=jnp.float32)
        rate_cols = part if rate_cols is None else rate_cols + part
    for r, span in enumerate(spans):
        dec_out[r] = jnp.exp(-rate_cols * span)


def final_kernel(group_width, pole_count, sub, hb, q_ref, loc_ref, zo_ref, zp_ref, pk_ref, gt_ref, pf_ref, gf_ref,
                 d1_ref, rr_ref, info_ref, o_ref):
    length, width = q_ref.shape
    groups = sub // group_width
    core = lax.axis_index("ctx") % 2
    odd = core == 1
    mine_half = (pl.program_id(0) // hb) == core
    full = jnp.where(mine_half, zo_ref[...], zp_ref[...])
    even_s = jnp.where(odd, gt_ref[...], pk_ref[...])
    even_f = jnp.where(odd, gf_ref[:, 0:1], pf_ref[:, 0:1])
    joined = jnp.where(odd, (even_f * d1_ref[0]) * full + even_s, full)
    b_all = joined * info_ref[0:1, 1:2]
    tcol = (lax.broadcasted_iota(jnp.int32, (length, 1), 0) + 1).astype(jnp.float32)
    iw = rr_ref[1] * jnp.exp(-rr_ref[0] * tcol) * info_ref[:, 0:1]
    iw_hi, iw_lo = split2(iw)
    shape = (groups * pole_count, sub)
    row_group = lax.broadcasted_iota(jnp.int32, shape, 0) // pole_count
    lane_group = lax.broadcasted_iota(jnp.int32, shape, 1) // group_width
    same = row_group == lane_group
    for s in range(width // sub):
        cols = slice(s * sub, (s + 1) * sub)
        tiled = jnp.concatenate([b_all[:, cols]] * groups, axis=0)
        b_hi, b_lo = split2(jnp.where(same, tiled, 0.0))
        poles = slice(s * shape[0], (s + 1) * shape[0])
        ih = iw_hi[:, poles]
        car = jnp.dot(ih, b_hi, preferred_element_type=jnp.float32)
        car = car + jnp.dot(ih, b_lo, preferred_element_type=jnp.float32)
        car = car + jnp.dot(iw_lo[:, poles], b_hi, preferred_element_type=jnp.float32)
        o_ref[:, cols] = (q_ref[:, cols] * (loc_ref[:, cols] + car)).astype(o_ref.dtype)


def swap_cores(shard, axis):
    peers = lax.axis_size(axis)
    return lax.ppermute(shard, axis, [(i, i ^ 1) for i in range(peers)])


def chip_scan(packed, decays, span_of, channels, pole_count, peers, me):
    core = me % 2
    odd = core == 1
    half = channels // 2
    mine = lambda x: lax.dynamic_slice_in_dim(x, core * half, half, axis=1)
    got = swap_cores(packed, "ctx")
    own_s, own_f = packed[:, :channels], packed[:, channels:channels + 1]
    other_s, other_f = got[:, :channels], got[:, channels:channels + 1]
    even_s = jnp.where(odd, other_s, own_s)
    odd_s = jnp.where(odd, own_s, other_s)
    even_f = jnp.where(odd, other_f, own_f)
    odd_f = jnp.where(odd, own_f, other_f)
    total = (odd_f * mine(decays[span_of[1]])) * mine(even_s) + mine(odd_s)
    flag = even_f * odd_f
    chips = peers // 2
    prefix = jnp.zeros_like(total)
    prefix_flag = jnp.ones_like(flag)
    offset = 1
    while offset < chips:
        load = jnp.concatenate([total, jnp.broadcast_to(flag, (pole_count, LANES))], axis=1)
        got_load = from_behind(load, "ctx", 2 * offset)
        came, came_flag = got_load[:, :half], got_load[:, half:half + 1]
        if offset == 1:
            prefix = prefix + prefix_flag * came
        else:
            prefix = prefix + (prefix_flag * mine(decays[span_of[2 * offset - 2]])) * came
        prefix_flag = prefix_flag * came_flag
        if 2 * offset < chips:
            total = total + (flag * mine(decays[span_of[2 * offset]])) * came
            flag = flag * came_flag
        offset *= 2
    return prefix, swap_cores(prefix, "ctx"), got


def scan_spans(peers):
    chips = peers // 2
    spans = {1}
    offset = 1
    while offset < chips:
        if offset > 1:
            spans.add(2 * offset - 2)
        if 2 * offset < chips:
            spans.add(2 * offset)
        offset *= 2
    return sorted(spans)


def on_device(qkv, doc_ids, short_w, rates, residues):
    length = qkv.shape[0]
    taps = short_w.shape[0]
    channels = qkv.shape[1] // 3
    filters, pole_count = rates.shape
    group_width = channels // filters
    width = min(WIDTH, channels)
    nb = channels // width
    gpb = width // group_width
    final_width = min(FINAL_WIDTH, channels)
    peers = lax.axis_size("ctx")
    me = lax.axis_index("ctx")

    tail_docs = jnp.broadcast_to(doc_ids[length - RIM:, None].astype(jnp.bfloat16), (RIM, LANES))
    rim = from_behind(jnp.concatenate([qkv[length - RIM:], tail_docs], axis=1), "ctx", 1)
    prev_docs = rim[:, 3 * channels].astype(jnp.int32)
    prev_last = prev_docs[RIM - 1]

    span_r = 2 * LANES
    e_vec = jnp.concatenate([doc_ids, prev_docs, jnp.full((span_r - length - RIM,), -1, jnp.int32)]).astype(jnp.float32)
    e_rows = jnp.broadcast_to(e_vec[None, :], (8, span_r))

    both_t = jnp.stack([rates, residues]).reshape(2, nb, gpb, pole_count).transpose(0, 1, 3, 2)
    rates_t, residues_t = both_t[0], both_t[1]
    span_list = scan_spans(peers)
    span_of = {v: i for i, v in enumerate(span_list)}
    rounds = len(span_list)
    spans = tuple(float(length * v) for v in span_list)

    col = lambda off: (lambda j: (0, j + off))
    fixed = lambda j: (0, 0)
    q_part, local_part, packed, decays, info = pl.pallas_call(
        functools.partial(local_kernel, taps, group_width, spans),
        grid=(nb,),
        in_specs=[
            pl.BlockSpec((length, width), col(0)),
            pl.BlockSpec((length, width), col(nb)),
            pl.BlockSpec((length, width), col(2 * nb)),
            pl.BlockSpec((RIM, width), col(0)),
            pl.BlockSpec((RIM, width), col(nb)),
            pl.BlockSpec((RIM, width), col(2 * nb)),
            pl.BlockSpec((taps, width), col(0)),
            pl.BlockSpec((taps, width), col(nb)),
            pl.BlockSpec((taps, width), col(2 * nb)),
            pl.BlockSpec((8, span_r), fixed),
            pl.BlockSpec((1, pole_count, gpb), lambda j: (j, 0, 0)),
            pl.BlockSpec((1, pole_count, gpb), lambda j: (j, 0, 0)),
        ],
        out_specs=[
            pl.BlockSpec((length, width), col(0)),
            pl.BlockSpec((length, width), col(0)),
            pl.BlockSpec((pole_count, channels + LANES), fixed),
            pl.BlockSpec((rounds, pole_count, width), lambda j: (0, 0, j)),
            pl.BlockSpec((length, LANES), fixed),
        ],
        out_shape=[
            jax.ShapeDtypeStruct((length, channels), jnp.float32),
            jax.ShapeDtypeStruct((length, channels), jnp.float32),
            jax.ShapeDtypeStruct((pole_count, channels + LANES), jnp.float32),
            jax.ShapeDtypeStruct((rounds, pole_count, channels), jnp.float32),
            jax.ShapeDtypeStruct((length, LANES), jnp.float32),
        ],
        scratch_shapes=[
            pltpu.VMEM((span_r, width), jnp.bfloat16),
            pltpu.VMEM((taps * length, span_r), jnp.bfloat16),
            pltpu.VMEM((length, length), jnp.float32),
            pltpu.VMEM((8, length), jnp.float32),
        ],
        compiler_params=pltpu.CompilerParams(dimension_semantics=("arbitrary",)),
    )(qkv, qkv, qkv, rim, rim, rim, short_w, short_w, short_w, e_rows, rates_t, residues_t)

    prefix, partner, got = chip_scan(packed, decays, span_of, channels, pole_count, peers, me)
    half = channels // 2
    hb = max(half // final_width, 1)
    flag_block = channels // LANES
    rate_rows = jnp.stack([rates, residues]).reshape(2, 1, filters * pole_count)

    nbf = channels // final_width
    iw_width = final_width // group_width * pole_count
    return pl.pallas_call(
        functools.partial(final_kernel, group_width, pole_count, min(256, width), hb),
        grid=(nbf,),
        in_specs=[
            pl.BlockSpec((length, final_width), col(0)),
            pl.BlockSpec((length, final_width), col(0)),
            pl.BlockSpec((pole_count, final_width), lambda j: (0, j % hb)),
            pl.BlockSpec((pole_count, final_width), lambda j: (0, j % hb)),
            pl.BlockSpec((pole_count, final_width), col(0)),
            pl.BlockSpec((pole_count, final_width), col(0)),
            pl.BlockSpec((pole_count, LANES), lambda j: (0, flag_block)),
            pl.BlockSpec((pole_count, LANES), lambda j: (0, flag_block)),
            pl.BlockSpec((1, pole_count, final_width), lambda j: (span_of[1], 0, j)),
            pl.BlockSpec((2, 1, iw_width), lambda j: (0, 0, j)),
            pl.BlockSpec((length, LANES), fixed),
        ],
        out_specs=pl.BlockSpec((length, final_width), col(0)),
        out_shape=jax.ShapeDtypeStruct((length, channels), jnp.bfloat16),
        compiler_params=pltpu.CompilerParams(dimension_semantics=("arbitrary",)),
    )(q_part, local_part, prefix, partner, packed, got, packed, got, decays, rate_rows, info)


def solution(mesh):
    return jax.shard_map(
        on_device,
        mesh=mesh,
        in_specs=(P(("groups", "ctx"), None), P(("groups", "ctx")), P(), P(), P()),
        out_specs=P(("groups", "ctx"), None),
        check_vma=False,
    )
```

```python
import functools

import jax
import jax.numpy as jnp
from jax import lax
from jax.experimental import pallas as pl
from jax.experimental.pallas import tpu as pltpu
from jax.sharding import PartitionSpec as P

WIDTH = 512
FINAL_WIDTH = 2048
RIM = 8
SUB = 256
LANES = 128


def from_behind(shard, axis, by):
    peers = lax.axis_size(axis)
    pairs = [(i, i + by) for i in range(peers) if 0 <= i + by < peers]
    return lax.ppermute(shard, axis, pairs)


def split2(x):
    hi = x.astype(jnp.bfloat16)
    lo = (x - hi.astype(jnp.float32)).astype(jnp.bfloat16)
    return hi, lo


def split3(x):
    hi = x.astype(jnp.bfloat16)
    rest = x - hi.astype(jnp.float32)
    mid = rest.astype(jnp.bfloat16)
    lo = (rest - mid.astype(jnp.float32)).astype(jnp.bfloat16)
    return hi, mid, lo


def local_kernel(taps, group_width, spans,
                 xq, xk, xv, rq, rk, rv, wq, wk, wv, e_ref, rt_ref, et_ref,
                 q_out, loc_out, pk_out, dec_out, info_out, ext_s, shift_s, vis_s, tail_s):
    length, width = xq.shape
    groups = width // group_width
    pole_count = rt_ref.shape[1]
    channels = pk_out.shape[1] - LANES
    span_r = e_ref.shape[1]
    step = pl.program_id(0)

    @pl.when(step == 0)
    def _():
        e_row = e_ref[0:1, :]
        t_col = lax.broadcasted_iota(jnp.int32, (length, span_r), 0)
        r_row = lax.broadcasted_iota(jnp.int32, (length, span_r), 1)
        doc_col = jnp.sum(jnp.where(r_row == t_col, e_row, 0.0), axis=1, keepdims=True)
        eq = e_row == doc_col
        place = jnp.where(r_row < length, r_row, r_row - length - RIM)
        for j in range(taps):
            hit = eq & (place == t_col - j) & (r_row < length + RIM)
            shift_s[j * length:(j + 1) * length, :] = jnp.where(hit, 1.0, 0.0).astype(jnp.bfloat16)
        eqf = jnp.where(eq, 1.0, 0.0)
        causal = r_row[:, :length] <= t_col[:, :length]
        vis_s[...] = jnp.where(causal, eqf[:, :length], 0.0)
        tail_s[...] = jnp.broadcast_to(eqf[length - 1:length, :length], tail_s.shape)
        into = eqf[0:1, length + RIM - 1:length + RIM]
        flag = into * eqf[length - 1:length, 0:1]
        pk_out[:, channels:channels + LANES] = jnp.broadcast_to(flag, (pole_count, LANES))
        lane = lax.broadcasted_iota(jnp.int32, info_out.shape, 1)
        info_out[...] = jnp.where(lane == 0, eqf[:, 0:1], jnp.broadcast_to(into, info_out.shape))
        ext_s[...] = jnp.zeros_like(ext_s)


    def conv(x_ref, r_ref, w_ref):
        ext_s[0:length, :] = x_ref[...]
        ext_s[length:length + RIM, :] = r_ref[...]
        ext = ext_s[...]
        w = w_ref[...]
        acc = w[0:1, :] * x_ref[...].astype(jnp.float32)
        for j in range(1, taps):
            window = jnp.dot(shift_s[j * length:(j + 1) * length, :], ext, preferred_element_type=jnp.float32)
            acc = acc + w[j:j + 1, :] * window
        return acc

    cq = conv(xq, rq, wq)
    ck = conv(xk, rk, wk)
    cv = conv(xv, rv, wv)
    q_out[...] = cq
    gated = (ck * cv).astype(jnp.bfloat16)

    rt = rt_ref[0]
    et = et_ref[0]
    lane = lax.broadcasted_iota(jnp.int32, (1, length), 1)
    lags = ((length - lane) % length).astype(jnp.float32)
    to_end = (length - 1 - lane).astype(jnp.float32)
    at_tail = tail_s[0:1, :]
    visible = vis_s[...] > 0.5
    sub = min(SUB, width)
    sub_groups = sub // group_width
    lane_group = lax.broadcasted_iota(jnp.int32, (length, sub), 1) // group_width
    for h in range(width // sub):
        part = gated[:, h * sub:(h + 1) * sub]
        zero = jnp.zeros_like(part)
        xbd = jnp.concatenate([jnp.where(lane_group == g, part, zero) for g in range(sub_groups)], axis=0)
        pieces = []
        ends = []
        for g in range(h * sub_groups, (h + 1) * sub_groups):
            a_col = rt[:, g:g + 1]
            r_col = et[:, g:g + 1]
            base = jnp.sum(r_col * jnp.exp(-a_col * lags), axis=0, keepdims=True)
            row = jnp.broadcast_to(base.astype(jnp.bfloat16), (length, length))
            rolled = pltpu.roll(row, 0, 1, stride=1, stride_axis=0)
            pieces.append(jnp.where(visible, rolled, jnp.zeros_like(rolled)))
            ends.append(jnp.exp(-a_col * to_end) * at_tail)
        e_hi, e_lo = split2(jnp.concatenate(ends, axis=1))
        t_hi = jnp.concatenate(pieces, axis=1)
        res = jnp.dot(jnp.concatenate([t_hi, e_hi, e_lo], axis=0), xbd, preferred_element_type=jnp.float32)
        loc_out[:, h * sub:(h + 1) * sub] = res[0:length]
        st = res[length:length + pole_count] + res[length + pole_count:length + 2 * pole_count]
        pk_out[:, pl.ds(pl.multiple_of(step * width + h * sub, sub), sub)] = st

    spread = (lax.broadcasted_iota(jnp.int32, (groups, width), 1) // group_width
              == lax.broadcasted_iota(jnp.int32, (groups, width), 0)).astype(jnp.bfloat16)
    rate_cols = None
    for piece in split3(rt):
        part = jnp.dot(piece, spread, preferred_element_type=jnp.float32)
        rate_cols = part if rate_cols is None else rate_cols + part
    for r, span in enumerate(spans):
        dec_out[r] = jnp.exp(-rate_cols * span)


def final_kernel(group_width, pole_count, sub, hb, q_ref, loc_ref, zo_ref, zp_ref, pk_ref, gt_ref, pf_ref, gf_ref,
                 d1_ref, rr_ref, info_ref, o_ref):
    length, width = q_ref.shape
    groups = sub // group_width
    core = lax.axis_index("ctx") % 2
    odd = core == 1
    mine_half = (pl.program_id(0) // hb) == core
    full = jnp.where(mine_half, zo_ref[...], zp_ref[...])
    even_s = jnp.where(odd, gt_ref[...], pk_ref[...])
    even_f = jnp.where(odd, gf_ref[:, 0:1], pf_ref[:, 0:1])
    joined = jnp.where(odd, (even_f * d1_ref[0]) * full + even_s, full)
    b_all = joined * info_ref[0:1, 1:2]
    tcol = (lax.broadcasted_iota(jnp.int32, (length, 1), 0) + 1).astype(jnp.float32)
    iw = rr_ref[1] * jnp.exp(-rr_ref[0] * tcol) * info_ref[:, 0:1]
    iw_hi, iw_lo = split2(iw)
    shape = (groups * pole_count, sub)
    row_group = lax.broadcasted_iota(jnp.int32, shape, 0) // pole_count
    lane_group = lax.broadcasted_iota(jnp.int32, shape, 1) // group_width
    same = row_group == lane_group
    for s in range(width // sub):
        cols = slice(s * sub, (s + 1) * sub)
        tiled = jnp.concatenate([b_all[:, cols]] * groups, axis=0)
        b_hi, b_lo = split2(jnp.where(same, tiled, 0.0))
        poles = slice(s * shape[0], (s + 1) * shape[0])
        ih = iw_hi[:, poles]
        car = jnp.dot(ih, b_hi, preferred_element_type=jnp.float32)
        car = car + jnp.dot(ih, b_lo, preferred_element_type=jnp.float32)
        car = car + jnp.dot(iw_lo[:, poles], b_hi, preferred_element_type=jnp.float32)
        o_ref[:, cols] = (q_ref[:, cols] * (loc_ref[:, cols] + car)).astype(o_ref.dtype)


def swap_cores(shard, axis):
    peers = lax.axis_size(axis)
    return lax.ppermute(shard, axis, [(i, i ^ 1) for i in range(peers)])


def chip_scan(packed, decays, span_of, channels, pole_count, peers, me):
    core = me % 2
    odd = core == 1
    half = channels // 2
    mine = lambda x: lax.dynamic_slice_in_dim(x, core * half, half, axis=1)
    got = swap_cores(packed, "ctx")
    own_s, own_f = packed[:, :channels], packed[:, channels:channels + 1]
    other_s, other_f = got[:, :channels], got[:, channels:channels + 1]
    even_s = jnp.where(odd, other_s, own_s)
    odd_s = jnp.where(odd, own_s, other_s)
    even_f = jnp.where(odd, other_f, own_f)
    odd_f = jnp.where(odd, own_f, other_f)
    total = (odd_f * mine(decays[span_of[1]])) * mine(even_s) + mine(odd_s)
    flag = even_f * odd_f
    chips = peers // 2
    prefix = jnp.zeros_like(total)
    prefix_flag = jnp.ones_like(flag)
    offset = 1
    while offset < chips:
        load = jnp.concatenate([total, jnp.broadcast_to(flag, (pole_count, LANES))], axis=1)
        got_load = from_behind(load, "ctx", 2 * offset)
        came, came_flag = got_load[:, :half], got_load[:, half:half + 1]
        if offset == 1:
            prefix = prefix + prefix_flag * came
        else:
            prefix = prefix + (prefix_flag * mine(decays[span_of[2 * offset - 2]])) * came
        prefix_flag = prefix_flag * came_flag
        if 2 * offset < chips:
            total = total + (flag * mine(decays[span_of[2 * offset]])) * came
            flag = flag * came_flag
        offset *= 2
    return prefix, swap_cores(prefix, "ctx"), got


def scan_spans(peers):
    chips = peers // 2
    spans = {1}
    offset = 1
    while offset < chips:
        if offset > 1:
            spans.add(2 * offset - 2)
        if 2 * offset < chips:
            spans.add(2 * offset)
        offset *= 2
    return sorted(spans)


def on_device(qkv, doc_ids, short_w, rates, residues):
    length = qkv.shape[0]
    taps = short_w.shape[0]
    channels = qkv.shape[1] // 3
    filters, pole_count = rates.shape
    group_width = channels // filters
    width = min(WIDTH, channels)
    nb = channels // width
    gpb = width // group_width
    final_width = min(FINAL_WIDTH, channels)
    peers = lax.axis_size("ctx")
    me = lax.axis_index("ctx")

    tail_docs = jnp.broadcast_to(doc_ids[length - RIM:, None].astype(jnp.bfloat16), (RIM, LANES))
    rim = from_behind(jnp.concatenate([qkv[length - RIM:], tail_docs], axis=1), "ctx", 1)
    prev_docs = rim[:, 3 * channels].astype(jnp.int32)
    prev_last = prev_docs[RIM - 1]

    span_r = 2 * LANES
    e_vec = jnp.concatenate([doc_ids, prev_docs, jnp.full((span_r - length - RIM,), -1, jnp.int32)]).astype(jnp.float32)
    e_rows = jnp.broadcast_to(e_vec[None, :], (8, span_r))

    both_t = jnp.stack([rates, residues]).reshape(2, nb, gpb, pole_count).transpose(0, 1, 3, 2)
    rates_t, residues_t = both_t[0], both_t[1]
    span_list = scan_spans(peers)
    span_of = {v: i for i, v in enumerate(span_list)}
    rounds = len(span_list)
    spans = tuple(float(length * v) for v in span_list)

    col = lambda off: (lambda j: (0, j + off))
    fixed = lambda j: (0, 0)
    q_part, local_part, packed, decays, info = pl.pallas_call(
        functools.partial(local_kernel, taps, group_width, spans),
        grid=(nb,),
        in_specs=[
            pl.BlockSpec((length, width), col(0)),
            pl.BlockSpec((length, width), col(nb)),
            pl.BlockSpec((length, width), col(2 * nb)),
            pl.BlockSpec((RIM, width), col(0)),
            pl.BlockSpec((RIM, width), col(nb)),
            pl.BlockSpec((RIM, width), col(2 * nb)),
            pl.BlockSpec((taps, width), col(0)),
            pl.BlockSpec((taps, width), col(nb)),
            pl.BlockSpec((taps, width), col(2 * nb)),
            pl.BlockSpec((8, span_r), fixed),
            pl.BlockSpec((1, pole_count, gpb), lambda j: (j, 0, 0)),
            pl.BlockSpec((1, pole_count, gpb), lambda j: (j, 0, 0)),
        ],
        out_specs=[
            pl.BlockSpec((length, width), col(0)),
            pl.BlockSpec((length, width), col(0)),
            pl.BlockSpec((pole_count, channels + LANES), fixed),
            pl.BlockSpec((rounds, pole_count, width), lambda j: (0, 0, j)),
            pl.BlockSpec((length, LANES), fixed),
        ],
        out_shape=[
            jax.ShapeDtypeStruct((length, channels), jnp.float32),
            jax.ShapeDtypeStruct((length, channels), jnp.float32),
            jax.ShapeDtypeStruct((pole_count, channels + LANES), jnp.float32),
            jax.ShapeDtypeStruct((rounds, pole_count, channels), jnp.float32),
            jax.ShapeDtypeStruct((length, LANES), jnp.float32),
        ],
        scratch_shapes=[
            pltpu.VMEM((span_r, width), jnp.bfloat16),
            pltpu.VMEM((taps * length, span_r), jnp.bfloat16),
            pltpu.VMEM((length, length), jnp.float32),
            pltpu.VMEM((8, length), jnp.float32),
        ],
        compiler_params=pltpu.CompilerParams(dimension_semantics=("arbitrary",)),
    )(qkv, qkv, qkv, rim, rim, rim, short_w, short_w, short_w, e_rows, rates_t, residues_t)

    prefix, partner, got = chip_scan(packed, decays, span_of, channels, pole_count, peers, me)
    half = channels // 2
    hb = max(half // final_width, 1)
    flag_block = channels // LANES
    rate_rows = jnp.stack([rates, residues]).reshape(2, 1, filters * pole_count)

    nbf = channels // final_width
    iw_width = final_width // group_width * pole_count
    return pl.pallas_call(
        functools.partial(final_kernel, group_width, pole_count, min(256, width), hb),
        grid=(nbf,),
        in_specs=[
            pl.BlockSpec((length, final_width), col(0)),
            pl.BlockSpec((length, final_width), col(0)),
            pl.BlockSpec((pole_count, final_width), lambda j: (0, j % hb)),
            pl.BlockSpec((pole_count, final_width), lambda j: (0, j % hb)),
            pl.BlockSpec((pole_count, final_width), col(0)),
            pl.BlockSpec((pole_count, final_width), col(0)),
            pl.BlockSpec((pole_count, LANES), lambda j: (0, flag_block)),
            pl.BlockSpec((pole_count, LANES), lambda j: (0, flag_block)),
            pl.BlockSpec((1, pole_count, final_width), lambda j: (span_of[1], 0, j)),
            pl.BlockSpec((2, 1, iw_width), lambda j: (0, 0, j)),
            pl.BlockSpec((length, LANES), fixed),
        ],
        out_specs=pl.BlockSpec((length, final_width), col(0)),
        out_shape=jax.ShapeDtypeStruct((length, channels), jnp.bfloat16),
        compiler_params=pltpu.CompilerParams(dimension_semantics=("arbitrary",)),
    )(q_part, local_part, prefix, partner, packed, got, packed, got, decays, rate_rows, info)


def solution(mesh):
    return jax.shard_map(
        on_device,
        mesh=mesh,
        in_specs=(P(("groups", "ctx"), None), P(("groups", "ctx")), P(), P(), P()),
        out_specs=P(("groups", "ctx"), None),
        check_vma=False,
    )
```

```python
import functools

import jax
import jax.numpy as jnp
from jax import lax
from jax.experimental import pallas as pl
from jax.experimental.pallas import tpu as pltpu
from jax.sharding import PartitionSpec as P

WIDTH = 1024
FINAL_WIDTH = 2048
RIM = 8
SUB = 256
LANES = 128


def from_behind(shard, axis, by):
    peers = lax.axis_size(axis)
    pairs = [(i, i + by) for i in range(peers) if 0 <= i + by < peers]
    return lax.ppermute(shard, axis, pairs)


def split2(x):
    hi = x.astype(jnp.bfloat16)
    lo = (x - hi.astype(jnp.float32)).astype(jnp.bfloat16)
    return hi, lo


def split3(x):
    hi = x.astype(jnp.bfloat16)
    rest = x - hi.astype(jnp.float32)
    mid = rest.astype(jnp.bfloat16)
    lo = (rest - mid.astype(jnp.float32)).astype(jnp.bfloat16)
    return hi, mid, lo


def local_kernel(taps, group_width, spans,
                 xq, xk, xv, rq, rk, rv, wq, wk, wv, e_ref, rt_ref, et_ref,
                 q_out, loc_out, pk_out, dec_out, info_out, ext_s, shift_s, vis_s, tail_s):
    length, width = xq.shape
    groups = width // group_width
    pole_count = rt_ref.shape[1]
    channels = pk_out.shape[1] - LANES
    span_r = e_ref.shape[1]
    step = pl.program_id(0)

    @pl.when(step == 0)
    def _():
        e_row = e_ref[0:1, :]
        t_col = lax.broadcasted_iota(jnp.int32, (length, span_r), 0)
        r_row = lax.broadcasted_iota(jnp.int32, (length, span_r), 1)
        doc_col = jnp.sum(jnp.where(r_row == t_col, e_row, 0.0), axis=1, keepdims=True)
        eq = e_row == doc_col
        place = jnp.where(r_row < length, r_row, r_row - length - RIM)
        for j in range(taps):
            hit = eq & (place == t_col - j) & (r_row < length + RIM)
            shift_s[j * length:(j + 1) * length, :] = jnp.where(hit, 1.0, 0.0).astype(jnp.bfloat16)
        eqf = jnp.where(eq, 1.0, 0.0)
        causal = r_row[:, :length] <= t_col[:, :length]
        vis_s[...] = jnp.where(causal, eqf[:, :length], 0.0)
        tail_s[...] = jnp.broadcast_to(eqf[length - 1:length, :length], tail_s.shape)
        into = eqf[0:1, length + RIM - 1:length + RIM]
        flag = into * eqf[length - 1:length, 0:1]
        pk_out[:, channels:channels + LANES] = jnp.broadcast_to(flag, (pole_count, LANES))
        lane = lax.broadcasted_iota(jnp.int32, info_out.shape, 1)
        info_out[...] = jnp.where(lane == 0, eqf[:, 0:1], jnp.broadcast_to(into, info_out.shape))
        ext_s[...] = jnp.zeros_like(ext_s)


    def conv(x_ref, r_ref, w_ref):
        ext_s[0:length, :] = x_ref[...]
        ext_s[length:length + RIM, :] = r_ref[...]
        ext = ext_s[...]
        w = w_ref[...]
        acc = w[0:1, :] * x_ref[...].astype(jnp.float32)
        for j in range(1, taps):
            window = jnp.dot(shift_s[j * length:(j + 1) * length, :], ext, preferred_element_type=jnp.float32)
            acc = acc + w[j:j + 1, :] * window
        return acc

    cq = conv(xq, rq, wq)
    ck = conv(xk, rk, wk)
    cv = conv(xv, rv, wv)
    q_out[...] = cq
    gated = (ck * cv).astype(jnp.bfloat16)

    rt = rt_ref[0]
    et = et_ref[0]
    lane = lax.broadcasted_iota(jnp.int32, (1, length), 1)
    lags = ((length - lane) % length).astype(jnp.float32)
    to_end = (length - 1 - lane).astype(jnp.float32)
    at_tail = tail_s[0:1, :]
    visible = vis_s[...] > 0.5
    sub = min(SUB, width)
    sub_groups = sub // group_width
    lane_group = lax.broadcasted_iota(jnp.int32, (length, sub), 1) // group_width
    for h in range(width // sub):
        part = gated[:, h * sub:(h + 1) * sub]
        zero = jnp.zeros_like(part)
        xbd = jnp.concatenate([jnp.where(lane_group == g, part, zero) for g in range(sub_groups)], axis=0)
        pieces = []
        ends = []
        for g in range(h * sub_groups, (h + 1) * sub_groups):
            a_col = rt[:, g:g + 1]
            r_col = et[:, g:g + 1]
            base = jnp.sum(r_col * jnp.exp(-a_col * lags), axis=0, keepdims=True)
            row = jnp.broadcast_to(base.astype(jnp.bfloat16), (length, length))
            rolled = pltpu.roll(row, 0, 1, stride=1, stride_axis=0)
            pieces.append(jnp.where(visible, rolled, jnp.zeros_like(rolled)))
            ends.append(jnp.exp(-a_col * to_end) * at_tail)
        e_hi, e_lo = split2(jnp.concatenate(ends, axis=1))
        t_hi = jnp.concatenate(pieces, axis=1)
        res = jnp.dot(jnp.concatenate([t_hi, e_hi, e_lo], axis=0), xbd, preferred_element_type=jnp.float32)
        loc_out[:, h * sub:(h + 1) * sub] = res[0:length]
        st = res[length:length + pole_count] + res[length + pole_count:length + 2 * pole_count]
        pk_out[:, pl.ds(pl.multiple_of(step * width + h * sub, sub), sub)] = st

    spread = (lax.broadcasted_iota(jnp.int32, (groups, width), 1) // group_width
              == lax.broadcasted_iota(jnp.int32, (groups, width), 0)).astype(jnp.bfloat16)
    rate_cols = None
    for piece in split3(rt):
        part = jnp.dot(piece, spread, preferred_element_type=jnp.float32)
        rate_cols = part if rate_cols is None else rate_cols + part
    for r, span in enumerate(spans):
        dec_out[r] = jnp.exp(-rate_cols * span)


def final_kernel(group_width, pole_count, sub, hb, q_ref, loc_ref, zo_ref, zp_ref, pk_ref, gt_ref, pf_ref, gf_ref,
                 d1_ref, rr_ref, info_ref, o_ref):
    length, width = q_ref.shape
    groups = sub // group_width
    core = lax.axis_index("ctx") % 2
    odd = core == 1
    mine_half = (pl.program_id(0) // hb) == core
    full = jnp.where(mine_half, zo_ref[...], zp_ref[...])
    even_s = jnp.where(odd, gt_ref[...], pk_ref[...])
    even_f = jnp.where(odd, gf_ref[:, 0:1], pf_ref[:, 0:1])
    joined = jnp.where(odd, (even_f * d1_ref[0]) * full + even_s, full)
    b_all = joined * info_ref[0:1, 1:2]
    tcol = (lax.broadcasted_iota(jnp.int32, (length, 1), 0) + 1).astype(jnp.float32)
    iw = rr_ref[1] * jnp.exp(-rr_ref[0] * tcol) * info_ref[:, 0:1]
    iw_hi, iw_lo = split2(iw)
    shape = (groups * pole_count, sub)
    row_group = lax.broadcasted_iota(jnp.int32, shape, 0) // pole_count
    lane_group = lax.broadcasted_iota(jnp.int32, shape, 1) // group_width
    same = row_group == lane_group
    for s in range(width // sub):
        cols = slice(s * sub, (s + 1) * sub)
        tiled = jnp.concatenate([b_all[:, cols]] * groups, axis=0)
        b_hi, b_lo = split2(jnp.where(same, tiled, 0.0))
        poles = slice(s * shape[0], (s + 1) * shape[0])
        ih = iw_hi[:, poles]
        car = jnp.dot(ih, b_hi, preferred_element_type=jnp.float32)
        car = car + jnp.dot(ih, b_lo, preferred_element_type=jnp.float32)
        car = car + jnp.dot(iw_lo[:, poles], b_hi, preferred_element_type=jnp.float32)
        o_ref[:, cols] = (q_ref[:, cols] * (loc_ref[:, cols] + car)).astype(o_ref.dtype)


def swap_cores(shard, axis):
    peers = lax.axis_size(axis)
    return lax.ppermute(shard, axis, [(i, i ^ 1) for i in range(peers)])


def chip_scan(packed, decays, span_of, channels, pole_count, peers, me):
    core = me % 2
    odd = core == 1
    half = channels // 2
    mine = lambda x: lax.dynamic_slice_in_dim(x, core * half, half, axis=1)
    got = swap_cores(packed, "ctx")
    own_s, own_f = packed[:, :channels], packed[:, channels:channels + 1]
    other_s, other_f = got[:, :channels], got[:, channels:channels + 1]
    even_s = jnp.where(odd, other_s, own_s)
    odd_s = jnp.where(odd, own_s, other_s)
    even_f = jnp.where(odd, other_f, own_f)
    odd_f = jnp.where(odd, own_f, other_f)
    total = (odd_f * mine(decays[span_of[1]])) * mine(even_s) + mine(odd_s)
    flag = even_f * odd_f
    chips = peers // 2
    prefix = jnp.zeros_like(total)
    prefix_flag = jnp.ones_like(flag)
    offset = 1
    while offset < chips:
        load = jnp.concatenate([total, jnp.broadcast_to(flag, (pole_count, LANES))], axis=1)
        got_load = from_behind(load, "ctx", 2 * offset)
        came, came_flag = got_load[:, :half], got_load[:, half:half + 1]
        if offset == 1:
            prefix = prefix + prefix_flag * came
        else:
            prefix = prefix + (prefix_flag * mine(decays[span_of[2 * offset - 2]])) * came
        prefix_flag = prefix_flag * came_flag
        if 2 * offset < chips:
            total = total + (flag * mine(decays[span_of[2 * offset]])) * came
            flag = flag * came_flag
        offset *= 2
    return prefix, swap_cores(prefix, "ctx"), got


def scan_spans(peers):
    chips = peers // 2
    spans = {1}
    offset = 1
    while offset < chips:
        if offset > 1:
            spans.add(2 * offset - 2)
        if 2 * offset < chips:
            spans.add(2 * offset)
        offset *= 2
    return sorted(spans)


def on_device(qkv, doc_ids, short_w, rates, residues):
    length = qkv.shape[0]
    taps = short_w.shape[0]
    channels = qkv.shape[1] // 3
    filters, pole_count = rates.shape
    group_width = channels // filters
    width = min(WIDTH, channels)
    nb = channels // width
    gpb = width // group_width
    final_width = min(FINAL_WIDTH, channels)
    peers = lax.axis_size("ctx")
    me = lax.axis_index("ctx")

    tail_docs = jnp.broadcast_to(doc_ids[length - RIM:, None].astype(jnp.bfloat16), (RIM, LANES))
    rim = from_behind(jnp.concatenate([qkv[length - RIM:], tail_docs], axis=1), "ctx", 1)
    prev_docs = rim[:, 3 * channels].astype(jnp.int32)
    prev_last = prev_docs[RIM - 1]

    span_r = 2 * LANES
    e_vec = jnp.concatenate([doc_ids, prev_docs, jnp.full((span_r - length - RIM,), -1, jnp.int32)]).astype(jnp.float32)
    e_rows = jnp.broadcast_to(e_vec[None, :], (8, span_r))

    both_t = jnp.stack([rates, residues]).reshape(2, nb, gpb, pole_count).transpose(0, 1, 3, 2)
    rates_t, residues_t = both_t[0], both_t[1]
    span_list = scan_spans(peers)
    span_of = {v: i for i, v in enumerate(span_list)}
    rounds = len(span_list)
    spans = tuple(float(length * v) for v in span_list)

    col = lambda off: (lambda j: (0, j + off))
    fixed = lambda j: (0, 0)
    q_part, local_part, packed, decays, info = pl.pallas_call(
        functools.partial(local_kernel, taps, group_width, spans),
        grid=(nb,),
        in_specs=[
            pl.BlockSpec((length, width), col(0)),
            pl.BlockSpec((length, width), col(nb)),
            pl.BlockSpec((length, width), col(2 * nb)),
            pl.BlockSpec((RIM, width), col(0)),
            pl.BlockSpec((RIM, width), col(nb)),
            pl.BlockSpec((RIM, width), col(2 * nb)),
            pl.BlockSpec((taps, width), col(0)),
            pl.BlockSpec((taps, width), col(nb)),
            pl.BlockSpec((taps, width), col(2 * nb)),
            pl.BlockSpec((8, span_r), fixed),
            pl.BlockSpec((1, pole_count, gpb), lambda j: (j, 0, 0)),
            pl.BlockSpec((1, pole_count, gpb), lambda j: (j, 0, 0)),
        ],
        out_specs=[
            pl.BlockSpec((length, width), col(0)),
            pl.BlockSpec((length, width), col(0)),
            pl.BlockSpec((pole_count, channels + LANES), fixed),
            pl.BlockSpec((rounds, pole_count, width), lambda j: (0, 0, j)),
            pl.BlockSpec((length, LANES), fixed),
        ],
        out_shape=[
            jax.ShapeDtypeStruct((length, channels), jnp.float32),
            jax.ShapeDtypeStruct((length, channels), jnp.float32),
            jax.ShapeDtypeStruct((pole_count, channels + LANES), jnp.float32),
            jax.ShapeDtypeStruct((rounds, pole_count, channels), jnp.float32),
            jax.ShapeDtypeStruct((length, LANES), jnp.float32),
        ],
        scratch_shapes=[
            pltpu.VMEM((span_r, width), jnp.bfloat16),
            pltpu.VMEM((taps * length, span_r), jnp.bfloat16),
            pltpu.VMEM((length, length), jnp.float32),
            pltpu.VMEM((8, length), jnp.float32),
        ],
        compiler_params=pltpu.CompilerParams(dimension_semantics=("arbitrary",)),
    )(qkv, qkv, qkv, rim, rim, rim, short_w, short_w, short_w, e_rows, rates_t, residues_t)

    prefix, partner, got = chip_scan(packed, decays, span_of, channels, pole_count, peers, me)
    half = channels // 2
    hb = max(half // final_width, 1)
    flag_block = channels // LANES
    rate_rows = jnp.stack([rates, residues]).reshape(2, 1, filters * pole_count)

    nbf = channels // final_width
    iw_width = final_width // group_width * pole_count
    return pl.pallas_call(
        functools.partial(final_kernel, group_width, pole_count, min(256, width), hb),
        grid=(nbf,),
        in_specs=[
            pl.BlockSpec((length, final_width), col(0)),
            pl.BlockSpec((length, final_width), col(0)),
            pl.BlockSpec((pole_count, final_width), lambda j: (0, j % hb)),
            pl.BlockSpec((pole_count, final_width), lambda j: (0, j % hb)),
            pl.BlockSpec((pole_count, final_width), col(0)),
            pl.BlockSpec((pole_count, final_width), col(0)),
            pl.BlockSpec((pole_count, LANES), lambda j: (0, flag_block)),
            pl.BlockSpec((pole_count, LANES), lambda j: (0, flag_block)),
            pl.BlockSpec((1, pole_count, final_width), lambda j: (span_of[1], 0, j)),
            pl.BlockSpec((2, 1, iw_width), lambda j: (0, 0, j)),
            pl.BlockSpec((length, LANES), fixed),
        ],
        out_specs=pl.BlockSpec((length, final_width), col(0)),
        out_shape=jax.ShapeDtypeStruct((length, channels), jnp.bfloat16),
        compiler_params=pltpu.CompilerParams(dimension_semantics=("arbitrary",)),
    )(q_part, local_part, prefix, partner, packed, got, packed, got, decays, rate_rows, info)


def solution(mesh):
    return jax.shard_map(
        on_device,
        mesh=mesh,
        in_specs=(P(("groups", "ctx"), None), P(("groups", "ctx")), P(), P(), P()),
        out_specs=P(("groups", "ctx"), None),
        check_vma=False,
    )
```

```python
import functools

import jax
import jax.numpy as jnp
from jax import lax
from jax.experimental import pallas as pl
from jax.experimental.pallas import tpu as pltpu
from jax.sharding import PartitionSpec as P

WIDTH = 1024
FINAL_WIDTH = 2048
RIM = 8
SUB = 256
LANES = 128


def from_behind(shard, axis, by):
    peers = lax.axis_size(axis)
    pairs = [(i, i + by) for i in range(peers) if 0 <= i + by < peers]
    return lax.ppermute(shard, axis, pairs)


def split2(x):
    hi = x.astype(jnp.bfloat16)
    lo = (x - hi.astype(jnp.float32)).astype(jnp.bfloat16)
    return hi, lo


def split3(x):
    hi = x.astype(jnp.bfloat16)
    rest = x - hi.astype(jnp.float32)
    mid = rest.astype(jnp.bfloat16)
    lo = (rest - mid.astype(jnp.float32)).astype(jnp.bfloat16)
    return hi, mid, lo


def local_kernel(taps, group_width, spans,
                 xq, xk, xv, rq, rk, rv, wq, wk, wv, e_ref, rt_ref, et_ref,
                 q_out, loc_out, pk_out, dec_out, info_out, ext_s, shift_s, vis_s, tail_s):
    length, width = xq.shape
    groups = width // group_width
    pole_count = rt_ref.shape[1]
    channels = pk_out.shape[1] - LANES
    span_r = e_ref.shape[1]
    step = pl.program_id(0)

    @pl.when(step == 0)
    def _():
        e_row = e_ref[0:1, :]
        t_col = lax.broadcasted_iota(jnp.int32, (length, span_r), 0)
        r_row = lax.broadcasted_iota(jnp.int32, (length, span_r), 1)
        doc_col = jnp.sum(jnp.where(r_row == t_col, e_row, 0.0), axis=1, keepdims=True)
        eq = e_row == doc_col
        place = jnp.where(r_row < length, r_row, r_row - length - RIM)
        for j in range(taps):
            hit = eq & (place == t_col - j) & (r_row < length + RIM)
            shift_s[j * length:(j + 1) * length, :] = jnp.where(hit, 1.0, 0.0).astype(jnp.bfloat16)
        eqf = jnp.where(eq, 1.0, 0.0)
        causal = r_row[:, :length] <= t_col[:, :length]
        vis_s[...] = jnp.where(causal, eqf[:, :length], 0.0)
        tail_s[...] = jnp.broadcast_to(eqf[length - 1:length, :length], tail_s.shape)
        into = eqf[0:1, length + RIM - 1:length + RIM]
        flag = into * eqf[length - 1:length, 0:1]
        pk_out[:, channels:channels + LANES] = jnp.broadcast_to(flag, (pole_count, LANES))
        lane = lax.broadcasted_iota(jnp.int32, info_out.shape, 1)
        info_out[...] = jnp.where(lane == 0, eqf[:, 0:1], jnp.broadcast_to(into, info_out.shape))
        ext_s[...] = jnp.zeros_like(ext_s)


    def conv(x_ref, r_ref, w_ref):
        ext_s[0:length, :] = x_ref[...]
        ext_s[length:length + RIM, :] = r_ref[...]
        ext = ext_s[...]
        w = w_ref[...]
        acc = w[0:1, :] * x_ref[...].astype(jnp.float32)
        for j in range(1, taps):
            window = jnp.dot(shift_s[j * length:(j + 1) * length, :], ext, preferred_element_type=jnp.float32)
            acc = acc + w[j:j + 1, :] * window
        return acc

    cq = conv(xq, rq, wq)
    ck = conv(xk, rk, wk)
    cv = conv(xv, rv, wv)
    q_out[...] = cq
    gated = (ck * cv).astype(jnp.bfloat16)

    rt = rt_ref[0]
    et = et_ref[0]
    lane = lax.broadcasted_iota(jnp.int32, (1, length), 1)
    lags = ((length - lane) % length).astype(jnp.float32)
    to_end = (length - 1 - lane).astype(jnp.float32)
    at_tail = tail_s[0:1, :]
    visible = vis_s[...] > 0.5
    sub = min(SUB, width)
    sub_groups = sub // group_width
    lane_group = lax.broadcasted_iota(jnp.int32, (length, sub), 1) // group_width
    for h in range(width // sub):
        part = gated[:, h * sub:(h + 1) * sub]
        zero = jnp.zeros_like(part)
        xbd = jnp.concatenate([jnp.where(lane_group == g, part, zero) for g in range(sub_groups)], axis=0)
        pieces = []
        ends = []
        for g in range(h * sub_groups, (h + 1) * sub_groups):
            a_col = rt[:, g:g + 1]
            r_col = et[:, g:g + 1]
            base = jnp.sum(r_col * jnp.exp(-a_col * lags), axis=0, keepdims=True)
            row = jnp.broadcast_to(base.astype(jnp.bfloat16), (length, length))
            rolled = pltpu.roll(row, 0, 1, stride=1, stride_axis=0)
            pieces.append(jnp.where(visible, rolled, jnp.zeros_like(rolled)))
            ends.append(jnp.exp(-a_col * to_end) * at_tail)
        e_hi, e_lo = split2(jnp.concatenate(ends, axis=1))
        t_hi = jnp.concatenate(pieces, axis=1)
        res = jnp.dot(jnp.concatenate([t_hi, e_hi, e_lo], axis=0), xbd, preferred_element_type=jnp.float32)
        loc_out[:, h * sub:(h + 1) * sub] = res[0:length]
        st = res[length:length + pole_count] + res[length + pole_count:length + 2 * pole_count]
        pk_out[:, pl.ds(pl.multiple_of(step * width + h * sub, sub), sub)] = st

    spread = (lax.broadcasted_iota(jnp.int32, (groups, width), 1) // group_width
              == lax.broadcasted_iota(jnp.int32, (groups, width), 0)).astype(jnp.bfloat16)
    rate_cols = None
    for piece in split3(rt):
        part = jnp.dot(piece, spread, preferred_element_type=jnp.float32)
        rate_cols = part if rate_cols is None else rate_cols + part
    for r, span in enumerate(spans):
        dec_out[r] = jnp.exp(-rate_cols * span)


def final_kernel(group_width, pole_count, sub, hb, q_ref, loc_ref, zo_ref, zp_ref, pk_ref, gt_ref, pf_ref, gf_ref,
                 d1_ref, rr_ref, info_ref, o_ref):
    length, width = q_ref.shape
    groups = sub // group_width
    core = lax.axis_index("ctx") % 2
    odd = core == 1
    mine_half = (pl.program_id(0) // hb) == core
    full = jnp.where(mine_half, zo_ref[...], zp_ref[...])
    even_s = jnp.where(odd, gt_ref[...], pk_ref[...])
    even_f = jnp.where(odd, gf_ref[:, 0:1], pf_ref[:, 0:1])
    joined = jnp.where(odd, (even_f * d1_ref[0]) * full + even_s, full)
    b_all = joined * info_ref[0:1, 1:2]
    tcol = (lax.broadcasted_iota(jnp.int32, (length, 1), 0) + 1).astype(jnp.float32)
    iw = rr_ref[1] * jnp.exp(-rr_ref[0] * tcol) * info_ref[:, 0:1]
    iw_hi, iw_lo = split2(iw)
    shape = (groups * pole_count, sub)
    row_group = lax.broadcasted_iota(jnp.int32, shape, 0) // pole_count
    lane_group = lax.broadcasted_iota(jnp.int32, shape, 1) // group_width
    same = row_group == lane_group
    for s in range(width // sub):
        cols = slice(s * sub, (s + 1) * sub)
        tiled = jnp.concatenate([b_all[:, cols]] * groups, axis=0)
        b_hi, b_lo = split2(jnp.where(same, tiled, 0.0))
        poles = slice(s * shape[0], (s + 1) * shape[0])
        ih = iw_hi[:, poles]
        car = jnp.dot(ih, b_hi, preferred_element_type=jnp.float32)
        car = car + jnp.dot(ih, b_lo, preferred_element_type=jnp.float32)
        car = car + jnp.dot(iw_lo[:, poles], b_hi, preferred_element_type=jnp.float32)
        o_ref[:, cols] = (q_ref[:, cols] * (loc_ref[:, cols] + car)).astype(o_ref.dtype)


def swap_cores(shard, axis):
    peers = lax.axis_size(axis)
    return lax.ppermute(shard, axis, [(i, i ^ 1) for i in range(peers)])


def chip_scan(packed, decays, span_of, channels, pole_count, peers, me):
    core = me % 2
    odd = core == 1
    half = channels // 2
    mine = lambda x: lax.dynamic_slice_in_dim(x, core * half, half, axis=1)
    got = swap_cores(packed, "ctx")
    own_s, own_f = packed[:, :channels], packed[:, channels:channels + 1]
    other_s, other_f = got[:, :channels], got[:, channels:channels + 1]
    even_s = jnp.where(odd, other_s, own_s)
    odd_s = jnp.where(odd, own_s, other_s)
    even_f = jnp.where(odd, other_f, own_f)
    odd_f = jnp.where(odd, own_f, other_f)
    total = (odd_f * mine(decays[span_of[1]])) * mine(even_s) + mine(odd_s)
    flag = even_f * odd_f
    chips = peers // 2
    prefix = jnp.zeros_like(total)
    prefix_flag = jnp.ones_like(flag)
    offset = 1
    while offset < chips:
        load = jnp.concatenate([total, jnp.broadcast_to(flag, (pole_count, LANES))], axis=1)
        got_load = from_behind(load, "ctx", 2 * offset)
        came, came_flag = got_load[:, :half], got_load[:, half:half + 1]
        if offset == 1:
            prefix = prefix + prefix_flag * came
        else:
            prefix = prefix + (prefix_flag * mine(decays[span_of[2 * offset - 2]])) * came
        prefix_flag = prefix_flag * came_flag
        if 2 * offset < chips:
            total = total + (flag * mine(decays[span_of[2 * offset]])) * came
            flag = flag * came_flag
        offset *= 2
    return prefix, swap_cores(prefix, "ctx"), got


def scan_spans(peers):
    chips = peers // 2
    spans = {1}
    offset = 1
    while offset < chips:
        if offset > 1:
            spans.add(2 * offset - 2)
        if 2 * offset < chips:
            spans.add(2 * offset)
        offset *= 2
    return sorted(spans)


def on_device(qkv, doc_ids, short_w, rates, residues):
    length = qkv.shape[0]
    taps = short_w.shape[0]
    channels = qkv.shape[1] // 3
    filters, pole_count = rates.shape
    group_width = channels // filters
    width = min(WIDTH, channels)
    nb = channels // width
    gpb = width // group_width
    final_width = min(FINAL_WIDTH, channels)
    peers = lax.axis_size("ctx")
    me = lax.axis_index("ctx")

    tail_docs = jnp.broadcast_to(doc_ids[length - RIM:, None].astype(jnp.bfloat16), (RIM, LANES))
    rim = from_behind(jnp.concatenate([qkv[length - RIM:], tail_docs], axis=1), "ctx", 1)
    prev_docs = rim[:, 3 * channels].astype(jnp.int32)
    prev_last = prev_docs[RIM - 1]

    span_r = 2 * LANES
    e_vec = jnp.concatenate([doc_ids, prev_docs, jnp.full((span_r - length - RIM,), -1, jnp.int32)]).astype(jnp.float32)
    e_rows = e_vec.reshape(1, span_r)

    both_t = jnp.stack([rates, residues]).reshape(2, nb, gpb, pole_count).transpose(0, 1, 3, 2)
    rates_t, residues_t = both_t[0], both_t[1]
    span_list = scan_spans(peers)
    span_of = {v: i for i, v in enumerate(span_list)}
    rounds = len(span_list)
    spans = tuple(float(length * v) for v in span_list)

    col = lambda off: (lambda j: (0, j + off))
    fixed = lambda j: (0, 0)
    q_part, local_part, packed, decays, info = pl.pallas_call(
        functools.partial(local_kernel, taps, group_width, spans),
        grid=(nb,),
        in_specs=[
            pl.BlockSpec((length, width), col(0)),
            pl.BlockSpec((length, width), col(nb)),
            pl.BlockSpec((length, width), col(2 * nb)),
            pl.BlockSpec((RIM, width), col(0)),
            pl.BlockSpec((RIM, width), col(nb)),
            pl.BlockSpec((RIM, width), col(2 * nb)),
            pl.BlockSpec((taps, width), col(0)),
            pl.BlockSpec((taps, width), col(nb)),
            pl.BlockSpec((taps, width), col(2 * nb)),
            pl.BlockSpec((1, span_r), fixed),
            pl.BlockSpec((1, pole_count, gpb), lambda j: (j, 0, 0)),
            pl.BlockSpec((1, pole_count, gpb), lambda j: (j, 0, 0)),
        ],
        out_specs=[
            pl.BlockSpec((length, width), col(0)),
            pl.BlockSpec((length, width), col(0)),
            pl.BlockSpec((pole_count, channels + LANES), fixed),
            pl.BlockSpec((rounds, pole_count, width), lambda j: (0, 0, j)),
            pl.BlockSpec((length, LANES), fixed),
        ],
        out_shape=[
            jax.ShapeDtypeStruct((length, channels), jnp.float32),
            jax.ShapeDtypeStruct((length, channels), jnp.float32),
            jax.ShapeDtypeStruct((pole_count, channels + LANES), jnp.float32),
            jax.ShapeDtypeStruct((rounds, pole_count, channels), jnp.float32),
            jax.ShapeDtypeStruct((length, LANES), jnp.float32),
        ],
        scratch_shapes=[
            pltpu.VMEM((span_r, width), jnp.bfloat16),
            pltpu.VMEM((taps * length, span_r), jnp.bfloat16),
            pltpu.VMEM((length, length), jnp.float32),
            pltpu.VMEM((8, length), jnp.float32),
        ],
        compiler_params=pltpu.CompilerParams(dimension_semantics=("arbitrary",)),
    )(qkv, qkv, qkv, rim, rim, rim, short_w, short_w, short_w, e_rows, rates_t, residues_t)

    prefix, partner, got = chip_scan(packed, decays, span_of, channels, pole_count, peers, me)
    half = channels // 2
    hb = max(half // final_width, 1)
    flag_block = channels // LANES
    rate_rows = jnp.stack([rates, residues]).reshape(2, 1, filters * pole_count)

    nbf = channels // final_width
    iw_width = final_width // group_width * pole_count
    return pl.pallas_call(
        functools.partial(final_kernel, group_width, pole_count, min(256, width), hb),
        grid=(nbf,),
        in_specs=[
            pl.BlockSpec((length, final_width), col(0)),
            pl.BlockSpec((length, final_width), col(0)),
            pl.BlockSpec((pole_count, final_width), lambda j: (0, j % hb)),
            pl.BlockSpec((pole_count, final_width), lambda j: (0, j % hb)),
            pl.BlockSpec((pole_count, final_width), col(0)),
            pl.BlockSpec((pole_count, final_width), col(0)),
            pl.BlockSpec((pole_count, LANES), lambda j: (0, flag_block)),
            pl.BlockSpec((pole_count, LANES), lambda j: (0, flag_block)),
            pl.BlockSpec((1, pole_count, final_width), lambda j: (span_of[1], 0, j)),
            pl.BlockSpec((2, 1, iw_width), lambda j: (0, 0, j)),
            pl.BlockSpec((length, LANES), fixed),
        ],
        out_specs=pl.BlockSpec((length, final_width), col(0)),
        out_shape=jax.ShapeDtypeStruct((length, channels), jnp.bfloat16),
        compiler_params=pltpu.CompilerParams(dimension_semantics=("arbitrary",)),
    )(q_part, local_part, prefix, partner, packed, got, packed, got, decays, rate_rows, info)


def solution(mesh):
    return jax.shard_map(
        on_device,
        mesh=mesh,
        in_specs=(P(("groups", "ctx"), None), P(("groups", "ctx")), P(), P(), P()),
        out_specs=P(("groups", "ctx"), None),
        check_vma=False,
    )
```

```python
import functools

import jax
import jax.numpy as jnp
from jax import lax
from jax.experimental import pallas as pl
from jax.experimental.pallas import tpu as pltpu
from jax.sharding import PartitionSpec as P

WIDTH = 1024
FINAL_WIDTH = 2048
RIM = 8
SUB = 256
LANES = 128


def from_behind(shard, axis, by):
    peers = lax.axis_size(axis)
    pairs = [(i, i + by) for i in range(peers) if 0 <= i + by < peers]
    return lax.ppermute(shard, axis, pairs)


def split2(x):
    hi = x.astype(jnp.bfloat16)
    lo = (x - hi.astype(jnp.float32)).astype(jnp.bfloat16)
    return hi, lo


def split3(x):
    hi = x.astype(jnp.bfloat16)
    rest = x - hi.astype(jnp.float32)
    mid = rest.astype(jnp.bfloat16)
    lo = (rest - mid.astype(jnp.float32)).astype(jnp.bfloat16)
    return hi, mid, lo


def local_kernel(taps, group_width, spans,
                 xq, xk, xv, rq, rk, rv, wq, wk, wv, e_ref, rt_ref, et_ref,
                 q_out, loc_out, pk_out, dec_out, info_out, ext_s, shift_s, vis_s, tail_s):
    length, width = xq.shape
    groups = width // group_width
    pole_count = rt_ref.shape[1]
    channels = pk_out.shape[1] - LANES
    span_r = e_ref.shape[1]
    step = pl.program_id(0)

    @pl.when(step == 0)
    def _():
        e_row = e_ref[0:1, :]
        t_col = lax.broadcasted_iota(jnp.int32, (length, span_r), 0)
        r_row = lax.broadcasted_iota(jnp.int32, (length, span_r), 1)
        doc_col = jnp.sum(jnp.where(r_row == t_col, e_row, 0.0), axis=1, keepdims=True)
        eq = e_row == doc_col
        place = jnp.where(r_row < length, r_row, r_row - length - RIM)
        for j in range(taps):
            hit = eq & (place == t_col - j) & (r_row < length + RIM)
            shift_s[j * length:(j + 1) * length, :] = jnp.where(hit, 1.0, 0.0).astype(jnp.bfloat16)
        eqf = jnp.where(eq, 1.0, 0.0)
        causal = r_row[:, :length] <= t_col[:, :length]
        vis_s[...] = jnp.where(causal, eqf[:, :length], 0.0)
        tail_s[...] = jnp.broadcast_to(eqf[length - 1:length, :length], tail_s.shape)
        into = eqf[0:1, length + RIM - 1:length + RIM]
        flag = into * eqf[length - 1:length, 0:1]
        pk_out[:, channels:channels + LANES] = jnp.broadcast_to(flag, (pole_count, LANES))
        lane = lax.broadcasted_iota(jnp.int32, info_out.shape, 1)
        info_out[...] = jnp.where(lane == 0, eqf[:, 0:1], jnp.broadcast_to(into, info_out.shape))
        ext_s[...] = jnp.zeros_like(ext_s)


    def conv(x_ref, r_ref, w_ref):
        ext_s[0:length, :] = x_ref[...]
        ext_s[length:length + RIM, :] = r_ref[...]
        w = w_ref[...]
        outs = []
        for c0 in range(0, width, 2 * SUB):
            cols = slice(c0, c0 + 2 * SUB)
            ext = ext_s[:, cols]
            acc = w[0:1, cols] * x_ref[:, cols].astype(jnp.float32)
            for j in range(1, taps):
                window = jnp.dot(shift_s[j * length:(j + 1) * length, :], ext, preferred_element_type=jnp.float32)
                acc = acc + w[j:j + 1, cols] * window
            outs.append(acc)
        return jnp.concatenate(outs, axis=1)

    cq = conv(xq, rq, wq)
    ck = conv(xk, rk, wk)
    cv = conv(xv, rv, wv)
    q_out[...] = cq
    gated = (ck * cv).astype(jnp.bfloat16)

    rt = rt_ref[0]
    et = et_ref[0]
    lane = lax.broadcasted_iota(jnp.int32, (1, length), 1)
    lags = ((length - lane) % length).astype(jnp.float32)
    to_end = (length - 1 - lane).astype(jnp.float32)
    at_tail = tail_s[0:1, :]
    visible = vis_s[...] > 0.5
    sub = min(SUB, width)
    sub_groups = sub // group_width
    lane_group = lax.broadcasted_iota(jnp.int32, (length, sub), 1) // group_width
    for h in range(width // sub):
        part = gated[:, h * sub:(h + 1) * sub]
        zero = jnp.zeros_like(part)
        xbd = jnp.concatenate([jnp.where(lane_group == g, part, zero) for g in range(sub_groups)], axis=0)
        pieces = []
        ends = []
        for g in range(h * sub_groups, (h + 1) * sub_groups):
            a_col = rt[:, g:g + 1]
            r_col = et[:, g:g + 1]
            base = jnp.sum(r_col * jnp.exp(-a_col * lags), axis=0, keepdims=True)
            row = jnp.broadcast_to(base.astype(jnp.bfloat16), (length, length))
            rolled = pltpu.roll(row, 0, 1, stride=1, stride_axis=0)
            pieces.append(jnp.where(visible, rolled, jnp.zeros_like(rolled)))
            ends.append(jnp.exp(-a_col * to_end) * at_tail)
        e_hi, e_lo = split2(jnp.concatenate(ends, axis=1))
        t_hi = jnp.concatenate(pieces, axis=1)
        res = jnp.dot(jnp.concatenate([t_hi, e_hi, e_lo], axis=0), xbd, preferred_element_type=jnp.float32)
        loc_out[:, h * sub:(h + 1) * sub] = res[0:length]
        st = res[length:length + pole_count] + res[length + pole_count:length + 2 * pole_count]
        pk_out[:, pl.ds(pl.multiple_of(step * width + h * sub, sub), sub)] = st

    spread = (lax.broadcasted_iota(jnp.int32, (groups, width), 1) // group_width
              == lax.broadcasted_iota(jnp.int32, (groups, width), 0)).astype(jnp.bfloat16)
    rate_cols = None
    for piece in split3(rt):
        part = jnp.dot(piece, spread, preferred_element_type=jnp.float32)
        rate_cols = part if rate_cols is None else rate_cols + part
    for r, span in enumerate(spans):
        dec_out[r] = jnp.exp(-rate_cols * span)


def final_kernel(group_width, pole_count, sub, hb, q_ref, loc_ref, zo_ref, zp_ref, pk_ref, gt_ref, pf_ref, gf_ref,
                 d1_ref, rr_ref, info_ref, o_ref):
    length, width = q_ref.shape
    groups = sub // group_width
    core = lax.axis_index("ctx") % 2
    odd = core == 1
    mine_half = (pl.program_id(0) // hb) == core
    full = jnp.where(mine_half, zo_ref[...], zp_ref[...])
    even_s = jnp.where(odd, gt_ref[...], pk_ref[...])
    even_f = jnp.where(odd, gf_ref[:, 0:1], pf_ref[:, 0:1])
    joined = jnp.where(odd, (even_f * d1_ref[0]) * full + even_s, full)
    b_all = joined * info_ref[0:1, 1:2]
    tcol = (lax.broadcasted_iota(jnp.int32, (length, 1), 0) + 1).astype(jnp.float32)
    iw = rr_ref[1] * jnp.exp(-rr_ref[0] * tcol) * info_ref[:, 0:1]
    iw_hi, iw_lo = split2(iw)
    shape = (groups * pole_count, sub)
    row_group = lax.broadcasted_iota(jnp.int32, shape, 0) // pole_count
    lane_group = lax.broadcasted_iota(jnp.int32, shape, 1) // group_width
    same = row_group == lane_group
    for s in range(width // sub):
        cols = slice(s * sub, (s + 1) * sub)
        tiled = jnp.concatenate([b_all[:, cols]] * groups, axis=0)
        b_hi, b_lo = split2(jnp.where(same, tiled, 0.0))
        poles = slice(s * shape[0], (s + 1) * shape[0])
        ih = iw_hi[:, poles]
        car = jnp.dot(ih, b_hi, preferred_element_type=jnp.float32)
        car = car + jnp.dot(ih, b_lo, preferred_element_type=jnp.float32)
        car = car + jnp.dot(iw_lo[:, poles], b_hi, preferred_element_type=jnp.float32)
        o_ref[:, cols] = (q_ref[:, cols] * (loc_ref[:, cols] + car)).astype(o_ref.dtype)


def swap_cores(shard, axis):
    peers = lax.axis_size(axis)
    return lax.ppermute(shard, axis, [(i, i ^ 1) for i in range(peers)])


def chip_scan(packed, decays, span_of, channels, pole_count, peers, me):
    core = me % 2
    odd = core == 1
    half = channels // 2
    mine = lambda x: lax.dynamic_slice_in_dim(x, core * half, half, axis=1)
    got = swap_cores(packed, "ctx")
    own_s, own_f = packed[:, :channels], packed[:, channels:channels + 1]
    other_s, other_f = got[:, :channels], got[:, channels:channels + 1]
    even_s = jnp.where(odd, other_s, own_s)
    odd_s = jnp.where(odd, own_s, other_s)
    even_f = jnp.where(odd, other_f, own_f)
    odd_f = jnp.where(odd, own_f, other_f)
    total = (odd_f * mine(decays[span_of[1]])) * mine(even_s) + mine(odd_s)
    flag = even_f * odd_f
    chips = peers // 2
    prefix = jnp.zeros_like(total)
    prefix_flag = jnp.ones_like(flag)
    offset = 1
    while offset < chips:
        load = jnp.concatenate([total, jnp.broadcast_to(flag, (pole_count, LANES))], axis=1)
        got_load = from_behind(load, "ctx", 2 * offset)
        came, came_flag = got_load[:, :half], got_load[:, half:half + 1]
        if offset == 1:
            prefix = prefix + prefix_flag * came
        else:
            prefix = prefix + (prefix_flag * mine(decays[span_of[2 * offset - 2]])) * came
        prefix_flag = prefix_flag * came_flag
        if 2 * offset < chips:
            total = total + (flag * mine(decays[span_of[2 * offset]])) * came
            flag = flag * came_flag
        offset *= 2
    return prefix, swap_cores(prefix, "ctx"), got


def scan_spans(peers):
    chips = peers // 2
    spans = {1}
    offset = 1
    while offset < chips:
        if offset > 1:
            spans.add(2 * offset - 2)
        if 2 * offset < chips:
            spans.add(2 * offset)
        offset *= 2
    return sorted(spans)


def on_device(qkv, doc_ids, short_w, rates, residues):
    length = qkv.shape[0]
    taps = short_w.shape[0]
    channels = qkv.shape[1] // 3
    filters, pole_count = rates.shape
    group_width = channels // filters
    width = min(WIDTH, channels)
    nb = channels // width
    gpb = width // group_width
    final_width = min(FINAL_WIDTH, channels)
    peers = lax.axis_size("ctx")
    me = lax.axis_index("ctx")

    tail_docs = jnp.broadcast_to(doc_ids[length - RIM:, None].astype(jnp.bfloat16), (RIM, LANES))
    rim = from_behind(jnp.concatenate([qkv[length - RIM:], tail_docs], axis=1), "ctx", 1)
    prev_docs = rim[:, 3 * channels].astype(jnp.int32)
    prev_last = prev_docs[RIM - 1]

    span_r = 2 * LANES
    e_vec = jnp.concatenate([doc_ids, prev_docs, jnp.full((span_r - length - RIM,), -1, jnp.int32)]).astype(jnp.float32)
    e_rows = jnp.broadcast_to(e_vec[None, :], (8, span_r))

    both_t = jnp.stack([rates, residues]).reshape(2, nb, gpb, pole_count).transpose(0, 1, 3, 2)
    rates_t, residues_t = both_t[0], both_t[1]
    span_list = scan_spans(peers)
    span_of = {v: i for i, v in enumerate(span_list)}
    rounds = len(span_list)
    spans = tuple(float(length * v) for v in span_list)

    col = lambda off: (lambda j: (0, j + off))
    fixed = lambda j: (0, 0)
    q_part, local_part, packed, decays, info = pl.pallas_call(
        functools.partial(local_kernel, taps, group_width, spans),
        grid=(nb,),
        in_specs=[
            pl.BlockSpec((length, width), col(0)),
            pl.BlockSpec((length, width), col(nb)),
            pl.BlockSpec((length, width), col(2 * nb)),
            pl.BlockSpec((RIM, width), col(0)),
            pl.BlockSpec((RIM, width), col(nb)),
            pl.BlockSpec((RIM, width), col(2 * nb)),
            pl.BlockSpec((taps, width), col(0)),
            pl.BlockSpec((taps, width), col(nb)),
            pl.BlockSpec((taps, width), col(2 * nb)),
            pl.BlockSpec((8, span_r), fixed),
            pl.BlockSpec((1, pole_count, gpb), lambda j: (j, 0, 0)),
            pl.BlockSpec((1, pole_count, gpb), lambda j: (j, 0, 0)),
        ],
        out_specs=[
            pl.BlockSpec((length, width), col(0)),
            pl.BlockSpec((length, width), col(0)),
            pl.BlockSpec((pole_count, channels + LANES), fixed),
            pl.BlockSpec((rounds, pole_count, width), lambda j: (0, 0, j)),
            pl.BlockSpec((length, LANES), fixed),
        ],
        out_shape=[
            jax.ShapeDtypeStruct((length, channels), jnp.float32),
            jax.ShapeDtypeStruct((length, channels), jnp.float32),
            jax.ShapeDtypeStruct((pole_count, channels + LANES), jnp.float32),
            jax.ShapeDtypeStruct((rounds, pole_count, channels), jnp.float32),
            jax.ShapeDtypeStruct((length, LANES), jnp.float32),
        ],
        scratch_shapes=[
            pltpu.VMEM((span_r, width), jnp.bfloat16),
            pltpu.VMEM((taps * length, span_r), jnp.bfloat16),
            pltpu.VMEM((length, length), jnp.float32),
            pltpu.VMEM((8, length), jnp.float32),
        ],
        compiler_params=pltpu.CompilerParams(dimension_semantics=("arbitrary",)),
    )(qkv, qkv, qkv, rim, rim, rim, short_w, short_w, short_w, e_rows, rates_t, residues_t)

    prefix, partner, got = chip_scan(packed, decays, span_of, channels, pole_count, peers, me)
    half = channels // 2
    hb = max(half // final_width, 1)
    flag_block = channels // LANES
    rate_rows = jnp.stack([rates, residues]).reshape(2, 1, filters * pole_count)

    nbf = channels // final_width
    iw_width = final_width // group_width * pole_count
    return pl.pallas_call(
        functools.partial(final_kernel, group_width, pole_count, min(256, width), hb),
        grid=(nbf,),
        in_specs=[
            pl.BlockSpec((length, final_width), col(0)),
            pl.BlockSpec((length, final_width), col(0)),
            pl.BlockSpec((pole_count, final_width), lambda j: (0, j % hb)),
            pl.BlockSpec((pole_count, final_width), lambda j: (0, j % hb)),
            pl.BlockSpec((pole_count, final_width), col(0)),
            pl.BlockSpec((pole_count, final_width), col(0)),
            pl.BlockSpec((pole_count, LANES), lambda j: (0, flag_block)),
            pl.BlockSpec((pole_count, LANES), lambda j: (0, flag_block)),
            pl.BlockSpec((1, pole_count, final_width), lambda j: (span_of[1], 0, j)),
            pl.BlockSpec((2, 1, iw_width), lambda j: (0, 0, j)),
            pl.BlockSpec((length, LANES), fixed),
        ],
        out_specs=pl.BlockSpec((length, final_width), col(0)),
        out_shape=jax.ShapeDtypeStruct((length, channels), jnp.bfloat16),
        compiler_params=pltpu.CompilerParams(dimension_semantics=("arbitrary",)),
    )(q_part, local_part, prefix, partner, packed, got, packed, got, decays, rate_rows, info)


def solution(mesh):
    return jax.shard_map(
        on_device,
        mesh=mesh,
        in_specs=(P(("groups", "ctx"), None), P(("groups", "ctx")), P(), P(), P()),
        out_specs=P(("groups", "ctx"), None),
        check_vma=False,
    )
```

```python
import functools

import jax
import jax.numpy as jnp
from jax import lax
from jax.experimental import pallas as pl
from jax.experimental.pallas import tpu as pltpu
from jax.sharding import PartitionSpec as P

WIDTH = 1024
FINAL_WIDTH = 2048
RIM = 8
SUB = 256
LANES = 128


def from_behind(shard, axis, by):
    peers = lax.axis_size(axis)
    pairs = [(i, i + by) for i in range(peers) if 0 <= i + by < peers]
    return lax.ppermute(shard, axis, pairs)


def split2(x):
    hi = x.astype(jnp.bfloat16)
    lo = (x - hi.astype(jnp.float32)).astype(jnp.bfloat16)
    return hi, lo


def split3(x):
    hi = x.astype(jnp.bfloat16)
    rest = x - hi.astype(jnp.float32)
    mid = rest.astype(jnp.bfloat16)
    lo = (rest - mid.astype(jnp.float32)).astype(jnp.bfloat16)
    return hi, mid, lo


def local_kernel(taps, group_width, spans,
                 xq, xk, xv, rq, rk, rv, wq, wk, wv, e_ref, rt_ref, et_ref,
                 q_out, loc_out, pk_out, dec_out, info_out, ext_s, shift_s, vis_s, tail_s):
    length, width = xq.shape
    groups = width // group_width
    pole_count = rt_ref.shape[1]
    channels = pk_out.shape[1] - LANES
    span_r = e_ref.shape[1]
    step = pl.program_id(0)

    @pl.when(step == 0)
    def _():
        e_row = e_ref[0:1, :]
        t_col = lax.broadcasted_iota(jnp.int32, (length, span_r), 0)
        r_row = lax.broadcasted_iota(jnp.int32, (length, span_r), 1)
        doc_col = jnp.sum(jnp.where(r_row == t_col, e_row, 0.0), axis=1, keepdims=True)
        eq = e_row == doc_col
        place = jnp.where(r_row < length, r_row, r_row - length - RIM)
        for j in range(taps):
            hit = eq & (place == t_col - j) & (r_row < length + RIM)
            shift_s[j * length:(j + 1) * length, :] = jnp.where(hit, 1.0, 0.0).astype(jnp.bfloat16)
        eqf = jnp.where(eq, 1.0, 0.0)
        causal = r_row[:, :length] <= t_col[:, :length]
        vis_s[...] = jnp.where(causal, eqf[:, :length], 0.0)
        tail_s[...] = jnp.broadcast_to(eqf[length - 1:length, :length], tail_s.shape)
        into = eqf[0:1, length + RIM - 1:length + RIM]
        flag = into * eqf[length - 1:length, 0:1]
        pk_out[:, channels:channels + LANES] = jnp.broadcast_to(flag, (pole_count, LANES))
        lane = lax.broadcasted_iota(jnp.int32, info_out.shape, 1)
        info_out[...] = jnp.where(lane == 0, eqf[:, 0:1], jnp.broadcast_to(into, info_out.shape))
        ext_s[...] = jnp.zeros_like(ext_s)


    def conv(x_ref, r_ref, w_ref):
        ext_s[0:length, :] = x_ref[...]
        ext_s[length:length + RIM, :] = r_ref[...]
        w = w_ref[...]
        outs = []
        for c0 in range(0, width, SUB):
            cols = slice(c0, c0 + SUB)
            ext = ext_s[:, cols]
            acc = w[0:1, cols] * x_ref[:, cols].astype(jnp.float32)
            for j in range(1, taps):
                window = jnp.dot(shift_s[j * length:(j + 1) * length, :], ext, preferred_element_type=jnp.float32)
                acc = acc + w[j:j + 1, cols] * window
            outs.append(acc)
        return jnp.concatenate(outs, axis=1)

    cq = conv(xq, rq, wq)
    ck = conv(xk, rk, wk)
    cv = conv(xv, rv, wv)
    q_out[...] = cq
    gated = (ck * cv).astype(jnp.bfloat16)

    rt = rt_ref[0]
    et = et_ref[0]
    lane = lax.broadcasted_iota(jnp.int32, (1, length), 1)
    lags = ((length - lane) % length).astype(jnp.float32)
    to_end = (length - 1 - lane).astype(jnp.float32)
    at_tail = tail_s[0:1, :]
    visible = vis_s[...] > 0.5
    sub = min(SUB, width)
    sub_groups = sub // group_width
    lane_group = lax.broadcasted_iota(jnp.int32, (length, sub), 1) // group_width
    for h in range(width // sub):
        part = gated[:, h * sub:(h + 1) * sub]
        zero = jnp.zeros_like(part)
        xbd = jnp.concatenate([jnp.where(lane_group == g, part, zero) for g in range(sub_groups)], axis=0)
        pieces = []
        ends = []
        for g in range(h * sub_groups, (h + 1) * sub_groups):
            a_col = rt[:, g:g + 1]
            r_col = et[:, g:g + 1]
            base = jnp.sum(r_col * jnp.exp(-a_col * lags), axis=0, keepdims=True)
            row = jnp.broadcast_to(base.astype(jnp.bfloat16), (length, length))
            rolled = pltpu.roll(row, 0, 1, stride=1, stride_axis=0)
            pieces.append(jnp.where(visible, rolled, jnp.zeros_like(rolled)))
            ends.append(jnp.exp(-a_col * to_end) * at_tail)
        e_hi, e_lo = split2(jnp.concatenate(ends, axis=1))
        t_hi = jnp.concatenate(pieces, axis=1)
        res = jnp.dot(jnp.concatenate([t_hi, e_hi, e_lo], axis=0), xbd, preferred_element_type=jnp.float32)
        loc_out[:, h * sub:(h + 1) * sub] = res[0:length]
        st = res[length:length + pole_count] + res[length + pole_count:length + 2 * pole_count]
        pk_out[:, pl.ds(pl.multiple_of(step * width + h * sub, sub), sub)] = st

    spread = (lax.broadcasted_iota(jnp.int32, (groups, width), 1) // group_width
              == lax.broadcasted_iota(jnp.int32, (groups, width), 0)).astype(jnp.bfloat16)
    rate_cols = None
    for piece in split3(rt):
        part = jnp.dot(piece, spread, preferred_element_type=jnp.float32)
        rate_cols = part if rate_cols is None else rate_cols + part
    for r, span in enumerate(spans):
        dec_out[r] = jnp.exp(-rate_cols * span)


def final_kernel(group_width, pole_count, sub, hb, q_ref, loc_ref, zo_ref, zp_ref, pk_ref, gt_ref, pf_ref, gf_ref,
                 d1_ref, rr_ref, info_ref, o_ref):
    length, width = q_ref.shape
    groups = sub // group_width
    core = lax.axis_index("ctx") % 2
    odd = core == 1
    mine_half = (pl.program_id(0) // hb) == core
    full = jnp.where(mine_half, zo_ref[...], zp_ref[...])
    even_s = jnp.where(odd, gt_ref[...], pk_ref[...])
    even_f = jnp.where(odd, gf_ref[:, 0:1], pf_ref[:, 0:1])
    joined = jnp.where(odd, (even_f * d1_ref[0]) * full + even_s, full)
    b_all = joined * info_ref[0:1, 1:2]
    tcol = (lax.broadcasted_iota(jnp.int32, (length, 1), 0) + 1).astype(jnp.float32)
    iw = rr_ref[1] * jnp.exp(-rr_ref[0] * tcol) * info_ref[:, 0:1]
    iw_hi, iw_lo = split2(iw)
    shape = (groups * pole_count, sub)
    row_group = lax.broadcasted_iota(jnp.int32, shape, 0) // pole_count
    lane_group = lax.broadcasted_iota(jnp.int32, shape, 1) // group_width
    same = row_group == lane_group
    for s in range(width // sub):
        cols = slice(s * sub, (s + 1) * sub)
        tiled = jnp.concatenate([b_all[:, cols]] * groups, axis=0)
        b_hi, b_lo = split2(jnp.where(same, tiled, 0.0))
        poles = slice(s * shape[0], (s + 1) * shape[0])
        ih = iw_hi[:, poles]
        car = jnp.dot(ih, b_hi, preferred_element_type=jnp.float32)
        car = car + jnp.dot(ih, b_lo, preferred_element_type=jnp.float32)
        car = car + jnp.dot(iw_lo[:, poles], b_hi, preferred_element_type=jnp.float32)
        o_ref[:, cols] = (q_ref[:, cols] * (loc_ref[:, cols] + car)).astype(o_ref.dtype)


def swap_cores(shard, axis):
    peers = lax.axis_size(axis)
    return lax.ppermute(shard, axis, [(i, i ^ 1) for i in range(peers)])


def chip_scan(packed, decays, span_of, channels, pole_count, peers, me):
    core = me % 2
    odd = core == 1
    half = channels // 2
    mine = lambda x: lax.dynamic_slice_in_dim(x, core * half, half, axis=1)
    got = swap_cores(packed, "ctx")
    own_s, own_f = packed[:, :channels], packed[:, channels:channels + 1]
    other_s, other_f = got[:, :channels], got[:, channels:channels + 1]
    even_s = jnp.where(odd, other_s, own_s)
    odd_s = jnp.where(odd, own_s, other_s)
    even_f = jnp.where(odd, other_f, own_f)
    odd_f = jnp.where(odd, own_f, other_f)
    total = (odd_f * mine(decays[span_of[1]])) * mine(even_s) + mine(odd_s)
    flag = even_f * odd_f
    chips = peers // 2
    prefix = jnp.zeros_like(total)
    prefix_flag = jnp.ones_like(flag)
    offset = 1
    while offset < chips:
        load = jnp.concatenate([total, jnp.broadcast_to(flag, (pole_count, LANES))], axis=1)
        got_load = from_behind(load, "ctx", 2 * offset)
        came, came_flag = got_load[:, :half], got_load[:, half:half + 1]
        if offset == 1:
            prefix = prefix + prefix_flag * came
        else:
            prefix = prefix + (prefix_flag * mine(decays[span_of[2 * offset - 2]])) * came
        prefix_flag = prefix_flag * came_flag
        if 2 * offset < chips:
            total = total + (flag * mine(decays[span_of[2 * offset]])) * came
            flag = flag * came_flag
        offset *= 2
    return prefix, swap_cores(prefix, "ctx"), got


def scan_spans(peers):
    chips = peers // 2
    spans = {1}
    offset = 1
    while offset < chips:
        if offset > 1:
            spans.add(2 * offset - 2)
        if 2 * offset < chips:
            spans.add(2 * offset)
        offset *= 2
    return sorted(spans)


def on_device(qkv, doc_ids, short_w, rates, residues):
    length = qkv.shape[0]
    taps = short_w.shape[0]
    channels = qkv.shape[1] // 3
    filters, pole_count = rates.shape
    group_width = channels // filters
    width = min(WIDTH, channels)
    nb = channels // width
    gpb = width // group_width
    final_width = min(FINAL_WIDTH, channels)
    peers = lax.axis_size("ctx")
    me = lax.axis_index("ctx")

    tail_docs = jnp.broadcast_to(doc_ids[length - RIM:, None].astype(jnp.bfloat16), (RIM, LANES))
    rim = from_behind(jnp.concatenate([qkv[length - RIM:], tail_docs], axis=1), "ctx", 1)
    prev_docs = rim[:, 3 * channels].astype(jnp.int32)
    prev_last = prev_docs[RIM - 1]

    span_r = 2 * LANES
    e_vec = jnp.concatenate([doc_ids, prev_docs, jnp.full((span_r - length - RIM,), -1, jnp.int32)]).astype(jnp.float32)
    e_rows = jnp.broadcast_to(e_vec[None, :], (8, span_r))

    both_t = jnp.stack([rates, residues]).reshape(2, nb, gpb, pole_count).transpose(0, 1, 3, 2)
    rates_t, residues_t = both_t[0], both_t[1]
    span_list = scan_spans(peers)
    span_of = {v: i for i, v in enumerate(span_list)}
    rounds = len(span_list)
    spans = tuple(float(length * v) for v in span_list)

    col = lambda off: (lambda j: (0, j + off))
    fixed = lambda j: (0, 0)
    q_part, local_part, packed, decays, info = pl.pallas_call(
        functools.partial(local_kernel, taps, group_width, spans),
        grid=(nb,),
        in_specs=[
            pl.BlockSpec((length, width), col(0)),
            pl.BlockSpec((length, width), col(nb)),
            pl.BlockSpec((length, width), col(2 * nb)),
            pl.BlockSpec((RIM, width), col(0)),
            pl.BlockSpec((RIM, width), col(nb)),
            pl.BlockSpec((RIM, width), col(2 * nb)),
            pl.BlockSpec((taps, width), col(0)),
            pl.BlockSpec((taps, width), col(nb)),
            pl.BlockSpec((taps, width), col(2 * nb)),
            pl.BlockSpec((8, span_r), fixed),
            pl.BlockSpec((1, pole_count, gpb), lambda j: (j, 0, 0)),
            pl.BlockSpec((1, pole_count, gpb), lambda j: (j, 0, 0)),
        ],
        out_specs=[
            pl.BlockSpec((length, width), col(0)),
            pl.BlockSpec((length, width), col(0)),
            pl.BlockSpec((pole_count, channels + LANES), fixed),
            pl.BlockSpec((rounds, pole_count, width), lambda j: (0, 0, j)),
            pl.BlockSpec((length, LANES), fixed),
        ],
        out_shape=[
            jax.ShapeDtypeStruct((length, channels), jnp.float32),
            jax.ShapeDtypeStruct((length, channels), jnp.float32),
            jax.ShapeDtypeStruct((pole_count, channels + LANES), jnp.float32),
            jax.ShapeDtypeStruct((rounds, pole_count, channels), jnp.float32),
            jax.ShapeDtypeStruct((length, LANES), jnp.float32),
        ],
        scratch_shapes=[
            pltpu.VMEM((span_r, width), jnp.bfloat16),
            pltpu.VMEM((taps * length, span_r), jnp.bfloat16),
            pltpu.VMEM((length, length), jnp.float32),
            pltpu.VMEM((8, length), jnp.float32),
        ],
        compiler_params=pltpu.CompilerParams(dimension_semantics=("arbitrary",)),
    )(qkv, qkv, qkv, rim, rim, rim, short_w, short_w, short_w, e_rows, rates_t, residues_t)

    prefix, partner, got = chip_scan(packed, decays, span_of, channels, pole_count, peers, me)
    half = channels // 2
    hb = max(half // final_width, 1)
    flag_block = channels // LANES
    rate_rows = jnp.stack([rates, residues]).reshape(2, 1, filters * pole_count)

    nbf = channels // final_width
    iw_width = final_width // group_width * pole_count
    return pl.pallas_call(
        functools.partial(final_kernel, group_width, pole_count, min(256, width), hb),
        grid=(nbf,),
        in_specs=[
            pl.BlockSpec((length, final_width), col(0)),
            pl.BlockSpec((length, final_width), col(0)),
            pl.BlockSpec((pole_count, final_width), lambda j: (0, j % hb)),
            pl.BlockSpec((pole_count, final_width), lambda j: (0, j % hb)),
            pl.BlockSpec((pole_count, final_width), col(0)),
            pl.BlockSpec((pole_count, final_width), col(0)),
            pl.BlockSpec((pole_count, LANES), lambda j: (0, flag_block)),
            pl.BlockSpec((pole_count, LANES), lambda j: (0, flag_block)),
            pl.BlockSpec((1, pole_count, final_width), lambda j: (span_of[1], 0, j)),
            pl.BlockSpec((2, 1, iw_width), lambda j: (0, 0, j)),
            pl.BlockSpec((length, LANES), fixed),
        ],
        out_specs=pl.BlockSpec((length, final_width), col(0)),
        out_shape=jax.ShapeDtypeStruct((length, channels), jnp.bfloat16),
        compiler_params=pltpu.CompilerParams(dimension_semantics=("arbitrary",)),
    )(q_part, local_part, prefix, partner, packed, got, packed, got, decays, rate_rows, info)


def solution(mesh):
    return jax.shard_map(
        on_device,
        mesh=mesh,
        in_specs=(P(("groups", "ctx"), None), P(("groups", "ctx")), P(), P(), P()),
        out_specs=P(("groups", "ctx"), None),
        check_vma=False,
    )
```
